32 devices in a mesh: req: 8 (over z, y), tp: 4 (over x, core).
Axes of the slice: x: 2, y: 2, z: 4, core: 2. Of those that a mesh axis runs over, the one named last changes fastest.
Arguments:
- hidden: bfloat16 [32, 128, 2304], P('req', None, 'tp')
- qkv: bfloat16 [32, 128, 4, 1024], P('req', None, 'tp')
- page_store: bfloat16 [16, 128, 4, 512], P('req', None, 'tp')
- page_owner: int32 [8], replicated, may hold values from 0 to 7, as said below
- page_slot: int32 [8], replicated, may hold values from 0 to 1
- lengths: int32 [32], replicated, may hold values from 1 to 128, 2048 in all
- request_perm: int32 [32], replicated, may hold values from 0 to 31, each once
- w_out: bfloat16 [2048, 2304], P(None, 'tp')
- post_gain: float32 [2304], P('tp'), may hold values from 0.25 to 1.75
Outputs:
- result: bfloat16 [32, 128, 2304], P('req', None, 'tp')
The draws below stay inside these ranges and needn't reach their ends.
Inputs may be any that keep to these rules, and one draw needn't show every extreme that they name: Page p lies in slot page_slot[p] of the device with index page_owner[p] along req; no two pages share an owner.
All inputs are finite; a program needn't handle non-finite values.
Results may differ from the reference program's by a relative error of at most 0.0043.
Values may be sent and summed in bfloat16 or wider, within the bound.
No kernel may reach another device: no remote copies, remote signals or barrier semaphores. Data moves between devices by JAX's collectives and lax.ppermute only.
A program may use at most 64 MiB of HBM per device.

```python
import math
import jax
import jax.numpy as jnp
import numpy as np
from jax import lax

D = 2304
H = 8
KVH = 4
HD = 256
PAGE = 128
PAGES = 8
SLOT_DEV = 2
SLEN = 128
REQS = 32
SLOTS = 16
N_REQ = 8


def column_scales(key):
    spread = jnp.exp(jax.random.uniform(key, (D,), jnp.float32, math.log(0.4), math.log(4.0)))
    trend = 3.0 ** (jnp.arange(D, dtype=jnp.float32) / D - 0.5)
    return spread * trend


def base_values(key, shape):
    return jax.random.normal(key, shape, jnp.float32)


def log_scale(key, shape, low, high):
    return jnp.exp(jax.random.uniform(key, shape, jnp.float32, math.log(low), math.log(high)))


def draw_hidden(key, part):
    first, second, third = jax.random.split(key, 3)
    base = jax.random.normal(first, (REQS, SLEN, D), jnp.float32)
    row_scale = log_scale(second, (REQS, SLEN, 1), 0.4, 4.0)
    return (base * row_scale * column_scales(third)).astype(jnp.bfloat16)


def draw_qkv(key, part):
    first, second, third = jax.random.split(key, 3)
    per_group = H // KVH
    base = base_values(first, (REQS, SLEN, KVH, per_group + 2, HD))
    query_scale = log_scale(second, (REQS, SLEN, KVH, per_group, 1), 0.3, 6.0)
    key_scale = log_scale(third, (REQS, SLEN, KVH, 1, 1), 0.5, 5.0)
    value_scale = jnp.ones((REQS, SLEN, KVH, 1, 1), jnp.float32)
    scale = jnp.concatenate([query_scale, key_scale, value_scale], 3)
    return (base * scale).reshape(REQS, SLEN, KVH, (per_group + 2) * HD).astype(jnp.bfloat16)


def draw_page_store(key, part):
    first, second = jax.random.split(key)
    base = base_values(first, (SLOTS, PAGE, KVH, 2, HD))
    key_scale = log_scale(second, (SLOTS, PAGE, KVH, 1, 1), 0.5, 5.0)
    scale = jnp.concatenate([key_scale, jnp.ones((SLOTS, PAGE, KVH, 1, 1), jnp.float32)], 3)
    return (base * scale).reshape(SLOTS, PAGE, KVH, 2 * HD).astype(jnp.bfloat16)


def draw_w_out(key, part):
    first, second = jax.random.split(key)
    base = jax.random.normal(first, (H * HD, D), jnp.float32)
    return (base * (H * HD) ** (-0.5) * column_scales(second)[None, :]).astype(jnp.bfloat16)


def draw_page_owner(key, part):
    return jax.random.permutation(jax.random.fold_in(key, 11), N_REQ)[:PAGES].astype(jnp.int32)


def draw_page_slot(key, part):
    return jax.random.randint(jax.random.fold_in(key, 23), (PAGES,), 0, SLOT_DEV).astype(jnp.int32)


def split_up(count, total, bound, lean):
    weights = [(1 << 20) // math.isqrt(rank ** lean) + 1 for rank in range(2, count + 1)]
    rest, counts = total - bound - (count - 1), [1] * (count - 1)
    while rest > 0:
        free = [i for i in range(count - 1) if counts[i] < bound]
        whole, left = sum([weights[i] for i in free]), rest
        for i in free:
            addition = min(bound - counts[i], max(1, left * weights[i] // whole), rest)
            counts[i] = counts[i] + addition
            rest = rest - addition
    return np.array([bound] + counts)


def uneven(key, count, total, most, lean):
    if count == 2:
        one = jax.random.randint(key, (), max(1, total - most), min(most, total - 1) + 1)
        return jnp.stack([one, total - one])
    tallies = jnp.asarray(split_up(count, total, most, lean), jnp.int32)
    pairs = (count - 1) // 2
    donor, sink = tallies[1:1 + 2 * pairs:2], tallies[2:2 + 2 * pairs:2]
    slack = jnp.minimum(donor - 1, most - sink)
    passed = jax.random.randint(jax.random.fold_in(key, 1), (pairs,), 0, 1 << 20) % (slack + 1)
    tallies = tallies.at[1:1 + 2 * pairs:2].set(donor - passed).at[2:2 + 2 * pairs:2].set(sink + passed)
    return tallies[jax.random.permutation(jax.random.fold_in(key, 2), count)]


def setup_inputs(seed: int = 0) -> dict:
    keys = jax.random.split(jax.random.key(seed), 10)
    hidden = draw_hidden(jax.random.fold_in(keys[9], 71), 0)
    qkv = draw_qkv(jax.random.fold_in(keys[9], 71), 0)
    page_store = draw_page_store(jax.random.fold_in(keys[9], 71), 0)
    page_owner = draw_page_owner(jax.random.fold_in(keys[9], 71), 0)
    page_slot = draw_page_slot(jax.random.fold_in(keys[9], 71), 0)
    lengths = uneven(keys[5], REQS, REQS * SLEN // 2, SLEN, 2).astype(jnp.int32)
    request_perm = jax.random.permutation(keys[6], REQS).astype(jnp.int32)
    w_out = draw_w_out(jax.random.fold_in(keys[9], 71), 0)
    post_gain = jnp.clip(1.0 + 0.15 * jax.random.normal(keys[8], (D,), jnp.float32), 0.25, 1.75)
    return {"hidden": hidden, "qkv": qkv, "page_store": page_store, "page_owner": page_owner, "page_slot": page_slot, "lengths": lengths, "request_perm": request_perm, "w_out": w_out, "post_gain": post_gain}


EPSILON = 1e-06
SOFT_CAP = 50.0

def tables(positions, width):
    half_width = width // 2
    frequency = 10000.0 ** (-(jnp.arange(half_width, dtype=jnp.float32) * 2.0 / width))
    angles = positions.astype(jnp.float32)[:, None] * frequency[None, :]
    return (jnp.cos(angles), jnp.sin(angles))

def rotate(values, cosine, sine):
    half_width = values.shape[-1] // 2
    first = values[..., :half_width]
    second = values[..., half_width:]
    return jnp.concatenate([first * cosine - second * sine, second * cosine + first * sine], -1)

def reference(hidden, qkv, page_store, page_owner, page_slot, lengths, request_perm, w_out, post_gain):
    per_group = H // KVH
    prefix_len = PAGES * PAGE
    chosen = page_store[page_owner * SLOT_DEV + page_slot].reshape(prefix_len, KVH, 2 * HD)
    prefix_keys = chosen[:, :, :HD].astype(jnp.float32)
    prefix_values = chosen[:, :, HD:].astype(jnp.float32)
    slot_lengths = lengths[request_perm]
    positions = prefix_len + jnp.arange(SLEN, dtype=jnp.int32)
    cosine, sine = tables(positions, HD)
    query_pos = jnp.arange(SLEN, dtype=jnp.int32)
    key_pos = jnp.arange(prefix_len + SLEN, dtype=jnp.int32)

    def one_request(inputs):
        rows_in, projections_in, length_now = inputs
        source = rows_in.astype(jnp.float32)
        projections = projections_in.astype(jnp.float32).reshape(SLEN, KVH, per_group + 2, HD)
        queries = (rotate(projections[:, :, :per_group], cosine[:, None, None, :], sine[:, None, None, :]) * HD ** (-0.5)).astype(jnp.bfloat16)
        fresh_keys = rotate(projections[:, :, per_group], cosine[:, None, :], sine[:, None, :]).astype(jnp.bfloat16)
        fresh_values = projections[:, :, per_group + 1].astype(jnp.bfloat16)
        all_keys = jnp.concatenate([prefix_keys, fresh_keys.astype(jnp.float32)], 0)
        all_values = jnp.concatenate([prefix_values, fresh_values.astype(jnp.float32)], 0)
        scores = jnp.einsum('sgqh,tgh->sgqt', queries.astype(jnp.float32), all_keys)
        capped = SOFT_CAP * jnp.tanh(scores / SOFT_CAP)
        suffix_pos = key_pos[None, :] - prefix_len
        allowed = (key_pos[None, :] < prefix_len) | (suffix_pos <= query_pos[:, None]) & (suffix_pos < length_now)
        weights_raw = jnp.where(allowed[:, None, None, :], jnp.exp(capped), 0.0)
        weights = (weights_raw / lax.optimization_barrier(jnp.sum(weights_raw, -1, keepdims=True))).astype(jnp.bfloat16)
        attended = jnp.einsum('sgqt,tgh->sgqh', weights.astype(jnp.float32), all_values).astype(jnp.bfloat16).reshape(SLEN, H * HD)
        projected = jnp.dot(attended, w_out, preferred_element_type=jnp.float32)
        branch = projected * lax.rsqrt(lax.optimization_barrier(jnp.mean(projected * projected, -1, keepdims=True)) + EPSILON) * post_gain
        live_mask = (query_pos < length_now).astype(jnp.float32)
        return ((source + branch) * live_mask[:, None]).astype(jnp.bfloat16)
    return lax.map(one_request, (hidden, qkv, slot_lengths))
```

```python
import jax
import jax.numpy as jnp
from jax import lax
from jax.sharding import PartitionSpec as P

D = 2304
HD = 256


EPSILON = 1e-06
SOFT_CAP = 50.0


def tables(positions, width):
    half_width = width // 2
    frequency = 10000.0 ** (-(jnp.arange(half_width, dtype=jnp.float32) * 2.0 / width))
    angles = positions.astype(jnp.float32)[:, None] * frequency[None, :]
    return (jnp.cos(angles), jnp.sin(angles))


def rotate(values, cosine, sine):
    half_width = values.shape[-1] // 2
    first = values[..., :half_width]
    second = values[..., half_width:]
    return jnp.concatenate([first * cosine - second * sine, second * cosine + first * sine], -1)


def capped_exp(scores):
    return jnp.exp(SOFT_CAP * jnp.tanh(scores / SOFT_CAP))


def shifted(value, axis, size, shift):
    return lax.ppermute(value, axis, [(i, (i + shift) % size) for i in range(size)])


def swapped(value, axis, size, mask):
    return lax.ppermute(value, axis, [(i, i ^ mask) for i in range(size)])


def gather_prefix(page_store, page_owner, page_slot, n_req):
    device_row = lax.axis_index("req")
    page_count = page_owner.shape[0]
    if n_req <= page_count:
        mine = page_owner == device_row
        slot = jnp.sum(jnp.where(mine, page_slot, 0))
        own = lax.dynamic_index_in_dim(page_store, slot, 0, keepdims=False)[:, 0]
        blocks = [own]
        sources = [device_row]
        for shift in range(1, n_req):
            blocks.append(shifted(own, "req", n_req, shift))
            sources.append((device_row - shift) % n_req)
        sources = jnp.stack(sources)
        valid = jnp.any(page_owner[None, :] == sources[:, None], 1)
        return jnp.stack(blocks), valid
    picked = page_store[page_slot][:, :, 0]
    held_here = page_owner == device_row
    offered = jnp.where(held_here[:, None, None], picked, jnp.zeros_like(picked))
    prefix = lax.psum(offered, "req")
    return prefix, jnp.ones((page_count,), jnp.bool_)


def on_device(
    hidden, qkv, page_store, page_owner, page_slot, lengths, request_perm, w_out, post_gain,
    *, n_req, n_tp
):
    requests, slots, local_width = hidden.shape
    per_group = qkv.shape[3] // HD - 2
    token_rows = requests * slots
    tp_index = lax.axis_index("tp")

    blocks, valid = gather_prefix(page_store, page_owner, page_slot, n_req)
    block_count, page_len = blocks.shape[0], blocks.shape[1]
    prefix_keys = blocks[:, :, :HD].reshape(block_count * page_len, HD)
    prefix_values = blocks[:, :, HD:].reshape(block_count * page_len, HD)
    key_valid = jnp.repeat(valid, page_len)

    device_row = lax.axis_index("req")
    my_requests = lax.dynamic_slice_in_dim(request_perm, device_row * requests, requests)
    matches = my_requests[:, None] == jnp.arange(lengths.shape[0], dtype=jnp.int32)[None, :]
    my_lengths = jnp.sum(jnp.where(matches, lengths[None, :], 0), 1)
    position = jnp.arange(slots, dtype=jnp.int32)
    live_mask = (position[None, :] < my_lengths[:, None]).astype(jnp.float32)

    projections = qkv[:, :, 0].astype(jnp.float32).reshape(requests, slots, per_group + 2, HD)
    prefix_len = page_store.shape[1] * page_owner.shape[0]
    cosine, sine = tables(prefix_len + position, HD)
    queries = (
        rotate(projections[:, :, :per_group], cosine[None, :, None, :], sine[None, :, None, :])
        * HD ** (-0.5)
    ).astype(jnp.bfloat16)
    fresh_keys = rotate(projections[:, :, per_group], cosine[None], sine[None]).astype(jnp.bfloat16)
    fresh_values = projections[:, :, per_group + 1].astype(jnp.bfloat16)

    prefix_weights = capped_exp(
        jnp.einsum("rsqh,th->rsqt", queries, prefix_keys, preferred_element_type=jnp.float32)
    )
    prefix_weights = jnp.where(key_valid[None, None, None, :], prefix_weights, 0.0)
    allowed = (position[None, None, :] <= position[None, :, None]) & (
        position[None, None, :] < my_lengths[:, None, None]
    )
    suffix_raw = capped_exp(
        jnp.einsum("rsqh,rth->rsqt", queries, fresh_keys, preferred_element_type=jnp.float32)
    )
    suffix_weights = jnp.where(allowed[:, :, None, :], suffix_raw, 0.0)
    totals = jnp.sum(prefix_weights, -1) + jnp.sum(suffix_weights, -1)
    prefix_probs = (prefix_weights / totals[..., None]).astype(jnp.bfloat16)
    suffix_probs = (suffix_weights / totals[..., None]).astype(jnp.bfloat16)
    attended = jnp.einsum(
        "rsqt,th->rsqh", prefix_probs, prefix_values, preferred_element_type=jnp.float32
    )
    attended = attended + jnp.einsum(
        "rsqt,rth->rsqh", suffix_probs, fresh_values, preferred_element_type=jnp.float32
    )
    own = attended.astype(jnp.bfloat16).reshape(token_rows, per_group * HD)

    group_width = per_group * HD
    w_blocks = w_out.reshape(n_tp, group_width, local_width)
    if n_tp == 4:
        near = swapped(own, "tp", n_tp, 1)
        far = swapped(own, "tp", n_tp, 2)
        farther = swapped(far, "tp", n_tp, 1)
        parts = [(own, tp_index), (near, tp_index ^ 1), (far, tp_index ^ 2), (farther, tp_index ^ 3)]
    else:
        parts = [(own, tp_index)]
        for shift in range(1, n_tp):
            parts.append((shifted(own, "tp", n_tp, shift), (tp_index - shift) % n_tp))
    projected = None
    for block, group in parts:
        rows = lax.dynamic_index_in_dim(w_blocks, group, 0, keepdims=False)
        term = jnp.dot(block, rows, preferred_element_type=jnp.float32)
        projected = term if projected is None else projected + term
    projected = projected.reshape(requests, slots, local_width)

    squares = jnp.sum(projected * projected, -1)
    branch_total = squares
    for shift in range(1, n_tp):
        branch_total = branch_total + shifted(squares, "tp", n_tp, shift)
    branch = projected * lax.rsqrt(branch_total / D + EPSILON)[..., None] * post_gain
    source = hidden.astype(jnp.float32)
    return ((source + branch) * live_mask[..., None]).astype(jnp.bfloat16)


def solution(mesh):
    placed = (
        P("req", None, "tp"),
        P("req", None, "tp", None),
        P("req", None, "tp", None),
        P(),
        P(),
        P(),
        P(),
        P(None, "tp"),
        P("tp"),
    )
    body = lambda *args: on_device(*args, n_req=mesh.shape["req"], n_tp=mesh.shape["tp"])
    return jax.shard_map(
        body, mesh=mesh, in_specs=placed, out_specs=P("req", None, "tp"), check_vma=False
    )
```

```python
import jax
import jax.numpy as jnp
from jax import lax
from jax.sharding import PartitionSpec as P

D = 2304
HD = 256


EPSILON = 1e-06
SOFT_CAP = 50.0


def tables(positions, width):
    half_width = width // 2
    frequency = 10000.0 ** (-(jnp.arange(half_width, dtype=jnp.float32) * 2.0 / width))
    angles = positions.astype(jnp.float32)[:, None] * frequency[None, :]
    return (jnp.cos(angles), jnp.sin(angles))


def rotate(values, cosine, sine):
    half_width = values.shape[-1] // 2
    first = values[..., :half_width]
    second = values[..., half_width:]
    return jnp.concatenate([first * cosine - second * sine, second * cosine + first * sine], -1)


def capped_exp(scores):
    return jnp.exp(SOFT_CAP * jnp.tanh(scores / SOFT_CAP))


def shifted(value, axis, size, shift):
    return lax.ppermute(value, axis, [(i, (i + shift) % size) for i in range(size)])


def swapped(value, axis, size, mask):
    return lax.ppermute(value, axis, [(i, i ^ mask) for i in range(size)])


def gather_prefix(page_store, page_owner, page_slot, n_req):
    device_row = lax.axis_index("req")
    page_count = page_owner.shape[0]
    if n_req <= page_count:
        mine = page_owner == device_row
        slot = jnp.sum(jnp.where(mine, page_slot, 0))
        own = lax.dynamic_index_in_dim(page_store, slot, 0, keepdims=False)[:, 0]
        blocks = [own]
        sources = [device_row]
        for shift in range(1, n_req):
            blocks.append(shifted(own, "req", n_req, shift))
            sources.append((device_row - shift) % n_req)
        sources = jnp.stack(sources)
        valid = jnp.any(page_owner[None, :] == sources[:, None], 1)
        return blocks, valid
    picked = page_store[page_slot][:, :, 0]
    held_here = page_owner == device_row
    offered = jnp.where(held_here[:, None, None], picked, jnp.zeros_like(picked))
    prefix = lax.psum(offered, "req")
    return [prefix[p] for p in range(page_count)], jnp.ones((page_count,), jnp.bool_)


def on_device(
    hidden, qkv, page_store, page_owner, page_slot, lengths, request_perm, w_out, post_gain,
    *, n_req, n_tp
):
    requests, slots, local_width = hidden.shape
    per_group = qkv.shape[3] // HD - 2
    token_rows = requests * slots
    tp_index = lax.axis_index("tp")

    blocks, valid = gather_prefix(page_store, page_owner, page_slot, n_req)

    device_row = lax.axis_index("req")
    my_requests = lax.dynamic_slice_in_dim(request_perm, device_row * requests, requests)
    matches = my_requests[:, None] == jnp.arange(lengths.shape[0], dtype=jnp.int32)[None, :]
    my_lengths = jnp.sum(jnp.where(matches, lengths[None, :], 0), 1)
    position = jnp.arange(slots, dtype=jnp.int32)
    live_mask = (position[None, :] < my_lengths[:, None]).astype(jnp.float32)

    projections = qkv[:, :, 0].astype(jnp.float32).reshape(requests, slots, per_group + 2, HD)
    prefix_len = page_store.shape[1] * page_owner.shape[0]
    cosine, sine = tables(prefix_len + position, HD)
    queries = (
        rotate(projections[:, :, :per_group], cosine[None, :, None, :], sine[None, :, None, :])
        * HD ** (-0.5)
    ).astype(jnp.bfloat16)
    fresh_keys = rotate(projections[:, :, per_group], cosine[None], sine[None]).astype(jnp.bfloat16)
    fresh_values = projections[:, :, per_group + 1].astype(jnp.bfloat16)

    allowed = (position[None, None, :] <= position[None, :, None]) & (
        position[None, None, :] < my_lengths[:, None, None]
    )
    suffix_raw = capped_exp(
        jnp.einsum("rsqh,rth->rsqt", queries, fresh_keys, preferred_element_type=jnp.float32)
    )
    suffix_weights = jnp.where(allowed[:, :, None, :], suffix_raw, 0.0)
    totals = jnp.sum(suffix_weights, -1)
    attended = jnp.einsum(
        "rsqt,rth->rsqh", suffix_weights.astype(jnp.bfloat16), fresh_values,
        preferred_element_type=jnp.float32,
    )
    for index, block in enumerate(blocks):
        raw = capped_exp(
            jnp.einsum("rsqh,th->rsqt", queries, block[:, :HD], preferred_element_type=jnp.float32)
        )
        weights = jnp.where(valid[index], raw, 0.0)
        totals = totals + jnp.sum(weights, -1)
        attended = attended + jnp.einsum(
            "rsqt,th->rsqh", weights.astype(jnp.bfloat16), block[:, HD:],
            preferred_element_type=jnp.float32,
        )
    attended = attended / totals[..., None]
    own = attended.astype(jnp.bfloat16).reshape(token_rows, per_group * HD)

    group_width = per_group * HD
    if n_tp == 4:
        near = swapped(own, "tp", n_tp, 1)
        far = swapped(own, "tp", n_tp, 2)
        farther = swapped(far, "tp", n_tp, 1)
        parts = [(own, tp_index), (near, tp_index ^ 1), (far, tp_index ^ 2), (farther, tp_index ^ 3)]
    else:
        parts = [(own, tp_index)]
        for shift in range(1, n_tp):
            parts.append((shifted(own, "tp", n_tp, shift), (tp_index - shift) % n_tp))
    projected = None
    for block, group in parts:
        rows = lax.dynamic_slice_in_dim(w_out, group * group_width, group_width, 0)
        term = jnp.dot(block, rows, preferred_element_type=jnp.float32)
        projected = term if projected is None else projected + term
    projected = projected.reshape(requests, slots, local_width)

    squares = jnp.sum(projected * projected, -1)
    branch_total = squares
    for shift in range(1, n_tp):
        branch_total = branch_total + shifted(squares, "tp", n_tp, shift)
    branch = projected * lax.rsqrt(branch_total / D + EPSILON)[..., None] * post_gain
    source = hidden.astype(jnp.float32)
    return ((source + branch) * live_mask[..., None]).astype(jnp.bfloat16)


def solution(mesh):
    placed = (
        P("req", None, "tp"),
        P("req", None, "tp", None),
        P("req", None, "tp", None),
        P(),
        P(),
        P(),
        P(),
        P(None, "tp"),
        P("tp"),
    )
    body = lambda *args: on_device(*args, n_req=mesh.shape["req"], n_tp=mesh.shape["tp"])
    return jax.shard_map(
        body, mesh=mesh, in_specs=placed, out_specs=P("req", None, "tp"), check_vma=False
    )
```

```python
import numpy as np
import jax
import jax.numpy as jnp
from jax import lax
from jax.experimental import pallas as pl
from jax.experimental.pallas import tpu as pltpu
from jax.sharding import PartitionSpec as P

D = 2304
HD = 256


EPSILON = 1e-06
SOFT_CAP = 50.0


def capped_exp(scores):
    return jnp.exp(SOFT_CAP * jnp.tanh(scores / SOFT_CAP))


def shifted(value, axis, size, shift):
    return lax.ppermute(value, axis, [(i, (i + shift) % size) for i in range(size)])


def swapped(value, axis, size, mask):
    return lax.ppermute(value, axis, [(i, i ^ mask) for i in range(size)])


def gather_prefix(page_store, page_owner, page_slot, n_req):
    device_row = lax.axis_index("req")
    page_count = page_owner.shape[0]
    if n_req <= page_count:
        mine = page_owner == device_row
        slot = jnp.sum(jnp.where(mine, page_slot, 0))
        own = lax.dynamic_index_in_dim(page_store, slot, 0, keepdims=False)[:, 0]
        blocks = [own]
        sources = [device_row]
        for shift in range(1, n_req):
            blocks.append(shifted(own, "req", n_req, shift))
            sources.append((device_row - shift) % n_req)
        sources = jnp.stack(sources)
        valid = jnp.any(page_owner[None, :] == sources[:, None], 1)
        return blocks, valid
    picked = page_store[page_slot][:, :, 0]
    held_here = page_owner == device_row
    offered = jnp.where(held_here[:, None, None], picked, jnp.zeros_like(picked))
    prefix = lax.psum(offered, "req")
    return [prefix[p] for p in range(page_count)], jnp.ones((page_count,), jnp.bool_)


def static_tables(positions, width):
    half_width = width // 2
    exponent = np.arange(half_width, dtype=np.float32) * np.float32(2.0) / np.float32(width)
    frequency = np.power(np.float32(10000.0), -exponent).astype(np.float32)
    angles = positions.astype(np.float32)[:, None] * frequency[None, :]
    return np.cos(angles).astype(np.float32), np.sin(angles).astype(np.float32)


def attention_kernel(length_ref, valid_ref, qkv_ref, cos_ref, sin_ref, *rest):
    page_refs, out_ref = rest[:-1], rest[-1]
    request = pl.program_id(0)
    slots = qkv_ref.shape[1]
    per_group = qkv_ref.shape[2] // HD - 2
    half = HD // 2
    cosine = cos_ref[...]
    sine = sin_ref[...]
    values_in = qkv_ref[0].astype(jnp.float32)

    def rope(part):
        first = part[:, :half]
        second = part[:, half:]
        return jnp.concatenate([first * cosine - second * sine, second * cosine + first * sine], -1)

    queries = jnp.concatenate(
        [(rope(values_in[:, q * HD:(q + 1) * HD]) * HD ** (-0.5)).astype(jnp.bfloat16)
         for q in range(per_group)], 0)
    fresh_keys = rope(values_in[:, per_group * HD:(per_group + 1) * HD]).astype(jnp.bfloat16)
    fresh_values = values_in[:, (per_group + 1) * HD:].astype(jnp.bfloat16)
    pages = [ref[...] for ref in page_refs]
    keys = jnp.concatenate([page[:, :HD] for page in pages] + [fresh_keys], 0)
    values = jnp.concatenate([page[:, HD:] for page in pages] + [fresh_values], 0)
    prefix_len = len(pages) * pages[0].shape[0]
    key_count = keys.shape[0]
    rows = queries.shape[0]

    scores = lax.dot_general(queries, keys, (((1,), (1,)), ((), ())),
                             preferred_element_type=jnp.float32)
    page_column = lax.broadcasted_iota(jnp.int32, (1, key_count), 1) // pages[0].shape[0]
    page_flag = jnp.zeros((1, key_count), jnp.int32)
    for index in range(len(pages)):
        page_flag = page_flag + jnp.where(page_column == index, valid_ref[index], 0)
    page_flag = page_flag.astype(jnp.float32)
    column = lax.broadcasted_iota(jnp.int32, (rows, key_count), 1)
    slot = lax.broadcasted_iota(jnp.int32, (rows, key_count), 0) % slots
    suffix_pos = column - prefix_len
    suffix_ok = (suffix_pos >= 0) & (suffix_pos <= slot) & (suffix_pos < length_ref[request])
    exps = capped_exp(scores)
    raw = jnp.where(suffix_ok, exps, jnp.where(column < prefix_len, exps * page_flag, 0.0))
    totals = jnp.sum(raw, -1, keepdims=True)
    weights = (raw / totals).astype(jnp.bfloat16)
    attended = jnp.dot(weights, values, preferred_element_type=jnp.float32).astype(jnp.bfloat16)
    out_ref[0] = jnp.concatenate(
        [attended[q * slots:(q + 1) * slots] for q in range(per_group)], 1)


def attend(qkv, cosine, sine, blocks, lengths, valid):
    requests, slots, width = qkv.shape
    per_group = width // HD - 2
    page_len, page_width = blocks[0].shape
    full = lambda shape: pl.BlockSpec(shape, lambda r, *_: (0,) * len(shape))
    grid_spec = pltpu.PrefetchScalarGridSpec(
        num_scalar_prefetch=2,
        grid=(requests,),
        in_specs=[pl.BlockSpec((1, slots, width), lambda r, *_: (r, 0, 0)),
                  full(cosine.shape), full(sine.shape)]
                 + [full((page_len, page_width)) for _ in blocks],
        out_specs=pl.BlockSpec((1, slots, per_group * HD), lambda r, *_: (r, 0, 0)),
    )
    return pl.pallas_call(
        attention_kernel,
        grid_spec=grid_spec,
        out_shape=jax.ShapeDtypeStruct((requests, slots, per_group * HD), jnp.bfloat16),
    )(lengths, valid, qkv, cosine, sine, *blocks)


def on_device(
    hidden, qkv, page_store, page_owner, page_slot, lengths, request_perm, w_out, post_gain,
    *, n_req, n_tp
):
    requests, slots, local_width = hidden.shape
    per_group = qkv.shape[3] // HD - 2
    token_rows = requests * slots
    tp_index = lax.axis_index("tp")

    blocks, valid = gather_prefix(page_store, page_owner, page_slot, n_req)

    device_row = lax.axis_index("req")
    my_requests = lax.dynamic_slice_in_dim(request_perm, device_row * requests, requests)
    matches = my_requests[:, None] == jnp.arange(lengths.shape[0], dtype=jnp.int32)[None, :]
    my_lengths = jnp.sum(jnp.where(matches, lengths[None, :], 0), 1)
    position = jnp.arange(slots, dtype=jnp.int32)
    live_mask = (position[None, :] < my_lengths[:, None]).astype(jnp.float32)

    prefix_len = page_store.shape[1] * page_owner.shape[0]
    cosine, sine = static_tables(prefix_len + np.arange(slots), HD)
    attended = attend(qkv[:, :, 0], jnp.asarray(cosine), jnp.asarray(sine), blocks,
                      my_lengths, valid.astype(jnp.int32))
    own = attended.reshape(token_rows, per_group * HD)

    group_width = per_group * HD
    if n_tp == 4:
        near = swapped(own, "tp", n_tp, 1)
        far = swapped(own, "tp", n_tp, 2)
        farther = swapped(far, "tp", n_tp, 1)
        parts = [(own, tp_index), (near, tp_index ^ 1), (far, tp_index ^ 2), (farther, tp_index ^ 3)]
    else:
        parts = [(own, tp_index)]
        for shift in range(1, n_tp):
            parts.append((shifted(own, "tp", n_tp, shift), (tp_index - shift) % n_tp))
    projected = None
    for block, group in parts:
        rows = lax.dynamic_slice_in_dim(w_out, group * group_width, group_width, 0)
        term = jnp.dot(block, rows, preferred_element_type=jnp.float32)
        projected = term if projected is None else projected + term
    projected = projected.reshape(requests, slots, local_width)

    squares = jnp.sum(projected * projected, -1)
    branch_total = squares
    for shift in range(1, n_tp):
        branch_total = branch_total + shifted(squares, "tp", n_tp, shift)
    branch = projected * lax.rsqrt(branch_total / D + EPSILON)[..., None] * post_gain
    source = hidden.astype(jnp.float32)
    return ((source + branch) * live_mask[..., None]).astype(jnp.bfloat16)


def solution(mesh):
    placed = (
        P("req", None, "tp"),
        P("req", None, "tp", None),
        P("req", None, "tp", None),
        P(),
        P(),
        P(),
        P(),
        P(None, "tp"),
        P("tp"),
    )
    body = lambda *args: on_device(*args, n_req=mesh.shape["req"], n_tp=mesh.shape["tp"])
    return jax.shard_map(
        body, mesh=mesh, in_specs=placed, out_specs=P("req", None, "tp"), check_vma=False
    )
```

```python
import numpy as np
import jax
import jax.numpy as jnp
from jax import lax
from jax.experimental import pallas as pl
from jax.experimental.pallas import tpu as pltpu
from jax.sharding import PartitionSpec as P

D = 2304
HD = 256


EPSILON = 1e-06
SOFT_CAP = 50.0


def capped_exp(scores):
    return jnp.exp(SOFT_CAP * jnp.tanh(scores / SOFT_CAP))


def shifted(value, axis, size, shift):
    return lax.ppermute(value, axis, [(i, (i + shift) % size) for i in range(size)])


def swapped(value, axis, size, mask):
    return lax.ppermute(value, axis, [(i, i ^ mask) for i in range(size)])


def gather_prefix(page_store, page_owner, page_slot, n_req):
    device_row = lax.axis_index("req")
    page_count = page_owner.shape[0]
    if n_req <= page_count:
        mine = page_owner == device_row
        slot = jnp.sum(jnp.where(mine, page_slot, 0))
        own = lax.dynamic_index_in_dim(page_store, slot, 0, keepdims=False)[:, 0]
        blocks = [own]
        sources = [device_row]
        for shift in range(1, n_req):
            blocks.append(shifted(own, "req", n_req, shift))
            sources.append((device_row - shift) % n_req)
        sources = jnp.stack(sources)
        valid = jnp.any(page_owner[None, :] == sources[:, None], 1)
        return blocks, valid
    picked = page_store[page_slot][:, :, 0]
    held_here = page_owner == device_row
    offered = jnp.where(held_here[:, None, None], picked, jnp.zeros_like(picked))
    prefix = lax.psum(offered, "req")
    return [prefix[p] for p in range(page_count)], jnp.ones((page_count,), jnp.bool_)


def static_tables(positions, width):
    half_width = width // 2
    exponent = np.arange(half_width, dtype=np.float32) * np.float32(2.0) / np.float32(width)
    frequency = np.power(np.float32(10000.0), -exponent).astype(np.float32)
    angles = positions.astype(np.float32)[:, None] * frequency[None, :]
    return np.cos(angles).astype(np.float32), np.sin(angles).astype(np.float32)


def attention_kernel(length_ref, valid_ref, qkv_ref, cos_ref, sin_ref, *rest):
    page_refs, out_ref = rest[:-1], rest[-1]
    request = pl.program_id(0)
    slots = qkv_ref.shape[1]
    per_group = qkv_ref.shape[2] // HD - 2
    half = HD // 2
    cosine = cos_ref[...]
    sine = sin_ref[...]
    values_in = qkv_ref[0].astype(jnp.float32)

    def rope(part):
        first = part[:, :half]
        second = part[:, half:]
        return jnp.concatenate([first * cosine - second * sine, second * cosine + first * sine], -1)

    queries = jnp.concatenate(
        [(rope(values_in[:, q * HD:(q + 1) * HD]) * HD ** (-0.5)).astype(jnp.bfloat16)
         for q in range(per_group)], 0)
    fresh_keys = rope(values_in[:, per_group * HD:(per_group + 1) * HD]).astype(jnp.bfloat16)
    fresh_values = values_in[:, (per_group + 1) * HD:].astype(jnp.bfloat16)
    pages = [ref[...] for ref in page_refs]
    keys = jnp.concatenate([page[:, :HD] for page in pages] + [fresh_keys], 0)
    values = jnp.concatenate([page[:, HD:] for page in pages] + [fresh_values], 0)
    prefix_len = len(pages) * pages[0].shape[0]
    key_count = keys.shape[0]
    rows = queries.shape[0]

    scores = lax.dot_general(queries, keys, (((1,), (1,)), ((), ())),
                             preferred_element_type=jnp.float32)
    page_column = lax.broadcasted_iota(jnp.int32, (1, key_count), 1) // pages[0].shape[0]
    page_flag = jnp.zeros((1, key_count), jnp.int32)
    for index in range(len(pages)):
        page_flag = page_flag + jnp.where(page_column == index, valid_ref[index], 0)
    page_flag = page_flag.astype(jnp.float32)
    column = lax.broadcasted_iota(jnp.int32, (rows, key_count), 1)
    slot = lax.broadcasted_iota(jnp.int32, (rows, key_count), 0) % slots
    suffix_pos = column - prefix_len
    suffix_ok = (suffix_pos >= 0) & (suffix_pos <= slot) & (suffix_pos < length_ref[request])
    exps = capped_exp(scores)
    raw = jnp.where(suffix_ok, exps, jnp.where(column < prefix_len, exps * page_flag, 0.0))
    totals = jnp.sum(raw, -1, keepdims=True)
    weights = (raw / totals).astype(jnp.bfloat16)
    attended = jnp.dot(weights, values, preferred_element_type=jnp.float32).astype(jnp.bfloat16)
    out_ref[0] = jnp.concatenate(
        [attended[q * slots:(q + 1) * slots] for q in range(per_group)], 1)


def attend(qkv, cosine, sine, blocks, lengths, valid):
    requests, slots, width = qkv.shape
    per_group = width // HD - 2
    page_len, page_width = blocks[0].shape
    full = lambda shape: pl.BlockSpec(shape, lambda r, *_: (0,) * len(shape))
    grid_spec = pltpu.PrefetchScalarGridSpec(
        num_scalar_prefetch=2,
        grid=(requests,),
        in_specs=[pl.BlockSpec((1, slots, width), lambda r, *_: (r, 0, 0)),
                  full(cosine.shape), full(sine.shape)]
                 + [full((page_len, page_width)) for _ in blocks],
        out_specs=pl.BlockSpec((1, slots, per_group * HD), lambda r, *_: (r, 0, 0)),
    )
    return pl.pallas_call(
        attention_kernel,
        grid_spec=grid_spec,
        out_shape=jax.ShapeDtypeStruct((requests, slots, per_group * HD), jnp.bfloat16),
    )(lengths, valid, qkv, cosine, sine, *blocks)


def project(own, w_out, tp_index, n_tp, group_width):
    if n_tp == 4:
        near = swapped(own, "tp", n_tp, 1)
        far = swapped(own, "tp", n_tp, 2)
        farther = swapped(far, "tp", n_tp, 1)
        parts = [(own, tp_index), (near, tp_index ^ 1), (far, tp_index ^ 2), (farther, tp_index ^ 3)]
    else:
        parts = [(own, tp_index)]
        for shift in range(1, n_tp):
            parts.append((shifted(own, "tp", n_tp, shift), (tp_index - shift) % n_tp))
    projected = None
    for block, group in parts:
        rows = lax.dynamic_slice_in_dim(w_out, group * group_width, group_width, 0)
        term = jnp.dot(block, rows, preferred_element_type=jnp.float32)
        projected = term if projected is None else projected + term
    return projected


def on_device(
    hidden, qkv, page_store, page_owner, page_slot, lengths, request_perm, w_out, post_gain,
    *, n_req, n_tp
):
    requests, slots, local_width = hidden.shape
    per_group = qkv.shape[3] // HD - 2
    token_rows = requests * slots
    tp_index = lax.axis_index("tp")

    blocks, valid = gather_prefix(page_store, page_owner, page_slot, n_req)

    device_row = lax.axis_index("req")
    my_requests = lax.dynamic_slice_in_dim(request_perm, device_row * requests, requests)
    matches = my_requests[:, None] == jnp.arange(lengths.shape[0], dtype=jnp.int32)[None, :]
    my_lengths = jnp.sum(jnp.where(matches, lengths[None, :], 0), 1)
    position = jnp.arange(slots, dtype=jnp.int32)
    live_mask = (position[None, :] < my_lengths[:, None]).astype(jnp.float32)

    prefix_len = page_store.shape[1] * page_owner.shape[0]
    cosine, sine = static_tables(prefix_len + np.arange(slots), HD)
    group_width = per_group * HD
    chunk = max(1, requests // 2)
    projected_parts = []
    for start in range(0, requests, chunk):
        attended = attend(qkv[start:start + chunk, :, 0], jnp.asarray(cosine), jnp.asarray(sine),
                          blocks, my_lengths[start:start + chunk], valid.astype(jnp.int32))
        own = attended.reshape(chunk * slots, per_group * HD)
        projected_parts.append(project(own, w_out, tp_index, n_tp, group_width))
    projected = jnp.concatenate(projected_parts, 0).reshape(requests, slots, local_width)

    squares = jnp.sum(projected * projected, -1)
    branch_total = squares
    for shift in range(1, n_tp):
        branch_total = branch_total + shifted(squares, "tp", n_tp, shift)
    branch = projected * lax.rsqrt(branch_total / D + EPSILON)[..., None] * post_gain
    source = hidden.astype(jnp.float32)
    return ((source + branch) * live_mask[..., None]).astype(jnp.bfloat16)


def solution(mesh):
    placed = (
        P("req", None, "tp"),
        P("req", None, "tp", None),
        P("req", None, "tp", None),
        P(),
        P(),
        P(),
        P(),
        P(None, "tp"),
        P("tp"),
    )
    body = lambda *args: on_device(*args, n_req=mesh.shape["req"], n_tp=mesh.shape["tp"])
    return jax.shard_map(
        body, mesh=mesh, in_specs=placed, out_specs=P("req", None, "tp"), check_vma=False
    )
```

```python
import numpy as np
import jax
import jax.numpy as jnp
from jax import lax
from jax.experimental import pallas as pl
from jax.experimental.pallas import tpu as pltpu
from jax.sharding import PartitionSpec as P

D = 2304
HD = 256


EPSILON = 1e-06
SOFT_CAP = 50.0


def capped_exp(scores):
    return jnp.exp(SOFT_CAP * jnp.tanh(scores / SOFT_CAP))


def shifted(value, axis, size, shift):
    return lax.ppermute(value, axis, [(i, (i + shift) % size) for i in range(size)])


def swapped(value, axis, size, mask):
    return lax.ppermute(value, axis, [(i, i ^ mask) for i in range(size)])


def gather_prefix(page_store, page_owner, page_slot, n_req):
    device_row = lax.axis_index("req")
    page_count = page_owner.shape[0]
    if n_req <= page_count:
        mine = page_owner == device_row
        slot = jnp.sum(jnp.where(mine, page_slot, 0))
        own = lax.dynamic_index_in_dim(page_store, slot, 0, keepdims=False)[:, 0]
        blocks = [own]
        sources = [device_row]
        if n_req == 8:
            for mask in (1, 2, 3, 6):
                blocks.append(swapped(own, "req", n_req, mask))
                sources.append(device_row ^ mask)
            mirror = blocks[-1]
            for mask in (1, 2, 3):
                blocks.append(swapped(mirror, "req", n_req, mask))
                sources.append(device_row ^ 6 ^ mask)
        else:
            for shift in range(1, n_req):
                blocks.append(shifted(own, "req", n_req, shift))
                sources.append((device_row - shift) % n_req)
        sources = jnp.stack(sources)
        valid = jnp.any(page_owner[None, :] == sources[:, None], 1)
        return blocks, valid
    picked = page_store[page_slot][:, :, 0]
    held_here = page_owner == device_row
    offered = jnp.where(held_here[:, None, None], picked, jnp.zeros_like(picked))
    prefix = lax.psum(offered, "req")
    return [prefix[p] for p in range(page_count)], jnp.ones((page_count,), jnp.bool_)


def static_tables(positions, width):
    half_width = width // 2
    exponent = np.arange(half_width, dtype=np.float32) * np.float32(2.0) / np.float32(width)
    frequency = np.power(np.float32(10000.0), -exponent).astype(np.float32)
    angles = positions.astype(np.float32)[:, None] * frequency[None, :]
    return np.cos(angles).astype(np.float32), np.sin(angles).astype(np.float32)


def attention_kernel(length_ref, valid_ref, qkv_ref, cos_ref, sin_ref, *rest):
    page_refs, out_ref = rest[:-1], rest[-1]
    request = pl.program_id(0)
    slots = qkv_ref.shape[1]
    per_group = qkv_ref.shape[2] // HD - 2
    half = HD // 2
    cosine = cos_ref[...]
    sine = sin_ref[...]
    values_in = qkv_ref[0].astype(jnp.float32)

    def rope(part):
        first = part[:, :half]
        second = part[:, half:]
        return jnp.concatenate([first * cosine - second * sine, second * cosine + first * sine], -1)

    queries = jnp.concatenate(
        [(rope(values_in[:, q * HD:(q + 1) * HD]) * HD ** (-0.5)).astype(jnp.bfloat16)
         for q in range(per_group)], 0)
    fresh_keys = rope(values_in[:, per_group * HD:(per_group + 1) * HD]).astype(jnp.bfloat16)
    fresh_values = values_in[:, (per_group + 1) * HD:].astype(jnp.bfloat16)
    pages = [ref[...] for ref in page_refs]
    keys = jnp.concatenate([page[:, :HD] for page in pages] + [fresh_keys], 0)
    values = jnp.concatenate([page[:, HD:] for page in pages] + [fresh_values], 0)
    prefix_len = len(pages) * pages[0].shape[0]
    key_count = keys.shape[0]
    rows = queries.shape[0]

    scores = lax.dot_general(queries, keys, (((1,), (1,)), ((), ())),
                             preferred_element_type=jnp.float32)
    page_column = lax.broadcasted_iota(jnp.int32, (1, key_count), 1) // pages[0].shape[0]
    page_flag = jnp.zeros((1, key_count), jnp.int32)
    for index in range(len(pages)):
        page_flag = page_flag + jnp.where(page_column == index, valid_ref[index], 0)
    page_flag = page_flag.astype(jnp.float32)
    column = lax.broadcasted_iota(jnp.int32, (rows, key_count), 1)
    slot = lax.broadcasted_iota(jnp.int32, (rows, key_count), 0) % slots
    suffix_pos = column - prefix_len
    suffix_ok = (suffix_pos >= 0) & (suffix_pos <= slot) & (suffix_pos < length_ref[request])
    exps = capped_exp(scores)
    raw = jnp.where(suffix_ok, exps, jnp.where(column < prefix_len, exps * page_flag, 0.0))
    totals = jnp.sum(raw, -1, keepdims=True)
    weights = (raw / totals).astype(jnp.bfloat16)
    attended = jnp.dot(weights, values, preferred_element_type=jnp.float32).astype(jnp.bfloat16)
    out_ref[0] = jnp.concatenate(
        [attended[q * slots:(q + 1) * slots] for q in range(per_group)], 1)


def attend(qkv, cosine, sine, blocks, lengths, valid):
    requests, slots, width = qkv.shape
    per_group = width // HD - 2
    page_len, page_width = blocks[0].shape
    full = lambda shape: pl.BlockSpec(shape, lambda r, *_: (0,) * len(shape))
    grid_spec = pltpu.PrefetchScalarGridSpec(
        num_scalar_prefetch=2,
        grid=(requests,),
        in_specs=[pl.BlockSpec((1, slots, width), lambda r, *_: (r, 0, 0)),
                  full(cosine.shape), full(sine.shape)]
                 + [full((page_len, page_width)) for _ in blocks],
        out_specs=pl.BlockSpec((1, slots, per_group * HD), lambda r, *_: (r, 0, 0)),
    )
    return pl.pallas_call(
        attention_kernel,
        grid_spec=grid_spec,
        out_shape=jax.ShapeDtypeStruct((requests, slots, per_group * HD), jnp.bfloat16),
    )(lengths, valid, qkv, cosine, sine, *blocks)


def project(own, w_out, tp_index, n_tp, group_width):
    if n_tp == 4:
        near = swapped(own, "tp", n_tp, 1)
        far = swapped(own, "tp", n_tp, 2)
        farther = swapped(far, "tp", n_tp, 1)
        parts = [(own, tp_index), (near, tp_index ^ 1), (far, tp_index ^ 2), (farther, tp_index ^ 3)]
    else:
        parts = [(own, tp_index)]
        for shift in range(1, n_tp):
            parts.append((shifted(own, "tp", n_tp, shift), (tp_index - shift) % n_tp))
    projected = None
    for block, group in parts:
        rows = lax.dynamic_slice_in_dim(w_out, group * group_width, group_width, 0)
        term = jnp.dot(block, rows, preferred_element_type=jnp.float32)
        projected = term if projected is None else projected + term
    return projected


def on_device(
    hidden, qkv, page_store, page_owner, page_slot, lengths, request_perm, w_out, post_gain,
    *, n_req, n_tp
):
    requests, slots, local_width = hidden.shape
    per_group = qkv.shape[3] // HD - 2
    token_rows = requests * slots
    tp_index = lax.axis_index("tp")

    blocks, valid = gather_prefix(page_store, page_owner, page_slot, n_req)

    device_row = lax.axis_index("req")
    my_requests = lax.dynamic_slice_in_dim(request_perm, device_row * requests, requests)
    matches = my_requests[:, None] == jnp.arange(lengths.shape[0], dtype=jnp.int32)[None, :]
    my_lengths = jnp.sum(jnp.where(matches, lengths[None, :], 0), 1)
    position = jnp.arange(slots, dtype=jnp.int32)
    live_mask = (position[None, :] < my_lengths[:, None]).astype(jnp.float32)

    prefix_len = page_store.shape[1] * page_owner.shape[0]
    cosine, sine = static_tables(prefix_len + np.arange(slots), HD)
    group_width = per_group * HD
    chunk = max(1, requests // 2)
    projected_parts = []
    for start in range(0, requests, chunk):
        attended = attend(qkv[start:start + chunk, :, 0], jnp.asarray(cosine), jnp.asarray(sine),
                          blocks, my_lengths[start:start + chunk], valid.astype(jnp.int32))
        own = attended.reshape(chunk * slots, per_group * HD)
        projected_parts.append(project(own, w_out, tp_index, n_tp, group_width))
    projected = jnp.concatenate(projected_parts, 0).reshape(requests, slots, local_width)

    squares = jnp.sum(projected * projected, -1)
    branch_total = squares
    for shift in range(1, n_tp):
        branch_total = branch_total + shifted(squares, "tp", n_tp, shift)
    branch = projected * lax.rsqrt(branch_total / D + EPSILON)[..., None] * post_gain
    source = hidden.astype(jnp.float32)
    return ((source + branch) * live_mask[..., None]).astype(jnp.bfloat16)


def solution(mesh):
    placed = (
        P("req", None, "tp"),
        P("req", None, "tp", None),
        P("req", None, "tp", None),
        P(),
        P(),
        P(),
        P(),
        P(None, "tp"),
        P("tp"),
    )
    body = lambda *args: on_device(*args, n_req=mesh.shape["req"], n_tp=mesh.shape["tp"])
    return jax.shard_map(
        body, mesh=mesh, in_specs=placed, out_specs=P("req", None, "tp"), check_vma=False
    )
```

```python
import functools

import numpy as np
import jax
import jax.numpy as jnp
from jax import lax
from jax.experimental import pallas as pl
from jax.experimental.pallas import tpu as pltpu
from jax.sharding import PartitionSpec as P

D = 2304
HD = 256


EPSILON = 1e-06
SOFT_CAP = 50.0


def capped_exp(scores):
    return jnp.exp(SOFT_CAP * jnp.tanh(scores / SOFT_CAP))


def shifted(value, axis, size, shift):
    return lax.ppermute(value, axis, [(i, (i + shift) % size) for i in range(size)])


def swapped(value, axis, size, mask):
    return lax.ppermute(value, axis, [(i, i ^ mask) for i in range(size)])


def gather_prefix(page_store, page_owner, page_slot, n_req):
    device_row = lax.axis_index("req")
    page_count = page_owner.shape[0]
    if n_req <= page_count:
        mine = page_owner == device_row
        slot = jnp.sum(jnp.where(mine, page_slot, 0))
        own = page_store[0, :, 0]
        for index in range(1, page_store.shape[0]):
            own = jnp.where(slot == index, page_store[index, :, 0], own)
        blocks = [own]
        sources = [device_row]
        if n_req == 8:
            for mask in (1, 2, 3, 6):
                blocks.append(swapped(own, "req", n_req, mask))
                sources.append(device_row ^ mask)
            mirror = blocks[-1]
            for mask in (1, 2, 3):
                blocks.append(swapped(mirror, "req", n_req, mask))
                sources.append(device_row ^ 6 ^ mask)
        else:
            for shift in range(1, n_req):
                blocks.append(shifted(own, "req", n_req, shift))
                sources.append((device_row - shift) % n_req)
        sources = jnp.stack(sources)
        valid = jnp.any(page_owner[None, :] == sources[:, None], 1)
        return blocks, valid
    picked = page_store[page_slot][:, :, 0]
    held_here = page_owner == device_row
    offered = jnp.where(held_here[:, None, None], picked, jnp.zeros_like(picked))
    prefix = lax.psum(offered, "req")
    return [prefix[p] for p in range(page_count)], jnp.ones((page_count,), jnp.bool_)


def static_tables(positions, width):
    half_width = width // 2
    exponent = np.arange(half_width, dtype=np.float32) * np.float32(2.0) / np.float32(width)
    frequency = np.power(np.float32(10000.0), -exponent).astype(np.float32)
    angles = positions.astype(np.float32)[:, None] * frequency[None, :]
    return np.cos(angles).astype(np.float32), np.sin(angles).astype(np.float32)


def attention_kernel(length_ref, valid_ref, qkv_ref, cos_ref, sin_ref, *rest, offset):
    page_refs, out_ref = rest[:-1], rest[-1]
    request = pl.program_id(0) + offset
    slots = qkv_ref.shape[1]
    per_group = qkv_ref.shape[2] // HD - 2
    half = HD // 2
    cosine = cos_ref[...]
    sine = sin_ref[...]
    values_in = qkv_ref[0].astype(jnp.float32)

    def rope(part):
        first = part[:, :half]
        second = part[:, half:]
        return jnp.concatenate([first * cosine - second * sine, second * cosine + first * sine], -1)

    queries = jnp.concatenate(
        [(rope(values_in[:, q * HD:(q + 1) * HD]) * HD ** (-0.5)).astype(jnp.bfloat16)
         for q in range(per_group)], 0)
    fresh_keys = rope(values_in[:, per_group * HD:(per_group + 1) * HD]).astype(jnp.bfloat16)
    fresh_values = values_in[:, (per_group + 1) * HD:].astype(jnp.bfloat16)
    pages = [ref[...] for ref in page_refs]
    keys = jnp.concatenate([page[:, :HD] for page in pages] + [fresh_keys], 0)
    values = jnp.concatenate([page[:, HD:] for page in pages] + [fresh_values], 0)
    prefix_len = len(pages) * pages[0].shape[0]
    key_count = keys.shape[0]
    rows = queries.shape[0]

    scores = lax.dot_general(queries, keys, (((1,), (1,)), ((), ())),
                             preferred_element_type=jnp.float32)
    page_column = lax.broadcasted_iota(jnp.int32, (1, key_count), 1) // pages[0].shape[0]
    page_flag = jnp.zeros((1, key_count), jnp.int32)
    for index in range(len(pages)):
        page_flag = page_flag + jnp.where(page_column == index, valid_ref[index], 0)
    page_flag = page_flag.astype(jnp.float32)
    column = lax.broadcasted_iota(jnp.int32, (rows, key_count), 1)
    slot = lax.broadcasted_iota(jnp.int32, (rows, key_count), 0) % slots
    suffix_pos = column - prefix_len
    suffix_ok = (suffix_pos >= 0) & (suffix_pos <= slot) & (suffix_pos < length_ref[request])
    exps = capped_exp(scores)
    raw = jnp.where(suffix_ok, exps, jnp.where(column < prefix_len, exps * page_flag, 0.0))
    totals = jnp.sum(raw, -1, keepdims=True)
    weights = (raw / totals).astype(jnp.bfloat16)
    attended = jnp.dot(weights, values, preferred_element_type=jnp.float32).astype(jnp.bfloat16)
    out_ref[0] = jnp.concatenate(
        [attended[q * slots:(q + 1) * slots] for q in range(per_group)], 1)


def attend(qkv, cosine, sine, blocks, lengths, valid, offset, count):
    _, slots, width = qkv.shape
    per_group = width // HD - 2
    page_len, page_width = blocks[0].shape
    full = lambda shape: pl.BlockSpec(shape, lambda r, *_: (0,) * len(shape))
    grid_spec = pltpu.PrefetchScalarGridSpec(
        num_scalar_prefetch=2,
        grid=(count,),
        in_specs=[pl.BlockSpec((1, slots, width), lambda r, *_: (r + offset, 0, 0)),
                  full(cosine.shape), full(sine.shape)]
                 + [full((page_len, page_width)) for _ in blocks],
        out_specs=pl.BlockSpec((1, slots, per_group * HD), lambda r, *_: (r, 0, 0)),
    )
    return pl.pallas_call(
        functools.partial(attention_kernel, offset=offset),
        grid_spec=grid_spec,
        out_shape=jax.ShapeDtypeStruct((count, slots, per_group * HD), jnp.bfloat16),
    )(lengths, valid, qkv, cosine, sine, *blocks)

def project(own, w_out, tp_index, n_tp, group_width):
    if n_tp == 4:
        near = swapped(own, "tp", n_tp, 1)
        far = swapped(own, "tp", n_tp, 2)
        farther = swapped(far, "tp", n_tp, 1)
        parts = [(own, tp_index), (near, tp_index ^ 1), (far, tp_index ^ 2), (farther, tp_index ^ 3)]
    else:
        parts = [(own, tp_index)]
        for shift in range(1, n_tp):
            parts.append((shifted(own, "tp", n_tp, shift), (tp_index - shift) % n_tp))
    projected = None
    for block, group in parts:
        rows = lax.dynamic_slice_in_dim(w_out, group * group_width, group_width, 0)
        term = jnp.dot(block, rows, preferred_element_type=jnp.float32)
        projected = term if projected is None else projected + term
    return projected


def on_device(
    hidden, qkv, page_store, page_owner, page_slot, lengths, request_perm, w_out, post_gain,
    *, n_req, n_tp
):
    requests, slots, local_width = hidden.shape
    per_group = qkv.shape[3] // HD - 2
    token_rows = requests * slots
    tp_index = lax.axis_index("tp")

    blocks, valid = gather_prefix(page_store, page_owner, page_slot, n_req)

    device_row = lax.axis_index("req")
    my_requests = lax.dynamic_slice_in_dim(request_perm, device_row * requests, requests)
    matches = my_requests[:, None] == jnp.arange(lengths.shape[0], dtype=jnp.int32)[None, :]
    my_lengths = jnp.sum(jnp.where(matches, lengths[None, :], 0), 1)
    position = jnp.arange(slots, dtype=jnp.int32)
    live_mask = (position[None, :] < my_lengths[:, None]).astype(jnp.float32)

    prefix_len = page_store.shape[1] * page_owner.shape[0]
    cosine, sine = static_tables(prefix_len + np.arange(slots), HD)
    group_width = per_group * HD
    chunk = max(1, requests // 2)
    projected_parts = []
    for start in range(0, requests, chunk):
        attended = attend(qkv[:, :, 0], jnp.asarray(cosine), jnp.asarray(sine), blocks,
                          my_lengths, valid.astype(jnp.int32), start, chunk)
        own = attended.reshape(chunk * slots, per_group * HD)
        projected_parts.append(project(own, w_out, tp_index, n_tp, group_width))
    projected = jnp.concatenate(projected_parts, 0).reshape(requests, slots, local_width)

    squares = jnp.sum(projected * projected, -1)
    branch_total = squares
    for shift in range(1, n_tp):
        branch_total = branch_total + shifted(squares, "tp", n_tp, shift)
    branch = projected * lax.rsqrt(branch_total / D + EPSILON)[..., None] * post_gain
    source = hidden.astype(jnp.float32)
    return ((source + branch) * live_mask[..., None]).astype(jnp.bfloat16)


def solution(mesh):
    placed = (
        P("req", None, "tp"),
        P("req", None, "tp", None),
        P("req", None, "tp", None),
        P(),
        P(),
        P(),
        P(),
        P(None, "tp"),
        P("tp"),
    )
    body = lambda *args: on_device(*args, n_req=mesh.shape["req"], n_tp=mesh.shape["tp"])
    return jax.shard_map(
        body, mesh=mesh, in_specs=placed, out_specs=P("req", None, "tp"), check_vma=False
    )
```

```python
import functools

import numpy as np
import jax
import jax.numpy as jnp
from jax import lax
from jax.experimental import pallas as pl
from jax.experimental.pallas import tpu as pltpu
from jax.sharding import PartitionSpec as P

D = 2304
HD = 256


EPSILON = 1e-06
SOFT_CAP = 50.0


def capped_exp(scores):
    return jnp.exp(SOFT_CAP * jnp.tanh(scores / SOFT_CAP))


def shifted(value, axis, size, shift):
    return lax.ppermute(value, axis, [(i, (i + shift) % size) for i in range(size)])


def swapped(value, axis, size, mask):
    return lax.ppermute(value, axis, [(i, i ^ mask) for i in range(size)])


def gather_prefix(page_store, page_owner, page_slot, n_req):
    device_row = lax.axis_index("req")
    page_count = page_owner.shape[0]
    if n_req <= page_count:
        mine = page_owner == device_row
        slot = jnp.sum(jnp.where(mine, page_slot, 0))
        own = page_store[0, :, 0]
        for index in range(1, page_store.shape[0]):
            own = jnp.where(slot == index, page_store[index, :, 0], own)
        blocks = [own]
        sources = [device_row]
        if n_req == 8:
            for mask in (1, 2, 3, 6):
                blocks.append(swapped(own, "req", n_req, mask))
                sources.append(device_row ^ mask)
            mirror = blocks[-1]
            for mask in (1, 2, 3):
                blocks.append(swapped(mirror, "req", n_req, mask))
                sources.append(device_row ^ 6 ^ mask)
        else:
            for shift in range(1, n_req):
                blocks.append(shifted(own, "req", n_req, shift))
                sources.append((device_row - shift) % n_req)
        sources = jnp.stack(sources)
        valid = jnp.any(page_owner[None, :] == sources[:, None], 1)
        return blocks, valid
    picked = page_store[page_slot][:, :, 0]
    held_here = page_owner == device_row
    offered = jnp.where(held_here[:, None, None], picked, jnp.zeros_like(picked))
    prefix = lax.psum(offered, "req")
    return [prefix[p] for p in range(page_count)], jnp.ones((page_count,), jnp.bool_)


def static_tables(positions, width):
    half_width = width // 2
    exponent = np.arange(half_width, dtype=np.float32) * np.float32(2.0) / np.float32(width)
    frequency = np.power(np.float32(10000.0), -exponent).astype(np.float32)
    angles = positions.astype(np.float32)[:, None] * frequency[None, :]
    return np.cos(angles).astype(np.float32), np.sin(angles).astype(np.float32)


def attention_kernel(length_ref, valid_ref, qkv_ref, cos_ref, sin_ref, *rest, offset):
    page_refs, out_ref = rest[:-1], rest[-1]
    request = pl.program_id(0) + offset
    slots = qkv_ref.shape[1]
    per_group = qkv_ref.shape[2] // HD - 2
    half = HD // 2
    cosine = cos_ref[...]
    sine = sin_ref[...]
    values_in = qkv_ref[0].astype(jnp.float32)

    def rope(part):
        first = part[:, :half]
        second = part[:, half:]
        return jnp.concatenate([first * cosine - second * sine, second * cosine + first * sine], -1)

    queries = jnp.concatenate(
        [(rope(values_in[:, q * HD:(q + 1) * HD]) * HD ** (-0.5)).astype(jnp.bfloat16)
         for q in range(per_group)], 0)
    fresh_keys = rope(values_in[:, per_group * HD:(per_group + 1) * HD]).astype(jnp.bfloat16)
    fresh_values = values_in[:, (per_group + 1) * HD:].astype(jnp.bfloat16)
    pages = [ref[...] for ref in page_refs]
    keys = jnp.concatenate([page[:, :HD] for page in pages] + [fresh_keys], 0)
    values = jnp.concatenate([page[:, HD:] for page in pages] + [fresh_values], 0)
    prefix_len = len(pages) * pages[0].shape[0]
    key_count = keys.shape[0]
    rows = queries.shape[0]

    scores = lax.dot_general(queries, keys, (((1,), (1,)), ((), ())),
                             preferred_element_type=jnp.float32)
    page_column = lax.broadcasted_iota(jnp.int32, (1, key_count), 1) // pages[0].shape[0]
    page_flag = jnp.zeros((1, key_count), jnp.int32)
    for index in range(len(pages)):
        page_flag = page_flag + jnp.where(page_column == index, valid_ref[index], 0)
    page_flag = page_flag.astype(jnp.float32)
    column = lax.broadcasted_iota(jnp.int32, (rows, key_count), 1)
    slot = lax.broadcasted_iota(jnp.int32, (rows, key_count), 0) % slots
    suffix_pos = column - prefix_len
    suffix_ok = (suffix_pos >= 0) & (suffix_pos <= slot) & (suffix_pos < length_ref[request])
    exps = capped_exp(scores)
    raw = jnp.where(suffix_ok, exps, jnp.where(column < prefix_len, exps * page_flag, 0.0))
    totals = jnp.sum(raw, -1, keepdims=True)
    weights = (raw / totals).astype(jnp.bfloat16)
    attended = jnp.dot(weights, values, preferred_element_type=jnp.float32).astype(jnp.bfloat16)
    out_ref[0] = jnp.concatenate(
        [attended[q * slots:(q + 1) * slots] for q in range(per_group)], 1)


def attend(qkv, cosine, sine, blocks, lengths, valid, offset, count):
    _, slots, width = qkv.shape
    per_group = width // HD - 2
    page_len, page_width = blocks[0].shape
    full = lambda shape: pl.BlockSpec(shape, lambda r, *_: (0,) * len(shape))
    grid_spec = pltpu.PrefetchScalarGridSpec(
        num_scalar_prefetch=2,
        grid=(count,),
        in_specs=[pl.BlockSpec((1, slots, width), lambda r, *_: (r + offset, 0, 0)),
                  full(cosine.shape), full(sine.shape)]
                 + [full((page_len, page_width)) for _ in blocks],
        out_specs=pl.BlockSpec((1, slots, per_group * HD), lambda r, *_: (r, 0, 0)),
    )
    return pl.pallas_call(
        functools.partial(attention_kernel, offset=offset),
        grid_spec=grid_spec,
        out_shape=jax.ShapeDtypeStruct((count, slots, per_group * HD), jnp.bfloat16),
    )(lengths, valid, qkv, cosine, sine, *blocks)

def project(own, w_out, tp_index, n_tp, group_width):
    if n_tp == 4:
        near = swapped(own, "tp", n_tp, 1)
        far = swapped(own, "tp", n_tp, 2)
        farther = swapped(far, "tp", n_tp, 1)
        parts = [(own, tp_index), (near, tp_index ^ 1), (far, tp_index ^ 2), (farther, tp_index ^ 3)]
    else:
        parts = [(own, tp_index)]
        for shift in range(1, n_tp):
            parts.append((shifted(own, "tp", n_tp, shift), (tp_index - shift) % n_tp))
    projected = None
    for block, group in parts:
        rows = lax.dynamic_slice_in_dim(w_out, group * group_width, group_width, 0)
        term = jnp.dot(block, rows, preferred_element_type=jnp.float32)
        projected = term if projected is None else projected + term
    return projected


def on_device(
    hidden, qkv, page_store, page_owner, page_slot, lengths, request_perm, w_out, post_gain,
    *, n_req, n_tp
):
    requests, slots, local_width = hidden.shape
    per_group = qkv.shape[3] // HD - 2
    token_rows = requests * slots
    tp_index = lax.axis_index("tp")

    blocks, valid = gather_prefix(page_store, page_owner, page_slot, n_req)

    device_row = lax.axis_index("req")
    my_requests = lax.dynamic_slice_in_dim(request_perm, device_row * requests, requests)
    matches = my_requests[:, None] == jnp.arange(lengths.shape[0], dtype=jnp.int32)[None, :]
    my_lengths = jnp.sum(jnp.where(matches, lengths[None, :], 0), 1)
    position = jnp.arange(slots, dtype=jnp.int32)
    live_mask = (position[None, :] < my_lengths[:, None]).astype(jnp.float32)

    prefix_len = page_store.shape[1] * page_owner.shape[0]
    cosine, sine = static_tables(prefix_len + np.arange(slots), HD)
    group_width = per_group * HD
    chunk = max(1, requests // 2)
    results = []
    for start in range(0, requests, chunk):
        attended = attend(qkv[:, :, 0], jnp.asarray(cosine), jnp.asarray(sine), blocks,
                          my_lengths, valid.astype(jnp.int32), start, chunk)
        own = attended.reshape(chunk * slots, per_group * HD)
        projected = project(own, w_out, tp_index, n_tp, group_width)
        projected = projected.reshape(chunk, slots, local_width)
        squares = jnp.sum(projected * projected, -1)
        branch_total = squares
        for shift in range(1, n_tp):
            branch_total = branch_total + shifted(squares, "tp", n_tp, shift)
        branch = projected * lax.rsqrt(branch_total / D + EPSILON)[..., None] * post_gain
        source = hidden[start:start + chunk].astype(jnp.float32)
        live = live_mask[start:start + chunk, :, None]
        results.append(((source + branch) * live).astype(jnp.bfloat16))
    return jnp.concatenate(results, 0)


def solution(mesh):
    placed = (
        P("req", None, "tp"),
        P("req", None, "tp", None),
        P("req", None, "tp", None),
        P(),
        P(),
        P(),
        P(),
        P(None, "tp"),
        P("tp"),
    )
    body = lambda *args: on_device(*args, n_req=mesh.shape["req"], n_tp=mesh.shape["tp"])
    return jax.shard_map(
        body, mesh=mesh, in_specs=placed, out_specs=P("req", None, "tp"), check_vma=False
    )
```

```python
import functools

import numpy as np
import jax
import jax.numpy as jnp
from jax import lax
from jax.experimental import pallas as pl
from jax.experimental.pallas import tpu as pltpu
from jax.sharding import PartitionSpec as P

D = 2304
HD = 256


EPSILON = 1e-06
SOFT_CAP = 50.0


def capped_exp(scores):
    return jnp.exp(SOFT_CAP * jnp.tanh(scores / SOFT_CAP))


def shifted(value, axis, size, shift):
    return lax.ppermute(value, axis, [(i, (i + shift) % size) for i in range(size)])


def swapped(value, axis, size, mask):
    return lax.ppermute(value, axis, [(i, i ^ mask) for i in range(size)])


def gather_prefix(page_store, page_owner, page_slot, n_req):
    device_row = lax.axis_index("req")
    page_count = page_owner.shape[0]
    if n_req <= page_count:
        mine = page_owner == device_row
        slot = jnp.sum(jnp.where(mine, page_slot, 0))
        own = page_store[0, :, 0]
        for index in range(1, page_store.shape[0]):
            own = jnp.where(slot == index, page_store[index, :, 0], own)
        blocks = [own]
        sources = [device_row]
        if n_req == 8:
            for mask in (1, 2, 3, 6):
                blocks.append(swapped(own, "req", n_req, mask))
                sources.append(device_row ^ mask)
            mirror = blocks[-1]
            for mask in (1, 2, 3):
                blocks.append(swapped(mirror, "req", n_req, mask))
                sources.append(device_row ^ 6 ^ mask)
        else:
            for shift in range(1, n_req):
                blocks.append(shifted(own, "req", n_req, shift))
                sources.append((device_row - shift) % n_req)
        sources = jnp.stack(sources)
        valid = jnp.any(page_owner[None, :] == sources[:, None], 1)
        return blocks, valid
    picked = page_store[page_slot][:, :, 0]
    held_here = page_owner == device_row
    offered = jnp.where(held_here[:, None, None], picked, jnp.zeros_like(picked))
    prefix = lax.psum(offered, "req")
    return [prefix[p] for p in range(page_count)], jnp.ones((page_count,), jnp.bool_)


def static_tables(positions, width):
    half_width = width // 2
    exponent = np.arange(half_width, dtype=np.float32) * np.float32(2.0) / np.float32(width)
    frequency = np.power(np.float32(10000.0), -exponent).astype(np.float32)
    angles = positions.astype(np.float32)[:, None] * frequency[None, :]
    return np.cos(angles).astype(np.float32), np.sin(angles).astype(np.float32)


def attention_kernel(length_ref, valid_ref, qkv_ref, cos_ref, sin_ref, *rest, offset):
    page_refs, out_ref = rest[:-1], rest[-1]
    request = pl.program_id(0) + offset
    slots = qkv_ref.shape[1]
    per_group = qkv_ref.shape[2] // HD - 2
    half = HD // 2
    cosine = cos_ref[...]
    sine = sin_ref[...]
    values_in = qkv_ref[0].astype(jnp.float32)

    def rope(part):
        first = part[:, :half]
        second = part[:, half:]
        return jnp.concatenate([first * cosine - second * sine, second * cosine + first * sine], -1)

    queries = jnp.concatenate(
        [(rope(values_in[:, q * HD:(q + 1) * HD]) * HD ** (-0.5)).astype(jnp.bfloat16)
         for q in range(per_group)], 0)
    fresh_keys = rope(values_in[:, per_group * HD:(per_group + 1) * HD]).astype(jnp.bfloat16)
    fresh_values = values_in[:, (per_group + 1) * HD:].astype(jnp.bfloat16)
    rows = queries.shape[0]
    contract = (((1,), (1,)), ((), ()))

    page_weights = []
    totals = jnp.zeros((rows, 1), jnp.float32)
    for index, ref in enumerate(page_refs):
        scores = lax.dot_general(queries, ref[:, :HD], contract, preferred_element_type=jnp.float32)
        flag = jnp.where(valid_ref[index] != 0, 1.0, 0.0).astype(jnp.float32)
        raw = capped_exp(scores) * flag
        totals = totals + jnp.sum(raw, -1, keepdims=True)
        page_weights.append(raw)
    scores = lax.dot_general(queries, fresh_keys, contract, preferred_element_type=jnp.float32)
    column = lax.broadcasted_iota(jnp.int32, scores.shape, 1)
    slot = lax.broadcasted_iota(jnp.int32, scores.shape, 0) % slots
    allowed = (column <= slot) & (column < length_ref[request])
    fresh_raw = jnp.where(allowed, capped_exp(scores), 0.0)
    totals = totals + jnp.sum(fresh_raw, -1, keepdims=True)
    inverse = 1.0 / totals
    attended = jnp.dot((fresh_raw * inverse).astype(jnp.bfloat16), fresh_values,
                       preferred_element_type=jnp.float32)
    for raw, ref in zip(page_weights, page_refs):
        attended = attended + jnp.dot((raw * inverse).astype(jnp.bfloat16), ref[:, HD:],
                                      preferred_element_type=jnp.float32)
    attended = attended.astype(jnp.bfloat16)
    out_ref[0] = jnp.concatenate(
        [attended[q * slots:(q + 1) * slots] for q in range(per_group)], 1)


def attend(qkv, cosine, sine, blocks, lengths, valid, offset, count):
    _, slots, width = qkv.shape
    per_group = width // HD - 2
    page_len, page_width = blocks[0].shape
    full = lambda shape: pl.BlockSpec(shape, lambda r, *_: (0,) * len(shape))
    grid_spec = pltpu.PrefetchScalarGridSpec(
        num_scalar_prefetch=2,
        grid=(count,),
        in_specs=[pl.BlockSpec((1, slots, width), lambda r, *_: (r + offset, 0, 0)),
                  full(cosine.shape), full(sine.shape)]
                 + [full((page_len, page_width)) for _ in blocks],
        out_specs=pl.BlockSpec((1, slots, per_group * HD), lambda r, *_: (r, 0, 0)),
    )
    return pl.pallas_call(
        functools.partial(attention_kernel, offset=offset),
        grid_spec=grid_spec,
        out_shape=jax.ShapeDtypeStruct((count, slots, per_group * HD), jnp.bfloat16),
    )(lengths, valid, qkv, cosine, sine, *blocks)

def project(own, w_out, tp_index, n_tp, group_width):
    if n_tp == 4:
        near = swapped(own, "tp", n_tp, 1)
        far = swapped(own, "tp", n_tp, 2)
        farther = swapped(far, "tp", n_tp, 1)
        parts = [(own, tp_index), (near, tp_index ^ 1), (far, tp_index ^ 2), (farther, tp_index ^ 3)]
    else:
        parts = [(own, tp_index)]
        for shift in range(1, n_tp):
            parts.append((shifted(own, "tp", n_tp, shift), (tp_index - shift) % n_tp))
    projected = None
    for block, group in parts:
        rows = lax.dynamic_slice_in_dim(w_out, group * group_width, group_width, 0)
        term = jnp.dot(block, rows, preferred_element_type=jnp.float32)
        projected = term if projected is None else projected + term
    return projected


def on_device(
    hidden, qkv, page_store, page_owner, page_slot, lengths, request_perm, w_out, post_gain,
    *, n_req, n_tp
):
    requests, slots, local_width = hidden.shape
    per_group = qkv.shape[3] // HD - 2
    token_rows = requests * slots
    tp_index = lax.axis_index("tp")

    blocks, valid = gather_prefix(page_store, page_owner, page_slot, n_req)

    device_row = lax.axis_index("req")
    my_requests = lax.dynamic_slice_in_dim(request_perm, device_row * requests, requests)
    matches = my_requests[:, None] == jnp.arange(lengths.shape[0], dtype=jnp.int32)[None, :]
    my_lengths = jnp.sum(jnp.where(matches, lengths[None, :], 0), 1)
    position = jnp.arange(slots, dtype=jnp.int32)
    live_mask = (position[None, :] < my_lengths[:, None]).astype(jnp.float32)

    prefix_len = page_store.shape[1] * page_owner.shape[0]
    cosine, sine = static_tables(prefix_len + np.arange(slots), HD)
    group_width = per_group * HD
    chunk = max(1, requests // 2)
    projected_parts = []
    for start in range(0, requests, chunk):
        attended = attend(qkv[:, :, 0], jnp.asarray(cosine), jnp.asarray(sine), blocks,
                          my_lengths, valid.astype(jnp.int32), start, chunk)
        own = attended.reshape(chunk * slots, per_group * HD)
        projected_parts.append(project(own, w_out, tp_index, n_tp, group_width))
    projected = jnp.concatenate(projected_parts, 0).reshape(requests, slots, local_width)

    squares = jnp.sum(projected * projected, -1)
    branch_total = squares
    for shift in range(1, n_tp):
        branch_total = branch_total + shifted(squares, "tp", n_tp, shift)
    branch = projected * lax.rsqrt(branch_total / D + EPSILON)[..., None] * post_gain
    source = hidden.astype(jnp.float32)
    return ((source + branch) * live_mask[..., None]).astype(jnp.bfloat16)


def solution(mesh):
    placed = (
        P("req", None, "tp"),
        P("req", None, "tp", None),
        P("req", None, "tp", None),
        P(),
        P(),
        P(),
        P(),
        P(None, "tp"),
        P("tp"),
    )
    body = lambda *args: on_device(*args, n_req=mesh.shape["req"], n_tp=mesh.shape["tp"])
    return jax.shard_map(
        body, mesh=mesh, in_specs=placed, out_specs=P("req", None, "tp"), check_vma=False
    )
```

```python
import functools

import numpy as np
import jax
import jax.numpy as jnp
from jax import lax
from jax.experimental import pallas as pl
from jax.experimental.pallas import tpu as pltpu
from jax.sharding import PartitionSpec as P

D = 2304
HD = 256


EPSILON = 1e-06
SOFT_CAP = 50.0


def capped_exp(scores):
    return jnp.exp(SOFT_CAP * jnp.tanh(scores / SOFT_CAP))


def shifted(value, axis, size, shift):
    return lax.ppermute(value, axis, [(i, (i + shift) % size) for i in range(size)])


def swapped(value, axis, size, mask):
    return lax.ppermute(value, axis, [(i, i ^ mask) for i in range(size)])


def gather_prefix(page_store, page_owner, page_slot, n_req):
    device_row = lax.axis_index("req")
    page_count = page_owner.shape[0]
    if n_req <= page_count:
        mine = page_owner == device_row
        slot = jnp.sum(jnp.where(mine, page_slot, 0))
        own = page_store[0, :, 0]
        for index in range(1, page_store.shape[0]):
            own = jnp.where(slot == index, page_store[index, :, 0], own)
        blocks = [own]
        sources = [device_row]
        if n_req == 8:
            for mask in (1, 2, 3, 6):
                blocks.append(swapped(own, "req", n_req, mask))
                sources.append(device_row ^ mask)
            mirror = blocks[-1]
            for mask in (1, 2, 3):
                blocks.append(swapped(mirror, "req", n_req, mask))
                sources.append(device_row ^ 6 ^ mask)
        else:
            for shift in range(1, n_req):
                blocks.append(shifted(own, "req", n_req, shift))
                sources.append((device_row - shift) % n_req)
        sources = jnp.stack(sources)
        valid = jnp.any(page_owner[None, :] == sources[:, None], 1)
        return blocks, valid
    picked = page_store[page_slot][:, :, 0]
    held_here = page_owner == device_row
    offered = jnp.where(held_here[:, None, None], picked, jnp.zeros_like(picked))
    prefix = lax.psum(offered, "req")
    return [prefix[p] for p in range(page_count)], jnp.ones((page_count,), jnp.bool_)


def static_tables(positions, width):
    half_width = width // 2
    exponent = np.arange(half_width, dtype=np.float32) * np.float32(2.0) / np.float32(width)
    frequency = np.power(np.float32(10000.0), -exponent).astype(np.float32)
    angles = positions.astype(np.float32)[:, None] * frequency[None, :]
    return np.cos(angles).astype(np.float32), np.sin(angles).astype(np.float32)


def attention_kernel(length_ref, valid_ref, qkv_ref, cos_ref, sin_ref, *rest, offset):
    page_refs, out_ref = rest[:-1], rest[-1]
    request = pl.program_id(0) + offset
    slots = qkv_ref.shape[1]
    per_group = qkv_ref.shape[2] // HD - 2
    half = HD // 2
    cosine = cos_ref[...]
    sine = sin_ref[...]
    values_in = qkv_ref[0].astype(jnp.float32)

    def rope(part):
        first = part[:, :half]
        second = part[:, half:]
        return jnp.concatenate([first * cosine - second * sine, second * cosine + first * sine], -1)

    queries = jnp.concatenate(
        [(rope(values_in[:, q * HD:(q + 1) * HD]) * HD ** (-0.5)).astype(jnp.bfloat16)
         for q in range(per_group)], 0)
    fresh_keys = rope(values_in[:, per_group * HD:(per_group + 1) * HD]).astype(jnp.bfloat16)
    fresh_values = values_in[:, (per_group + 1) * HD:].astype(jnp.bfloat16)
    pages = [ref[...] for ref in page_refs]
    keys = jnp.concatenate([page[:, :HD] for page in pages] + [fresh_keys], 0)
    values = jnp.concatenate([page[:, HD:] for page in pages] + [fresh_values], 0)
    prefix_len = len(pages) * pages[0].shape[0]
    key_count = keys.shape[0]
    rows = queries.shape[0]

    scores = lax.dot_general(queries, keys, (((1,), (1,)), ((), ())),
                             preferred_element_type=jnp.float32)
    page_column = lax.broadcasted_iota(jnp.int32, (1, key_count), 1) // pages[0].shape[0]
    page_flag = jnp.zeros((1, key_count), jnp.int32)
    for index in range(len(pages)):
        page_flag = page_flag + jnp.where(page_column == index, valid_ref[index], 0)
    page_flag = page_flag.astype(jnp.float32)
    column = lax.broadcasted_iota(jnp.int32, (rows, key_count), 1)
    slot = lax.broadcasted_iota(jnp.int32, (rows, key_count), 0) % slots
    suffix_pos = column - prefix_len
    suffix_ok = (suffix_pos >= 0) & (suffix_pos <= slot) & (suffix_pos < length_ref[request])
    exps = capped_exp(scores)
    raw = jnp.where(suffix_ok, exps, jnp.where(column < prefix_len, exps * page_flag, 0.0))
    totals = jnp.sum(raw, -1, keepdims=True)
    weights = (raw / totals).astype(jnp.bfloat16)
    attended = jnp.dot(weights, values, preferred_element_type=jnp.float32).astype(jnp.bfloat16)
    out_ref[0] = jnp.concatenate(
        [attended[q * slots:(q + 1) * slots] for q in range(per_group)], 1)


def attend(qkv, cosine, sine, blocks, lengths, valid, offset, count):
    _, slots, width = qkv.shape
    per_group = width // HD - 2
    page_len, page_width = blocks[0].shape
    full = lambda shape: pl.BlockSpec(shape, lambda r, *_: (0,) * len(shape))
    grid_spec = pltpu.PrefetchScalarGridSpec(
        num_scalar_prefetch=2,
        grid=(count,),
        in_specs=[pl.BlockSpec((1, slots, width), lambda r, *_: (r + offset, 0, 0)),
                  full(cosine.shape), full(sine.shape)]
                 + [full((page_len, page_width)) for _ in blocks],
        out_specs=pl.BlockSpec((1, slots, per_group * HD), lambda r, *_: (r, 0, 0)),
    )
    return pl.pallas_call(
        functools.partial(attention_kernel, offset=offset),
        grid_spec=grid_spec,
        out_shape=jax.ShapeDtypeStruct((count, slots, per_group * HD), jnp.bfloat16),
    )(lengths, valid, qkv, cosine, sine, *blocks)

def project(own, w_out, tp_index, n_tp, group_width):
    if n_tp == 4:
        near = swapped(own, "tp", n_tp, 1)
        half_rows = own.shape[0] // 2
        far = jnp.concatenate([swapped(own[:half_rows], "tp", n_tp, 2),
                               swapped(own[half_rows:], "tp", n_tp, 2)], 0)
        farther = swapped(far, "tp", n_tp, 1)
        parts = [(own, tp_index), (near, tp_index ^ 1), (far, tp_index ^ 2), (farther, tp_index ^ 3)]
    else:
        parts = [(own, tp_index)]
        for shift in range(1, n_tp):
            parts.append((shifted(own, "tp", n_tp, shift), (tp_index - shift) % n_tp))
    projected = None
    for block, group in parts:
        rows = lax.dynamic_slice_in_dim(w_out, group * group_width, group_width, 0)
        term = jnp.dot(block, rows, preferred_element_type=jnp.float32)
        projected = term if projected is None else projected + term
    return projected


def on_device(
    hidden, qkv, page_store, page_owner, page_slot, lengths, request_perm, w_out, post_gain,
    *, n_req, n_tp
):
    requests, slots, local_width = hidden.shape
    per_group = qkv.shape[3] // HD - 2
    token_rows = requests * slots
    tp_index = lax.axis_index("tp")

    blocks, valid = gather_prefix(page_store, page_owner, page_slot, n_req)

    device_row = lax.axis_index("req")
    my_requests = lax.dynamic_slice_in_dim(request_perm, device_row * requests, requests)
    matches = my_requests[:, None] == jnp.arange(lengths.shape[0], dtype=jnp.int32)[None, :]
    my_lengths = jnp.sum(jnp.where(matches, lengths[None, :], 0), 1)
    position = jnp.arange(slots, dtype=jnp.int32)
    live_mask = (position[None, :] < my_lengths[:, None]).astype(jnp.float32)

    prefix_len = page_store.shape[1] * page_owner.shape[0]
    cosine, sine = static_tables(prefix_len + np.arange(slots), HD)
    group_width = per_group * HD
    chunk = max(1, requests // 2)
    projected_parts = []
    for start in range(0, requests, chunk):
        attended = attend(qkv[:, :, 0], jnp.asarray(cosine), jnp.asarray(sine), blocks,
                          my_lengths, valid.astype(jnp.int32), start, chunk)
        own = attended.reshape(chunk * slots, per_group * HD)
        projected_parts.append(project(own, w_out, tp_index, n_tp, group_width))
    projected = jnp.concatenate(projected_parts, 0).reshape(requests, slots, local_width)

    squares = jnp.sum(projected * projected, -1)
    branch_total = squares
    for shift in range(1, n_tp):
        branch_total = branch_total + shifted(squares, "tp", n_tp, shift)
    branch = projected * lax.rsqrt(branch_total / D + EPSILON)[..., None] * post_gain
    source = hidden.astype(jnp.float32)
    return ((source + branch) * live_mask[..., None]).astype(jnp.bfloat16)


def solution(mesh):
    placed = (
        P("req", None, "tp"),
        P("req", None, "tp", None),
        P("req", None, "tp", None),
        P(),
        P(),
        P(),
        P(),
        P(None, "tp"),
        P("tp"),
    )
    body = lambda *args: on_device(*args, n_req=mesh.shape["req"], n_tp=mesh.shape["tp"])
    return jax.shard_map(
        body, mesh=mesh, in_specs=placed, out_specs=P("req", None, "tp"), check_vma=False
    )
```

```python
import functools

import numpy as np
import jax
import jax.numpy as jnp
from jax import lax
from jax.experimental import pallas as pl
from jax.experimental.pallas import tpu as pltpu
from jax.sharding import PartitionSpec as P

D = 2304
HD = 256


EPSILON = 1e-06
SOFT_CAP = 50.0


def capped_exp(scores):
    return jnp.exp(SOFT_CAP * jnp.tanh(scores / SOFT_CAP))


def shifted(value, axis, size, shift):
    return lax.ppermute(value, axis, [(i, (i + shift) % size) for i in range(size)])


def swapped(value, axis, size, mask):
    return lax.ppermute(value, axis, [(i, i ^ mask) for i in range(size)])


def gather_prefix(page_store, page_owner, page_slot, n_req):
    device_row = lax.axis_index("req")
    page_count = page_owner.shape[0]
    if n_req <= page_count:
        mine = page_owner == device_row
        slot = jnp.sum(jnp.where(mine, page_slot, 0))
        own = page_store[0, :, 0]
        for index in range(1, page_store.shape[0]):
            own = jnp.where(slot == index, page_store[index, :, 0], own)
        blocks = [own]
        sources = [device_row]
        if n_req == 8:
            for mask in (1, 2, 3, 6):
                blocks.append(swapped(own, "req", n_req, mask))
                sources.append(device_row ^ mask)
            mirror = blocks[-1]
            for mask in (1, 2, 3):
                blocks.append(swapped(mirror, "req", n_req, mask))
                sources.append(device_row ^ 6 ^ mask)
        else:
            for shift in range(1, n_req):
                blocks.append(shifted(own, "req", n_req, shift))
                sources.append((device_row - shift) % n_req)
        sources = jnp.stack(sources)
        valid = jnp.any(page_owner[None, :] == sources[:, None], 1)
        return blocks, valid
    picked = page_store[page_slot][:, :, 0]
    held_here = page_owner == device_row
    offered = jnp.where(held_here[:, None, None], picked, jnp.zeros_like(picked))
    prefix = lax.psum(offered, "req")
    return [prefix[p] for p in range(page_count)], jnp.ones((page_count,), jnp.bool_)


def static_tables(positions, width):
    half_width = width // 2
    exponent = np.arange(half_width, dtype=np.float32) * np.float32(2.0) / np.float32(width)
    frequency = np.power(np.float32(10000.0), -exponent).astype(np.float32)
    angles = positions.astype(np.float32)[:, None] * frequency[None, :]
    return np.cos(angles).astype(np.float32), np.sin(angles).astype(np.float32)


def attention_kernel(length_ref, valid_ref, qkv_ref, cos_ref, sin_ref, *rest,
                     offset, first_block, page_count, first, last):
    index = 0
    if not first:
        sum_in_ref, total_in_ref = rest[0], rest[1]
        index = 2
    page_refs = rest[index:index + page_count]
    outs = rest[index + page_count:]
    request = pl.program_id(0) + offset
    slots = qkv_ref.shape[1]
    per_group = qkv_ref.shape[2] // HD - 2
    half = HD // 2
    cosine = cos_ref[...]
    sine = sin_ref[...]
    values_in = qkv_ref[0].astype(jnp.float32)

    def rope(part):
        first_half = part[:, :half]
        second_half = part[:, half:]
        return jnp.concatenate(
            [first_half * cosine - second_half * sine, second_half * cosine + first_half * sine], -1)

    queries = jnp.concatenate(
        [(rope(values_in[:, q * HD:(q + 1) * HD]) * HD ** (-0.5)).astype(jnp.bfloat16)
         for q in range(per_group)], 0)
    rows = queries.shape[0]
    pages = [ref[...] for ref in page_refs]
    key_parts = [page[:, :HD] for page in pages]
    value_parts = [page[:, HD:] for page in pages]
    if first:
        key_parts.append(rope(values_in[:, per_group * HD:(per_group + 1) * HD]).astype(jnp.bfloat16))
        value_parts.append(values_in[:, (per_group + 1) * HD:].astype(jnp.bfloat16))
    if first:
        sums = jnp.zeros((rows, HD), jnp.float32)
        totals = jnp.zeros((rows, 1), jnp.float32)
    else:
        sums = sum_in_ref[0]
        totals = total_in_ref[0]
    if key_parts:
        keys = jnp.concatenate(key_parts, 0)
        values = jnp.concatenate(value_parts, 0)
        key_count = keys.shape[0]
        prefix_len = sum(page.shape[0] for page in pages)
        scores = lax.dot_general(queries, keys, (((1,), (1,)), ((), ())),
                                 preferred_element_type=jnp.float32)
        exps = capped_exp(scores)
        column = lax.broadcasted_iota(jnp.int32, (rows, key_count), 1)
        if pages:
            page_len = pages[0].shape[0]
            page_column = lax.broadcasted_iota(jnp.int32, (1, key_count), 1) // page_len
            page_flag = jnp.zeros((1, key_count), jnp.int32)
            for number in range(len(pages)):
                page_flag = page_flag + jnp.where(
                    page_column == number, valid_ref[first_block + number], 0)
            page_flag = page_flag.astype(jnp.float32)
        else:
            page_flag = jnp.zeros((1, key_count), jnp.float32)
        if first:
            slot = lax.broadcasted_iota(jnp.int32, (rows, key_count), 0) % slots
            suffix_pos = column - prefix_len
            suffix_ok = (suffix_pos >= 0) & (suffix_pos <= slot) & (suffix_pos < length_ref[request])
            raw = jnp.where(suffix_ok, exps, jnp.where(column < prefix_len, exps * page_flag, 0.0))
        else:
            raw = exps * page_flag
        totals = totals + jnp.sum(raw, -1, keepdims=True)
        sums = sums + jnp.dot(raw.astype(jnp.bfloat16), values, preferred_element_type=jnp.float32)
    if last:
        attended = (sums / totals).astype(jnp.bfloat16)
        outs[0][0] = jnp.concatenate(
            [attended[q * slots:(q + 1) * slots] for q in range(per_group)], 1)
    else:
        outs[0][0] = sums
        outs[1][0] = totals


def attend(qkv, cosine, sine, blocks, lengths, valid, offset, count, first_block,
           partial=None, last=True):
    _, slots, width = qkv.shape
    per_group = width // HD - 2
    rows = per_group * slots
    first = partial is None
    full = lambda shape: pl.BlockSpec(shape, lambda r, *_: (0,) * len(shape))
    per_request = lambda shape: pl.BlockSpec((1,) + shape, lambda r, *_: (r + offset, 0, 0))
    in_specs = [per_request((slots, width)), full(cosine.shape), full(sine.shape)]
    operands = [qkv, cosine, sine]
    if not first:
        in_specs += [per_request((rows, HD)), per_request((rows, 1))]
        operands += list(partial)
    in_specs += [full(block.shape) for block in blocks]
    operands += list(blocks)
    own_block = lambda shape: pl.BlockSpec((1,) + shape, lambda r, *_: (r, 0, 0))
    if last:
        out_specs = [own_block((slots, per_group * HD))]
        out_shape = [jax.ShapeDtypeStruct((count, slots, per_group * HD), jnp.bfloat16)]
    else:
        out_specs = [own_block((rows, HD)), own_block((rows, 1))]
        out_shape = [jax.ShapeDtypeStruct((count, rows, HD), jnp.float32),
                     jax.ShapeDtypeStruct((count, rows, 1), jnp.float32)]
    grid_spec = pltpu.PrefetchScalarGridSpec(
        num_scalar_prefetch=2, grid=(count,), in_specs=in_specs, out_specs=out_specs)
    kernel = functools.partial(attention_kernel, offset=offset, first_block=first_block,
                               page_count=len(blocks), first=first, last=last)
    result = pl.pallas_call(kernel, grid_spec=grid_spec, out_shape=out_shape)(
        lengths, valid, *operands)
    return result[0] if last else result


def project(own, w_out, tp_index, n_tp, group_width):
    if n_tp == 4:
        near = swapped(own, "tp", n_tp, 1)
        far = swapped(own, "tp", n_tp, 2)
        farther = swapped(far, "tp", n_tp, 1)
        parts = [(own, tp_index), (near, tp_index ^ 1), (far, tp_index ^ 2), (farther, tp_index ^ 3)]
    else:
        parts = [(own, tp_index)]
        for shift in range(1, n_tp):
            parts.append((shifted(own, "tp", n_tp, shift), (tp_index - shift) % n_tp))
    projected = None
    for block, group in parts:
        rows = lax.dynamic_slice_in_dim(w_out, group * group_width, group_width, 0)
        term = jnp.dot(block, rows, preferred_element_type=jnp.float32)
        projected = term if projected is None else projected + term
    return projected


def on_device(
    hidden, qkv, page_store, page_owner, page_slot, lengths, request_perm, w_out, post_gain,
    *, n_req, n_tp
):
    requests, slots, local_width = hidden.shape
    per_group = qkv.shape[3] // HD - 2
    token_rows = requests * slots
    tp_index = lax.axis_index("tp")

    blocks, valid = gather_prefix(page_store, page_owner, page_slot, n_req)

    device_row = lax.axis_index("req")
    my_requests = lax.dynamic_slice_in_dim(request_perm, device_row * requests, requests)
    matches = my_requests[:, None] == jnp.arange(lengths.shape[0], dtype=jnp.int32)[None, :]
    my_lengths = jnp.sum(jnp.where(matches, lengths[None, :], 0), 1)
    position = jnp.arange(slots, dtype=jnp.int32)
    live_mask = (position[None, :] < my_lengths[:, None]).astype(jnp.float32)

    prefix_len = page_store.shape[1] * page_owner.shape[0]
    cosine, sine = static_tables(prefix_len + np.arange(slots), HD)
    group_width = per_group * HD
    chunk = max(1, requests // 2)
    early = min(len(blocks), 5)
    qkv_rows = qkv[:, :, 0]
    cos_in, sin_in = jnp.asarray(cosine), jnp.asarray(sine)
    valid_in = valid.astype(jnp.int32)
    partial = attend(qkv_rows, cos_in, sin_in, blocks[:early], my_lengths, valid_in,
                     0, requests, 0, last=False)
    projected_parts = []
    for start in range(0, requests, chunk):
        attended = attend(qkv_rows, cos_in, sin_in, blocks[early:], my_lengths, valid_in,
                          start, chunk, early, partial=partial)
        own = attended.reshape(chunk * slots, per_group * HD)
        projected_parts.append(project(own, w_out, tp_index, n_tp, group_width))
    projected = jnp.concatenate(projected_parts, 0).reshape(requests, slots, local_width)

    squares = jnp.sum(projected * projected, -1)
    branch_total = squares
    for shift in range(1, n_tp):
        branch_total = branch_total + shifted(squares, "tp", n_tp, shift)
    branch = projected * lax.rsqrt(branch_total / D + EPSILON)[..., None] * post_gain
    source = hidden.astype(jnp.float32)
    return ((source + branch) * live_mask[..., None]).astype(jnp.bfloat16)


def solution(mesh):
    placed = (
        P("req", None, "tp"),
        P("req", None, "tp", None),
        P("req", None, "tp", None),
        P(),
        P(),
        P(),
        P(),
        P(None, "tp"),
        P("tp"),
    )
    body = lambda *args: on_device(*args, n_req=mesh.shape["req"], n_tp=mesh.shape["tp"])
    return jax.shard_map(
        body, mesh=mesh, in_specs=placed, out_specs=P("req", None, "tp"), check_vma=False
    )
```

```python
import functools

import numpy as np
import jax
import jax.numpy as jnp
from jax import lax
from jax.experimental import pallas as pl
from jax.experimental.pallas import tpu as pltpu
from jax.sharding import PartitionSpec as P

D = 2304
HD = 256


EPSILON = 1e-06
SOFT_CAP = 50.0


def capped_exp(scores):
    return jnp.exp(SOFT_CAP * jnp.tanh(scores / SOFT_CAP))


def shifted(value, axis, size, shift):
    return lax.ppermute(value, axis, [(i, (i + shift) % size) for i in range(size)])


def swapped(value, axis, size, mask):
    return lax.ppermute(value, axis, [(i, i ^ mask) for i in range(size)])


def gather_prefix(page_store, page_owner, page_slot, n_req):
    device_row = lax.axis_index("req")
    page_count = page_owner.shape[0]
    if n_req <= page_count:
        mine = page_owner == device_row
        slot = jnp.sum(jnp.where(mine, page_slot, 0))
        own = page_store[0, :, 0]
        for index in range(1, page_store.shape[0]):
            own = jnp.where(slot == index, page_store[index, :, 0], own)
        blocks = [own]
        sources = [device_row]
        if n_req == 8:
            for mask in (1, 2, 3, 6):
                blocks.append(swapped(own, "req", n_req, mask))
                sources.append(device_row ^ mask)
            mirror = blocks[-1]
            for mask in (1, 2, 3):
                blocks.append(swapped(mirror, "req", n_req, mask))
                sources.append(device_row ^ 6 ^ mask)
        else:
            for shift in range(1, n_req):
                blocks.append(shifted(own, "req", n_req, shift))
                sources.append((device_row - shift) % n_req)
        sources = jnp.stack(sources)
        valid = jnp.any(page_owner[None, :] == sources[:, None], 1)
        return blocks, valid
    picked = page_store[page_slot][:, :, 0]
    held_here = page_owner == device_row
    offered = jnp.where(held_here[:, None, None], picked, jnp.zeros_like(picked))
    prefix = lax.psum(offered, "req")
    return [prefix[p] for p in range(page_count)], jnp.ones((page_count,), jnp.bool_)


def static_tables(positions, width):
    half_width = width // 2
    exponent = np.arange(half_width, dtype=np.float32) * np.float32(2.0) / np.float32(width)
    frequency = np.power(np.float32(10000.0), -exponent).astype(np.float32)
    angles = positions.astype(np.float32)[:, None] * frequency[None, :]
    return np.cos(angles).astype(np.float32), np.sin(angles).astype(np.float32)


def attention_kernel(length_ref, valid_ref, qkv_ref, cos_ref, sin_ref, *rest, offset):
    page_refs, out_ref = rest[:-1], rest[-1]
    request = pl.program_id(0) + offset
    slots = qkv_ref.shape[1]
    per_group = qkv_ref.shape[2] // HD - 2
    half = HD // 2
    cosine = cos_ref[...]
    sine = sin_ref[...]
    values_in = qkv_ref[0].astype(jnp.float32)

    def rope(part):
        first = part[:, :half]
        second = part[:, half:]
        return jnp.concatenate([first * cosine - second * sine, second * cosine + first * sine], -1)

    queries = jnp.concatenate(
        [(rope(values_in[:, q * HD:(q + 1) * HD]) * HD ** (-0.5)).astype(jnp.bfloat16)
         for q in range(per_group)], 0)
    fresh_keys = rope(values_in[:, per_group * HD:(per_group + 1) * HD]).astype(jnp.bfloat16)
    fresh_values = values_in[:, (per_group + 1) * HD:].astype(jnp.bfloat16)
    pages = [ref[...] for ref in page_refs]
    keys = jnp.concatenate([page[:, :HD] for page in pages] + [fresh_keys], 0)
    values = jnp.concatenate([page[:, HD:] for page in pages] + [fresh_values], 0)
    prefix_len = len(pages) * pages[0].shape[0]
    key_count = keys.shape[0]
    rows = queries.shape[0]

    scores = lax.dot_general(queries, keys, (((1,), (1,)), ((), ())),
                             preferred_element_type=jnp.float32)
    exps = capped_exp(scores)
    page_len = pages[0].shape[0]
    page_column = lax.broadcasted_iota(jnp.int32, (1, prefix_len), 1) // page_len
    page_flag = jnp.zeros((1, prefix_len), jnp.int32)
    for index in range(len(pages)):
        page_flag = page_flag + jnp.where(page_column == index, valid_ref[index], 0)
    prefix_raw = exps[:, :prefix_len] * page_flag.astype(jnp.float32)
    suffix_shape = (rows, key_count - prefix_len)
    column = lax.broadcasted_iota(jnp.int32, suffix_shape, 1)
    slot = lax.broadcasted_iota(jnp.int32, suffix_shape, 0) % slots
    allowed = (column <= slot) & (column < length_ref[request])
    suffix_raw = jnp.where(allowed, exps[:, prefix_len:], 0.0)
    totals = jnp.sum(prefix_raw, -1, keepdims=True) + jnp.sum(suffix_raw, -1, keepdims=True)
    inverse = 1.0 / totals
    weights = jnp.concatenate([(prefix_raw * inverse).astype(jnp.bfloat16),
                               (suffix_raw * inverse).astype(jnp.bfloat16)], 1)
    attended = jnp.dot(weights, values, preferred_element_type=jnp.float32).astype(jnp.bfloat16)
    out_ref[0] = jnp.concatenate(
        [attended[q * slots:(q + 1) * slots] for q in range(per_group)], 1)


def attend(qkv, cosine, sine, blocks, lengths, valid, offset, count):
    _, slots, width = qkv.shape
    per_group = width // HD - 2
    page_len, page_width = blocks[0].shape
    full = lambda shape: pl.BlockSpec(shape, lambda r, *_: (0,) * len(shape))
    grid_spec = pltpu.PrefetchScalarGridSpec(
        num_scalar_prefetch=2,
        grid=(count,),
        in_specs=[pl.BlockSpec((1, slots, width), lambda r, *_: (r + offset, 0, 0)),
                  full(cosine.shape), full(sine.shape)]
                 + [full((page_len, page_width)) for _ in blocks],
        out_specs=pl.BlockSpec((1, slots, per_group * HD), lambda r, *_: (r, 0, 0)),
    )
    return pl.pallas_call(
        functools.partial(attention_kernel, offset=offset),
        grid_spec=grid_spec,
        out_shape=jax.ShapeDtypeStruct((count, slots, per_group * HD), jnp.bfloat16),
    )(lengths, valid, qkv, cosine, sine, *blocks)

def project(own, w_out, tp_index, n_tp, group_width):
    if n_tp == 4:
        near = swapped(own, "tp", n_tp, 1)
        far = swapped(own, "tp", n_tp, 2)
        farther = swapped(far, "tp", n_tp, 1)
        parts = [(own, tp_index), (near, tp_index ^ 1), (far, tp_index ^ 2), (farther, tp_index ^ 3)]
    else:
        parts = [(own, tp_index)]
        for shift in range(1, n_tp):
            parts.append((shifted(own, "tp", n_tp, shift), (tp_index - shift) % n_tp))
    projected = None
    for block, group in parts:
        rows = lax.dynamic_slice_in_dim(w_out, group * group_width, group_width, 0)
        term = jnp.dot(block, rows, preferred_element_type=jnp.float32)
        projected = term if projected is None else projected + term
    return projected


def on_device(
    hidden, qkv, page_store, page_owner, page_slot, lengths, request_perm, w_out, post_gain,
    *, n_req, n_tp
):
    requests, slots, local_width = hidden.shape
    per_group = qkv.shape[3] // HD - 2
    token_rows = requests * slots
    tp_index = lax.axis_index("tp")

    blocks, valid = gather_prefix(page_store, page_owner, page_slot, n_req)

    device_row = lax.axis_index("req")
    my_requests = lax.dynamic_slice_in_dim(request_perm, device_row * requests, requests)
    matches = my_requests[:, None] == jnp.arange(lengths.shape[0], dtype=jnp.int32)[None, :]
    my_lengths = jnp.sum(jnp.where(matches, lengths[None, :], 0), 1)
    position = jnp.arange(slots, dtype=jnp.int32)
    live_mask = (position[None, :] < my_lengths[:, None]).astype(jnp.float32)

    prefix_len = page_store.shape[1] * page_owner.shape[0]
    cosine, sine = static_tables(prefix_len + np.arange(slots), HD)
    group_width = per_group * HD
    chunk = max(1, requests // 2)
    projected_parts = []
    for start in range(0, requests, chunk):
        attended = attend(qkv[:, :, 0], jnp.asarray(cosine), jnp.asarray(sine), blocks,
                          my_lengths, valid.astype(jnp.int32), start, chunk)
        own = attended.reshape(chunk * slots, per_group * HD)
        projected_parts.append(project(own, w_out, tp_index, n_tp, group_width))
    projected = jnp.concatenate(projected_parts, 0).reshape(requests, slots, local_width)

    squares = jnp.sum(projected * projected, -1)
    branch_total = squares
    for shift in range(1, n_tp):
        branch_total = branch_total + shifted(squares, "tp", n_tp, shift)
    branch = projected * lax.rsqrt(branch_total / D + EPSILON)[..., None] * post_gain
    source = hidden.astype(jnp.float32)
    return ((source + branch) * live_mask[..., None]).astype(jnp.bfloat16)


def solution(mesh):
    placed = (
        P("req", None, "tp"),
        P("req", None, "tp", None),
        P("req", None, "tp", None),
        P(),
        P(),
        P(),
        P(),
        P(None, "tp"),
        P("tp"),
    )
    body = lambda *args: on_device(*args, n_req=mesh.shape["req"], n_tp=mesh.shape["tp"])
    return jax.shard_map(
        body, mesh=mesh, in_specs=placed, out_specs=P("req", None, "tp"), check_vma=False
    )
```

```python
import functools

import numpy as np
import jax
import jax.numpy as jnp
from jax import lax
from jax.experimental import pallas as pl
from jax.experimental.pallas import tpu as pltpu
from jax.sharding import PartitionSpec as P

D = 2304
HD = 256


EPSILON = 1e-06
SOFT_CAP = 50.0


def capped_exp(scores):
    return jnp.exp(SOFT_CAP * jnp.tanh(scores / SOFT_CAP))


def shifted(value, axis, size, shift):
    return lax.ppermute(value, axis, [(i, (i + shift) % size) for i in range(size)])


def swapped(value, axis, size, mask):
    return lax.ppermute(value, axis, [(i, i ^ mask) for i in range(size)])


def gather_prefix(page_store, page_owner, page_slot, n_req):
    device_row = lax.axis_index("req")
    page_count = page_owner.shape[0]
    if n_req <= page_count:
        mine = page_owner == device_row
        slot = jnp.sum(jnp.where(mine, page_slot, 0))
        own = page_store[0, :, 0]
        for index in range(1, page_store.shape[0]):
            own = jnp.where(slot == index, page_store[index, :, 0], own)
        blocks = [own]
        sources = [device_row]
        if n_req == 8:
            for mask in (1, 2, 3, 6):
                blocks.append(swapped(own, "req", n_req, mask))
                sources.append(device_row ^ mask)
            mirror = blocks[-1]
            for mask in (1, 2, 3):
                blocks.append(swapped(mirror, "req", n_req, mask))
                sources.append(device_row ^ 6 ^ mask)
        else:
            for shift in range(1, n_req):
                blocks.append(shifted(own, "req", n_req, shift))
                sources.append((device_row - shift) % n_req)
        sources = jnp.stack(sources)
        valid = jnp.any(page_owner[None, :] == sources[:, None], 1)
        return blocks, valid
    picked = page_store[page_slot][:, :, 0]
    held_here = page_owner == device_row
    offered = jnp.where(held_here[:, None, None], picked, jnp.zeros_like(picked))
    prefix = lax.psum(offered, "req")
    return [prefix[p] for p in range(page_count)], jnp.ones((page_count,), jnp.bool_)


def static_tables(positions, width):
    half_width = width // 2
    exponent = np.arange(half_width, dtype=np.float32) * np.float32(2.0) / np.float32(width)
    frequency = np.power(np.float32(10000.0), -exponent).astype(np.float32)
    angles = positions.astype(np.float32)[:, None] * frequency[None, :]
    return np.cos(angles).astype(np.float32), np.sin(angles).astype(np.float32)


def attention_kernel(length_ref, valid_ref, qkv_ref, cos_ref, sin_ref, *rest, offset):
    page_refs, out_ref, key_scratch, value_scratch = rest[:-3], rest[-3], rest[-2], rest[-1]
    request = pl.program_id(0) + offset
    slots = qkv_ref.shape[1]
    per_group = qkv_ref.shape[2] // HD - 2
    half = HD // 2
    cosine = cos_ref[...]
    sine = sin_ref[...]
    values_in = qkv_ref[0].astype(jnp.float32)

    def rope(part):
        first = part[:, :half]
        second = part[:, half:]
        return jnp.concatenate([first * cosine - second * sine, second * cosine + first * sine], -1)

    queries = jnp.concatenate(
        [(rope(values_in[:, q * HD:(q + 1) * HD]) * HD ** (-0.5)).astype(jnp.bfloat16)
         for q in range(per_group)], 0)
    fresh_keys = rope(values_in[:, per_group * HD:(per_group + 1) * HD]).astype(jnp.bfloat16)
    fresh_values = values_in[:, (per_group + 1) * HD:].astype(jnp.bfloat16)
    page_len = page_refs[0].shape[0]
    prefix_len = len(page_refs) * page_len

    @pl.when(pl.program_id(0) == 0)
    def _():
        for index, ref in enumerate(page_refs):
            key_scratch[index * page_len:(index + 1) * page_len] = ref[:, :HD]
            value_scratch[index * page_len:(index + 1) * page_len] = ref[:, HD:]

    key_scratch[prefix_len:] = fresh_keys
    value_scratch[prefix_len:] = fresh_values
    keys = key_scratch[...]
    values = value_scratch[...]
    key_count = keys.shape[0]
    rows = queries.shape[0]

    scores = lax.dot_general(queries, keys, (((1,), (1,)), ((), ())),
                             preferred_element_type=jnp.float32)
    exps = capped_exp(scores)
    page_column = lax.broadcasted_iota(jnp.int32, (1, prefix_len), 1) // page_len
    page_flag = jnp.zeros((1, prefix_len), jnp.int32)
    for index in range(len(page_refs)):
        page_flag = page_flag + jnp.where(page_column == index, valid_ref[index], 0)
    prefix_raw = exps[:, :prefix_len] * page_flag.astype(jnp.float32)
    suffix_shape = (rows, key_count - prefix_len)
    column = lax.broadcasted_iota(jnp.int32, suffix_shape, 1)
    slot = lax.broadcasted_iota(jnp.int32, suffix_shape, 0) % slots
    allowed = (column <= slot) & (column < length_ref[request])
    suffix_raw = jnp.where(allowed, exps[:, prefix_len:], 0.0)
    totals = jnp.sum(prefix_raw, -1, keepdims=True) + jnp.sum(suffix_raw, -1, keepdims=True)
    inverse = 1.0 / totals
    weights = jnp.concatenate([(prefix_raw * inverse).astype(jnp.bfloat16),
                               (suffix_raw * inverse).astype(jnp.bfloat16)], 1)
    attended = jnp.dot(weights, values, preferred_element_type=jnp.float32).astype(jnp.bfloat16)
    out_ref[0] = jnp.concatenate(
        [attended[q * slots:(q + 1) * slots] for q in range(per_group)], 1)


def attend(qkv, cosine, sine, blocks, lengths, valid, offset, count):
    _, slots, width = qkv.shape
    per_group = width // HD - 2
    page_len, page_width = blocks[0].shape
    full = lambda shape: pl.BlockSpec(shape, lambda r, *_: (0,) * len(shape))
    grid_spec = pltpu.PrefetchScalarGridSpec(
        num_scalar_prefetch=2,
        grid=(count,),
        in_specs=[pl.BlockSpec((1, slots, width), lambda r, *_: (r + offset, 0, 0)),
                  full(cosine.shape), full(sine.shape)]
                 + [full((page_len, page_width)) for _ in blocks],
        out_specs=pl.BlockSpec((1, slots, per_group * HD), lambda r, *_: (r, 0, 0)),
        scratch_shapes=[pltpu.VMEM((len(blocks) * page_len + slots, HD), jnp.bfloat16),
                        pltpu.VMEM((len(blocks) * page_len + slots, HD), jnp.bfloat16)],
    )
    return pl.pallas_call(
        functools.partial(attention_kernel, offset=offset),
        grid_spec=grid_spec,
        out_shape=jax.ShapeDtypeStruct((count, slots, per_group * HD), jnp.bfloat16),
    )(lengths, valid, qkv, cosine, sine, *blocks)

def project(own, w_out, tp_index, n_tp, group_width):
    if n_tp == 4:
        near = swapped(own, "tp", n_tp, 1)
        far = swapped(own, "tp", n_tp, 2)
        farther = swapped(far, "tp", n_tp, 1)
        parts = [(own, tp_index), (near, tp_index ^ 1), (far, tp_index ^ 2), (farther, tp_index ^ 3)]
    else:
        parts = [(own, tp_index)]
        for shift in range(1, n_tp):
            parts.append((shifted(own, "tp", n_tp, shift), (tp_index - shift) % n_tp))
    projected = None
    for block, group in parts:
        rows = lax.dynamic_slice_in_dim(w_out, group * group_width, group_width, 0)
        term = jnp.dot(block, rows, preferred_element_type=jnp.float32)
        projected = term if projected is None else projected + term
    return projected


def on_device(
    hidden, qkv, page_store, page_owner, page_slot, lengths, request_perm, w_out, post_gain,
    *, n_req, n_tp
):
    requests, slots, local_width = hidden.shape
    per_group = qkv.shape[3] // HD - 2
    token_rows = requests * slots
    tp_index = lax.axis_index("tp")

    blocks, valid = gather_prefix(page_store, page_owner, page_slot, n_req)

    device_row = lax.axis_index("req")
    my_requests = lax.dynamic_slice_in_dim(request_perm, device_row * requests, requests)
    matches = my_requests[:, None] == jnp.arange(lengths.shape[0], dtype=jnp.int32)[None, :]
    my_lengths = jnp.sum(jnp.where(matches, lengths[None, :], 0), 1)
    position = jnp.arange(slots, dtype=jnp.int32)
    live_mask = (position[None, :] < my_lengths[:, None]).astype(jnp.float32)

    prefix_len = page_store.shape[1] * page_owner.shape[0]
    cosine, sine = static_tables(prefix_len + np.arange(slots), HD)
    group_width = per_group * HD
    chunk = max(1, requests // 2)
    projected_parts = []
    for start in range(0, requests, chunk):
        attended = attend(qkv[:, :, 0], jnp.asarray(cosine), jnp.asarray(sine), blocks,
                          my_lengths, valid.astype(jnp.int32), start, chunk)
        own = attended.reshape(chunk * slots, per_group * HD)
        projected_parts.append(project(own, w_out, tp_index, n_tp, group_width))
    projected = jnp.concatenate(projected_parts, 0).reshape(requests, slots, local_width)

    squares = jnp.sum(projected * projected, -1)
    branch_total = squares
    for shift in range(1, n_tp):
        branch_total = branch_total + shifted(squares, "tp", n_tp, shift)
    branch = projected * lax.rsqrt(branch_total / D + EPSILON)[..., None] * post_gain
    source = hidden.astype(jnp.float32)
    return ((source + branch) * live_mask[..., None]).astype(jnp.bfloat16)


def solution(mesh):
    placed = (
        P("req", None, "tp"),
        P("req", None, "tp", None),
        P("req", None, "tp", None),
        P(),
        P(),
        P(),
        P(),
        P(None, "tp"),
        P("tp"),
    )
    body = lambda *args: on_device(*args, n_req=mesh.shape["req"], n_tp=mesh.shape["tp"])
    return jax.shard_map(
        body, mesh=mesh, in_specs=placed, out_specs=P("req", None, "tp"), check_vma=False
    )
```

```python
import functools

import numpy as np
import jax
import jax.numpy as jnp
from jax import lax
from jax.experimental import pallas as pl
from jax.experimental.pallas import tpu as pltpu
from jax.sharding import PartitionSpec as P

D = 2304
HD = 256


EPSILON = 1e-06
SOFT_CAP = 50.0


def capped_exp(scores):
    return jnp.exp(SOFT_CAP * jnp.tanh(scores / SOFT_CAP))


def shifted(value, axis, size, shift):
    return lax.ppermute(value, axis, [(i, (i + shift) % size) for i in range(size)])


def swapped(value, axis, size, mask):
    return lax.ppermute(value, axis, [(i, i ^ mask) for i in range(size)])


def gather_prefix(page_store, page_owner, page_slot, n_req):
    device_row = lax.axis_index("req")
    page_count = page_owner.shape[0]
    if n_req <= page_count:
        mine = page_owner == device_row
        slot = jnp.sum(jnp.where(mine, page_slot, 0))
        own = page_store[0, :, 0]
        for index in range(1, page_store.shape[0]):
            own = jnp.where(slot == index, page_store[index, :, 0], own)
        blocks = [own]
        sources = [device_row]
        if n_req == 8:
            for mask in (1, 2, 3, 6):
                blocks.append(swapped(own, "req", n_req, mask))
                sources.append(device_row ^ mask)
            mirror = blocks[-1]
            for mask in (1, 2, 3):
                blocks.append(swapped(mirror, "req", n_req, mask))
                sources.append(device_row ^ 6 ^ mask)
        else:
            for shift in range(1, n_req):
                blocks.append(shifted(own, "req", n_req, shift))
                sources.append((device_row - shift) % n_req)
        sources = jnp.stack(sources)
        valid = jnp.any(page_owner[None, :] == sources[:, None], 1)
        return blocks, valid
    picked = page_store[page_slot][:, :, 0]
    held_here = page_owner == device_row
    offered = jnp.where(held_here[:, None, None], picked, jnp.zeros_like(picked))
    prefix = lax.psum(offered, "req")
    return [prefix[p] for p in range(page_count)], jnp.ones((page_count,), jnp.bool_)


def static_tables(positions, width):
    half_width = width // 2
    exponent = np.arange(half_width, dtype=np.float32) * np.float32(2.0) / np.float32(width)
    frequency = np.power(np.float32(10000.0), -exponent).astype(np.float32)
    angles = positions.astype(np.float32)[:, None] * frequency[None, :]
    return np.cos(angles).astype(np.float32), np.sin(angles).astype(np.float32)


def attention_kernel(length_ref, valid_ref, qkv_ref, cos_ref, sin_ref, *rest, offset):
    page_refs, out_ref = rest[:-1], rest[-1]
    request = pl.program_id(0) + offset
    slots = qkv_ref.shape[1]
    per_group = qkv_ref.shape[2] // HD - 2
    half = HD // 2
    cosine = cos_ref[...]
    sine = sin_ref[...]
    values_in = qkv_ref[0].astype(jnp.float32)

    def rope(part):
        first = part[:, :half]
        second = part[:, half:]
        return jnp.concatenate([first * cosine - second * sine, second * cosine + first * sine], -1)

    queries = jnp.concatenate(
        [(rope(values_in[:, q * HD:(q + 1) * HD]) * HD ** (-0.5)).astype(jnp.bfloat16)
         for q in range(per_group)], 0)
    fresh_keys = rope(values_in[:, per_group * HD:(per_group + 1) * HD]).astype(jnp.bfloat16)
    fresh_values = values_in[:, (per_group + 1) * HD:].astype(jnp.bfloat16)
    pages = [ref[...] for ref in page_refs]
    keys = jnp.concatenate([page[:, :HD] for page in pages] + [fresh_keys], 0)
    values = jnp.concatenate([page[:, HD:] for page in pages] + [fresh_values], 0)
    prefix_len = len(pages) * pages[0].shape[0]
    key_count = keys.shape[0]
    rows = queries.shape[0]

    scores = lax.dot_general(queries, keys, (((1,), (1,)), ((), ())),
                             preferred_element_type=jnp.float32)
    exps = capped_exp(scores)
    page_len = pages[0].shape[0]
    page_column = lax.broadcasted_iota(jnp.int32, (1, prefix_len), 1) // page_len
    page_flag = jnp.zeros((1, prefix_len), jnp.int32)
    for index in range(len(pages)):
        page_flag = page_flag + jnp.where(page_column == index, valid_ref[index], 0)
    prefix_raw = exps[:, :prefix_len] * page_flag.astype(jnp.float32)
    suffix_shape = (rows, key_count - prefix_len)
    column = lax.broadcasted_iota(jnp.int32, suffix_shape, 1)
    slot = lax.broadcasted_iota(jnp.int32, suffix_shape, 0) % slots
    allowed = (column <= slot) & (column < length_ref[request])
    suffix_raw = jnp.where(allowed, exps[:, prefix_len:], 0.0)
    totals = jnp.sum(prefix_raw, -1, keepdims=True) + jnp.sum(suffix_raw, -1, keepdims=True)
    inverse = 1.0 / totals
    weights = jnp.concatenate([(prefix_raw * inverse).astype(jnp.bfloat16),
                               (suffix_raw * inverse).astype(jnp.bfloat16)], 1)
    attended = jnp.dot(weights, values, preferred_element_type=jnp.float32).astype(jnp.bfloat16)
    out_ref[0] = jnp.concatenate(
        [attended[q * slots:(q + 1) * slots] for q in range(per_group)], 1)


def attend(qkv, cosine, sine, blocks, lengths, valid, offset, count):
    _, slots, width = qkv.shape
    per_group = width // HD - 2
    page_len, page_width = blocks[0].shape
    full = lambda shape: pl.BlockSpec(shape, lambda r, *_: (0,) * len(shape))
    grid_spec = pltpu.PrefetchScalarGridSpec(
        num_scalar_prefetch=2,
        grid=(count,),
        in_specs=[pl.BlockSpec((1, slots, width), lambda r, *_: (r + offset, 0, 0)),
                  full(cosine.shape), full(sine.shape)]
                 + [full((page_len, page_width)) for _ in blocks],
        out_specs=pl.BlockSpec((1, slots, per_group * HD), lambda r, *_: (r, 0, 0)),
    )
    return pl.pallas_call(
        functools.partial(attention_kernel, offset=offset),
        grid_spec=grid_spec,
        out_shape=jax.ShapeDtypeStruct((count, slots, per_group * HD), jnp.bfloat16),
    )(lengths, valid, qkv, cosine, sine, *blocks)

def project(own, w_out, tp_index, n_tp, group_width):
    if n_tp == 4:
        near = swapped(own, "tp", n_tp, 1)
        far = swapped(own, "tp", n_tp, 2)
        farther = swapped(far, "tp", n_tp, 1)
        parts = [(own, tp_index), (near, tp_index ^ 1), (far, tp_index ^ 2), (farther, tp_index ^ 3)]
    else:
        parts = [(own, tp_index)]
        for shift in range(1, n_tp):
            parts.append((shifted(own, "tp", n_tp, shift), (tp_index - shift) % n_tp))
    projected = None
    for block, group in parts:
        rows = lax.dynamic_slice_in_dim(w_out, group * group_width, group_width, 0)
        term = jnp.dot(block, rows, preferred_element_type=jnp.float32)
        projected = term if projected is None else projected + term
    return projected


def on_device(
    hidden, qkv, page_store, page_owner, page_slot, lengths, request_perm, w_out, post_gain,
    *, n_req, n_tp
):
    requests, slots, local_width = hidden.shape
    per_group = qkv.shape[3] // HD - 2
    token_rows = requests * slots
    tp_index = lax.axis_index("tp")

    blocks, valid = gather_prefix(page_store, page_owner, page_slot, n_req)

    device_row = lax.axis_index("req")
    my_requests = lax.dynamic_slice_in_dim(request_perm, device_row * requests, requests)
    matches = my_requests[:, None] == jnp.arange(lengths.shape[0], dtype=jnp.int32)[None, :]
    my_lengths = jnp.sum(jnp.where(matches, lengths[None, :], 0), 1)
    position = jnp.arange(slots, dtype=jnp.int32)
    live_mask = (position[None, :] < my_lengths[:, None]).astype(jnp.float32)

    prefix_len = page_store.shape[1] * page_owner.shape[0]
    cosine, sine = static_tables(prefix_len + np.arange(slots), HD)
    group_width = per_group * HD
    chunk = max(1, requests // 2)
    projected_parts = []
    for start in range(0, requests, chunk):
        attended = attend(qkv[:, :, 0], jnp.asarray(cosine), jnp.asarray(sine), blocks,
                          my_lengths, valid.astype(jnp.int32), start, chunk)
        own = attended.reshape(chunk * slots, per_group * HD)
        projected_parts.append(project(own, w_out, tp_index, n_tp, group_width))
    projected = jnp.concatenate(projected_parts, 0).reshape(requests, slots, local_width)

    squares = jnp.sum(projected * projected, -1)
    if n_tp == 4:
        branch_total = squares + swapped(squares, "tp", n_tp, 2)
        branch_total = branch_total + swapped(branch_total, "tp", n_tp, 1)
    else:
        branch_total = squares
        for shift in range(1, n_tp):
            branch_total = branch_total + shifted(squares, "tp", n_tp, shift)
    branch = projected * lax.rsqrt(branch_total / D + EPSILON)[..., None] * post_gain
    source = hidden.astype(jnp.float32)
    return ((source + branch) * live_mask[..., None]).astype(jnp.bfloat16)


def solution(mesh):
    placed = (
        P("req", None, "tp"),
        P("req", None, "tp", None),
        P("req", None, "tp", None),
        P(),
        P(),
        P(),
        P(),
        P(None, "tp"),
        P("tp"),
    )
    body = lambda *args: on_device(*args, n_req=mesh.shape["req"], n_tp=mesh.shape["tp"])
    return jax.shard_map(
        body, mesh=mesh, in_specs=placed, out_specs=P("req", None, "tp"), check_vma=False
    )
```

```python
import functools

import numpy as np
import jax
import jax.numpy as jnp
from jax import lax
from jax.experimental import pallas as pl
from jax.experimental.pallas import tpu as pltpu
from jax.sharding import PartitionSpec as P

D = 2304
HD = 256


EPSILON = 1e-06
SOFT_CAP = 50.0


def capped_exp(scores):
    return jnp.exp(SOFT_CAP * jnp.tanh(scores / SOFT_CAP))


def shifted(value, axis, size, shift):
    return lax.ppermute(value, axis, [(i, (i + shift) % size) for i in range(size)])


def swapped(value, axis, size, mask):
    return lax.ppermute(value, axis, [(i, i ^ mask) for i in range(size)])


def gather_prefix(page_store, page_owner, page_slot, n_req):
    device_row = lax.axis_index("req")
    page_count = page_owner.shape[0]
    if n_req <= page_count:
        mine = page_owner == device_row
        slot = jnp.sum(jnp.where(mine, page_slot, 0))
        own = page_store[0, :, 0]
        for index in range(1, page_store.shape[0]):
            own = jnp.where(slot == index, page_store[index, :, 0], own)
        blocks = [own]
        sources = [device_row]
        if n_req == 8:
            for mask in (1, 2, 3, 6):
                blocks.append(swapped(own, "req", n_req, mask))
                sources.append(device_row ^ mask)
            mirror = blocks[-1]
            for mask in (1, 2, 3):
                blocks.append(swapped(mirror, "req", n_req, mask))
                sources.append(device_row ^ 6 ^ mask)
        else:
            for shift in range(1, n_req):
                blocks.append(shifted(own, "req", n_req, shift))
                sources.append((device_row - shift) % n_req)
        sources = jnp.stack(sources)
        valid = jnp.any(page_owner[None, :] == sources[:, None], 1)
        return blocks, valid
    picked = page_store[page_slot][:, :, 0]
    held_here = page_owner == device_row
    offered = jnp.where(held_here[:, None, None], picked, jnp.zeros_like(picked))
    prefix = lax.psum(offered, "req")
    return [prefix[p] for p in range(page_count)], jnp.ones((page_count,), jnp.bool_)


def static_tables(positions, width):
    half_width = width // 2
    exponent = np.arange(half_width, dtype=np.float32) * np.float32(2.0) / np.float32(width)
    frequency = np.power(np.float32(10000.0), -exponent).astype(np.float32)
    angles = positions.astype(np.float32)[:, None] * frequency[None, :]
    return np.cos(angles).astype(np.float32), np.sin(angles).astype(np.float32)


def attention_kernel(length_ref, valid_ref, qkv_ref, cos_ref, sin_ref, *rest, offset):
    page_refs, out_ref = rest[:-1], rest[-1]
    request = pl.program_id(0) + offset
    slots = qkv_ref.shape[1]
    per_group = qkv_ref.shape[2] // HD - 2
    half = HD // 2
    cosine = cos_ref[...]
    sine = sin_ref[...]
    values_in = qkv_ref[0].astype(jnp.float32)

    def rope(part):
        first = part[:, :half]
        second = part[:, half:]
        return jnp.concatenate([first * cosine - second * sine, second * cosine + first * sine], -1)

    queries = jnp.concatenate(
        [(rope(values_in[:, q * HD:(q + 1) * HD]) * HD ** (-0.5)).astype(jnp.bfloat16)
         for q in range(per_group)], 0)
    fresh_keys = rope(values_in[:, per_group * HD:(per_group + 1) * HD]).astype(jnp.bfloat16)
    fresh_values = values_in[:, (per_group + 1) * HD:].astype(jnp.bfloat16)
    pages = [ref[...] for ref in page_refs]
    keys = jnp.concatenate([page[:, :HD] for page in pages] + [fresh_keys], 0)
    values = jnp.concatenate([page[:, HD:] for page in pages] + [fresh_values], 0)
    prefix_len = len(pages) * pages[0].shape[0]
    key_count = keys.shape[0]
    rows = queries.shape[0]

    scores = lax.dot_general(queries, keys, (((1,), (1,)), ((), ())),
                             preferred_element_type=jnp.float32)
    page_column = lax.broadcasted_iota(jnp.int32, (1, key_count), 1) // pages[0].shape[0]
    page_flag = jnp.zeros((1, key_count), jnp.int32)
    for index in range(len(pages)):
        page_flag = page_flag + jnp.where(page_column == index, valid_ref[index], 0)
    page_flag = page_flag.astype(jnp.float32)
    column = lax.broadcasted_iota(jnp.int32, (rows, key_count), 1)
    slot = lax.broadcasted_iota(jnp.int32, (rows, key_count), 0) % slots
    suffix_pos = column - prefix_len
    suffix_ok = (suffix_pos >= 0) & (suffix_pos <= slot) & (suffix_pos < length_ref[request])
    exps = capped_exp(scores)
    raw = jnp.where(suffix_ok, exps, jnp.where(column < prefix_len, exps * page_flag, 0.0))
    totals = jnp.sum(raw, -1, keepdims=True)
    weights = (raw / totals).astype(jnp.bfloat16)
    attended = jnp.dot(weights, values, preferred_element_type=jnp.float32).astype(jnp.bfloat16)
    out_ref[0] = jnp.concatenate(
        [attended[q * slots:(q + 1) * slots] for q in range(per_group)], 1)


def attend(qkv, cosine, sine, blocks, lengths, valid, offset, count):
    _, slots, width = qkv.shape
    per_group = width // HD - 2
    page_len, page_width = blocks[0].shape
    full = lambda shape: pl.BlockSpec(shape, lambda r, *_: (0,) * len(shape))
    grid_spec = pltpu.PrefetchScalarGridSpec(
        num_scalar_prefetch=2,
        grid=(count,),
        in_specs=[pl.BlockSpec((1, slots, width), lambda r, *_: (r + offset, 0, 0)),
                  full(cosine.shape), full(sine.shape)]
                 + [full((page_len, page_width)) for _ in blocks],
        out_specs=pl.BlockSpec((1, slots, per_group * HD), lambda r, *_: (r, 0, 0)),
    )
    return pl.pallas_call(
        functools.partial(attention_kernel, offset=offset),
        grid_spec=grid_spec,
        out_shape=jax.ShapeDtypeStruct((count, slots, per_group * HD), jnp.bfloat16),
    )(lengths, valid, qkv, cosine, sine, *blocks)

def exchange(own, tp_index, n_tp):
    if n_tp == 4:
        near = swapped(own, "tp", n_tp, 1)
        far = swapped(own, "tp", n_tp, 2)
        farther = swapped(far, "tp", n_tp, 1)
        return [(own, tp_index), (near, tp_index ^ 1), (far, tp_index ^ 2), (farther, tp_index ^ 3)]
    parts = [(own, tp_index)]
    for shift in range(1, n_tp):
        parts.append((shifted(own, "tp", n_tp, shift), (tp_index - shift) % n_tp))
    return parts

def on_device(
    hidden, qkv, page_store, page_owner, page_slot, lengths, request_perm, w_out, post_gain,
    *, n_req, n_tp
):
    requests, slots, local_width = hidden.shape
    per_group = qkv.shape[3] // HD - 2
    token_rows = requests * slots
    tp_index = lax.axis_index("tp")

    blocks, valid = gather_prefix(page_store, page_owner, page_slot, n_req)

    device_row = lax.axis_index("req")
    my_requests = lax.dynamic_slice_in_dim(request_perm, device_row * requests, requests)
    matches = my_requests[:, None] == jnp.arange(lengths.shape[0], dtype=jnp.int32)[None, :]
    my_lengths = jnp.sum(jnp.where(matches, lengths[None, :], 0), 1)
    position = jnp.arange(slots, dtype=jnp.int32)
    live_mask = (position[None, :] < my_lengths[:, None]).astype(jnp.float32)

    prefix_len = page_store.shape[1] * page_owner.shape[0]
    cosine, sine = static_tables(prefix_len + np.arange(slots), HD)
    group_width = per_group * HD
    chunk = max(1, requests // 2)
    chunk_parts = []
    for start in range(0, requests, chunk):
        attended = attend(qkv[:, :, 0], jnp.asarray(cosine), jnp.asarray(sine), blocks,
                          my_lengths, valid.astype(jnp.int32), start, chunk)
        chunk_parts.append(exchange(attended.reshape(chunk * slots, per_group * HD), tp_index, n_tp))
    projected = None
    for number in range(n_tp):
        block = jnp.concatenate([parts[number][0] for parts in chunk_parts], 0)
        group = chunk_parts[0][number][1]
        rows = lax.dynamic_slice_in_dim(w_out, group * group_width, group_width, 0)
        term = jnp.dot(block, rows, preferred_element_type=jnp.float32)
        projected = term if projected is None else projected + term
    projected = projected.reshape(requests, slots, local_width)

    squares = jnp.sum(projected * projected, -1)
    branch_total = squares
    for shift in range(1, n_tp):
        branch_total = branch_total + shifted(squares, "tp", n_tp, shift)
    branch = projected * lax.rsqrt(branch_total / D + EPSILON)[..., None] * post_gain
    source = hidden.astype(jnp.float32)
    return ((source + branch) * live_mask[..., None]).astype(jnp.bfloat16)


def solution(mesh):
    placed = (
        P("req", None, "tp"),
        P("req", None, "tp", None),
        P("req", None, "tp", None),
        P(),
        P(),
        P(),
        P(),
        P(None, "tp"),
        P("tp"),
    )
    body = lambda *args: on_device(*args, n_req=mesh.shape["req"], n_tp=mesh.shape["tp"])
    return jax.shard_map(
        body, mesh=mesh, in_specs=placed, out_specs=P("req", None, "tp"), check_vma=False
    )
```

```python
import functools

import numpy as np
import jax
import jax.numpy as jnp
from jax import lax
from jax.experimental import pallas as pl
from jax.experimental.pallas import tpu as pltpu
from jax.sharding import PartitionSpec as P

D = 2304
HD = 256


EPSILON = 1e-06
SOFT_CAP = 50.0


def capped_exp(scores):
    return jnp.exp(SOFT_CAP * jnp.tanh(scores / SOFT_CAP))


def shifted(value, axis, size, shift):
    return lax.ppermute(value, axis, [(i, (i + shift) % size) for i in range(size)])


def swapped(value, axis, size, mask):
    return lax.ppermute(value, axis, [(i, i ^ mask) for i in range(size)])


def gather_prefix(page_store, page_owner, page_slot, n_req):
    device_row = lax.axis_index("req")
    page_count = page_owner.shape[0]
    if n_req <= page_count:
        mine = page_owner == device_row
        slot = jnp.sum(jnp.where(mine, page_slot, 0))
        own = page_store[0, :, 0]
        for index in range(1, page_store.shape[0]):
            own = jnp.where(slot == index, page_store[index, :, 0], own)
        blocks = [own]
        sources = [device_row]
        if n_req == 8:
            for mask in (1, 2, 3, 6):
                blocks.append(swapped(own, "req", n_req, mask))
                sources.append(device_row ^ mask)
            mirror = blocks[-1]
            for mask in (1, 2, 3):
                blocks.append(swapped(mirror, "req", n_req, mask))
                sources.append(device_row ^ 6 ^ mask)
        else:
            for shift in range(1, n_req):
                blocks.append(shifted(own, "req", n_req, shift))
                sources.append((device_row - shift) % n_req)
        sources = jnp.stack(sources)
        valid = jnp.any(page_owner[None, :] == sources[:, None], 1)
        return blocks, valid
    picked = page_store[page_slot][:, :, 0]
    held_here = page_owner == device_row
    offered = jnp.where(held_here[:, None, None], picked, jnp.zeros_like(picked))
    prefix = lax.psum(offered, "req")
    return [prefix[p] for p in range(page_count)], jnp.ones((page_count,), jnp.bool_)


def static_tables(positions, width):
    half_width = width // 2
    exponent = np.arange(half_width, dtype=np.float32) * np.float32(2.0) / np.float32(width)
    frequency = np.power(np.float32(10000.0), -exponent).astype(np.float32)
    angles = positions.astype(np.float32)[:, None] * frequency[None, :]
    return np.cos(angles).astype(np.float32), np.sin(angles).astype(np.float32)


def attention_kernel(limit_ref, flag_ref, qkv_ref, cos_ref, sin_ref, *rest):
    page_refs, out_ref = rest[:-1], rest[-1]
    slots = qkv_ref.shape[1]
    per_group = qkv_ref.shape[2] // HD - 2
    half = HD // 2
    cosine = cos_ref[...]
    sine = sin_ref[...]
    values_in = qkv_ref[0].astype(jnp.float32)

    def rope(part):
        first = part[:, :half]
        second = part[:, half:]
        return jnp.concatenate([first * cosine - second * sine, second * cosine + first * sine], -1)

    queries = jnp.concatenate(
        [(rope(values_in[:, q * HD:(q + 1) * HD]) * HD ** (-0.5)).astype(jnp.bfloat16)
         for q in range(per_group)], 0)
    fresh_keys = rope(values_in[:, per_group * HD:(per_group + 1) * HD]).astype(jnp.bfloat16)
    fresh_values = values_in[:, (per_group + 1) * HD:].astype(jnp.bfloat16)
    pages = [ref[...] for ref in page_refs]
    keys = jnp.concatenate([page[:, :HD] for page in pages] + [fresh_keys], 0)
    values = jnp.concatenate([page[:, HD:] for page in pages] + [fresh_values], 0)
    prefix_len = len(pages) * pages[0].shape[0]
    key_count = keys.shape[0]
    rows = queries.shape[0]

    scores = lax.dot_general(queries, keys, (((1,), (1,)), ((), ())),
                             preferred_element_type=jnp.float32)
    column = lax.broadcasted_iota(jnp.int32, (rows, key_count), 1)
    slot = lax.broadcasted_iota(jnp.int32, (rows, key_count), 0) % slots
    suffix_pos = column - prefix_len
    limit = limit_ref[0]
    suffix_ok = (suffix_pos <= slot) & (suffix_pos < limit)
    exps = capped_exp(scores) * flag_ref[...]
    raw = jnp.where(suffix_ok, exps, 0.0)
    totals = jnp.sum(raw, -1, keepdims=True)
    weights = (raw / totals).astype(jnp.bfloat16)
    attended = jnp.dot(weights, values, preferred_element_type=jnp.float32).astype(jnp.bfloat16)
    out_ref[0] = jnp.concatenate(
        [attended[q * slots:(q + 1) * slots] for q in range(per_group)], 1)


def attend(qkv, cosine, sine, blocks, lengths, valid, offset, count):
    requests, slots, width = qkv.shape
    per_group = width // HD - 2
    page_len, page_width = blocks[0].shape
    prefix_len = page_len * len(blocks)
    key_count = prefix_len + slots
    flags = jnp.concatenate([jnp.repeat(valid.astype(jnp.float32), page_len),
                             jnp.ones((slots,), jnp.float32)])
    flags = flags[None, :]
    limits = jnp.concatenate(
        [jnp.broadcast_to(jnp.full((requests, 1), prefix_len + slots, jnp.int32), (requests, prefix_len)),
         jnp.broadcast_to(lengths[:, None], (requests, slots))], 1)
    limits = limits[:, None, :]
    full = lambda shape: pl.BlockSpec(shape, lambda r: (0,) * len(shape))
    return pl.pallas_call(
        attention_kernel,
        grid=(count,),
        in_specs=[pl.BlockSpec((1, 1, key_count), lambda r: (r + offset, 0, 0)),
                  full((1, key_count)),
                  pl.BlockSpec((1, slots, width), lambda r: (r + offset, 0, 0)),
                  full(cosine.shape), full(sine.shape)]
                 + [full((page_len, page_width)) for _ in blocks],
        out_specs=pl.BlockSpec((1, slots, per_group * HD), lambda r: (r, 0, 0)),
        out_shape=jax.ShapeDtypeStruct((count, slots, per_group * HD), jnp.bfloat16),
    )(limits, flags, qkv, cosine, sine, *blocks)

def project(own, w_out, tp_index, n_tp, group_width):
    if n_tp == 4:
        near = swapped(own, "tp", n_tp, 1)
        far = swapped(own, "tp", n_tp, 2)
        farther = swapped(far, "tp", n_tp, 1)
        parts = [(own, tp_index), (near, tp_index ^ 1), (far, tp_index ^ 2), (farther, tp_index ^ 3)]
    else:
        parts = [(own, tp_index)]
        for shift in range(1, n_tp):
            parts.append((shifted(own, "tp", n_tp, shift), (tp_index - shift) % n_tp))
    projected = None
    for block, group in parts:
        rows = lax.dynamic_slice_in_dim(w_out, group * group_width, group_width, 0)
        term = jnp.dot(block, rows, preferred_element_type=jnp.float32)
        projected = term if projected is None else projected + term
    return projected


def on_device(
    hidden, qkv, page_store, page_owner, page_slot, lengths, request_perm, w_out, post_gain,
    *, n_req, n_tp
):
    requests, slots, local_width = hidden.shape
    per_group = qkv.shape[3] // HD - 2
    token_rows = requests * slots
    tp_index = lax.axis_index("tp")

    blocks, valid = gather_prefix(page_store, page_owner, page_slot, n_req)

    device_row = lax.axis_index("req")
    my_requests = lax.dynamic_slice_in_dim(request_perm, device_row * requests, requests)
    matches = my_requests[:, None] == jnp.arange(lengths.shape[0], dtype=jnp.int32)[None, :]
    my_lengths = jnp.sum(jnp.where(matches, lengths[None, :], 0), 1)
    position = jnp.arange(slots, dtype=jnp.int32)
    live_mask = (position[None, :] < my_lengths[:, None]).astype(jnp.float32)

    prefix_len = page_store.shape[1] * page_owner.shape[0]
    cosine, sine = static_tables(prefix_len + np.arange(slots), HD)
    group_width = per_group * HD
    chunk = max(1, requests // 2)
    projected_parts = []
    for start in range(0, requests, chunk):
        attended = attend(qkv[:, :, 0], jnp.asarray(cosine), jnp.asarray(sine), blocks,
                          my_lengths, valid.astype(jnp.int32), start, chunk)
        own = attended.reshape(chunk * slots, per_group * HD)
        projected_parts.append(project(own, w_out, tp_index, n_tp, group_width))
    projected = jnp.concatenate(projected_parts, 0).reshape(requests, slots, local_width)

    squares = jnp.sum(projected * projected, -1)
    branch_total = squares
    for shift in range(1, n_tp):
        branch_total = branch_total + shifted(squares, "tp", n_tp, shift)
    branch = projected * lax.rsqrt(branch_total / D + EPSILON)[..., None] * post_gain
    source = hidden.astype(jnp.float32)
    return ((source + branch) * live_mask[..., None]).astype(jnp.bfloat16)


def solution(mesh):
    placed = (
        P("req", None, "tp"),
        P("req", None, "tp", None),
        P("req", None, "tp", None),
        P(),
        P(),
        P(),
        P(),
        P(None, "tp"),
        P("tp"),
    )
    body = lambda *args: on_device(*args, n_req=mesh.shape["req"], n_tp=mesh.shape["tp"])
    return jax.shard_map(
        body, mesh=mesh, in_specs=placed, out_specs=P("req", None, "tp"), check_vma=False
    )
```

```python
import functools

import numpy as np
import jax
import jax.numpy as jnp
from jax import lax
from jax.experimental import pallas as pl
from jax.experimental.pallas import tpu as pltpu
from jax.sharding import PartitionSpec as P

D = 2304
HD = 256


EPSILON = 1e-06
SOFT_CAP = 50.0


def capped_exp(scores):
    return jnp.exp(SOFT_CAP * jnp.tanh(scores / SOFT_CAP))


def shifted(value, axis, size, shift):
    return lax.ppermute(value, axis, [(i, (i + shift) % size) for i in range(size)])


def swapped(value, axis, size, mask):
    return lax.ppermute(value, axis, [(i, i ^ mask) for i in range(size)])


def gather_prefix(page_store, page_owner, page_slot, n_req):
    device_row = lax.axis_index("req")
    page_count = page_owner.shape[0]
    if n_req <= page_count:
        mine = page_owner == device_row
        slot = jnp.sum(jnp.where(mine, page_slot, 0))
        own = page_store[0, :, 0]
        for index in range(1, page_store.shape[0]):
            own = jnp.where(slot == index, page_store[index, :, 0], own)
        blocks = [own]
        sources = [device_row]
        if n_req == 8:
            for mask in (1, 2, 3, 6):
                blocks.append(swapped(own, "req", n_req, mask))
                sources.append(device_row ^ mask)
            mirror = blocks[-1]
            for mask in (1, 2, 3):
                blocks.append(swapped(mirror, "req", n_req, mask))
                sources.append(device_row ^ 6 ^ mask)
        else:
            for shift in range(1, n_req):
                blocks.append(shifted(own, "req", n_req, shift))
                sources.append((device_row - shift) % n_req)
        sources = jnp.stack(sources)
        valid = jnp.any(page_owner[None, :] == sources[:, None], 1)
        return blocks, valid
    picked = page_store[page_slot][:, :, 0]
    held_here = page_owner == device_row
    offered = jnp.where(held_here[:, None, None], picked, jnp.zeros_like(picked))
    prefix = lax.psum(offered, "req")
    return [prefix[p] for p in range(page_count)], jnp.ones((page_count,), jnp.bool_)


def static_tables(positions, width):
    half_width = width // 2
    exponent = np.arange(half_width, dtype=np.float32) * np.float32(2.0) / np.float32(width)
    frequency = np.power(np.float32(10000.0), -exponent).astype(np.float32)
    angles = positions.astype(np.float32)[:, None] * frequency[None, :]
    return np.cos(angles).astype(np.float32), np.sin(angles).astype(np.float32)


def attention_kernel(limit_ref, flag_ref, qkv_ref, cos_ref, sin_ref, *rest):
    page_refs, out_ref = rest[:-1], rest[-1]
    count, slots = qkv_ref.shape[0], qkv_ref.shape[1]
    per_group = qkv_ref.shape[2] // HD - 2
    half = HD // 2
    cosine = cos_ref[...]
    sine = sin_ref[...]
    pages = [ref[...] for ref in page_refs]
    prefix_keys = [page[:, :HD] for page in pages]
    prefix_values = [page[:, HD:] for page in pages]
    prefix_len = len(pages) * pages[0].shape[0]
    flag = flag_ref[...]

    def rope(part):
        first = part[:, :half]
        second = part[:, half:]
        return jnp.concatenate([first * cosine - second * sine, second * cosine + first * sine], -1)

    for request in range(count):
        values_in = qkv_ref[request].astype(jnp.float32)
        queries = jnp.concatenate(
            [(rope(values_in[:, q * HD:(q + 1) * HD]) * HD ** (-0.5)).astype(jnp.bfloat16)
             for q in range(per_group)], 0)
        fresh_keys = rope(values_in[:, per_group * HD:(per_group + 1) * HD]).astype(jnp.bfloat16)
        fresh_values = values_in[:, (per_group + 1) * HD:].astype(jnp.bfloat16)
        keys = jnp.concatenate(prefix_keys + [fresh_keys], 0)
        values = jnp.concatenate(prefix_values + [fresh_values], 0)
        key_count = keys.shape[0]
        rows = queries.shape[0]
        scores = lax.dot_general(queries, keys, (((1,), (1,)), ((), ())),
                                 preferred_element_type=jnp.float32)
        column = lax.broadcasted_iota(jnp.int32, (rows, key_count), 1)
        slot = lax.broadcasted_iota(jnp.int32, (rows, key_count), 0) % slots
        suffix_pos = column - prefix_len
        suffix_ok = (suffix_pos <= slot) & (suffix_pos < limit_ref[request])
        raw = jnp.where(suffix_ok, capped_exp(scores) * flag, 0.0)
        totals = jnp.sum(raw, -1, keepdims=True)
        weights = (raw / totals).astype(jnp.bfloat16)
        attended = jnp.dot(weights, values, preferred_element_type=jnp.float32).astype(jnp.bfloat16)
        out_ref[request] = jnp.concatenate(
            [attended[q * slots:(q + 1) * slots] for q in range(per_group)], 1)


def attend(qkv, cosine, sine, blocks, lengths, valid, offset, count):
    requests, slots, width = qkv.shape
    per_group = width // HD - 2
    page_len, page_width = blocks[0].shape
    prefix_len = page_len * len(blocks)
    key_count = prefix_len + slots
    flags = jnp.concatenate([jnp.repeat(valid.astype(jnp.float32), page_len),
                             jnp.ones((slots,), jnp.float32)])
    flags = flags[None, :]
    limits = jnp.concatenate(
        [jnp.broadcast_to(jnp.full((requests, 1), prefix_len + slots, jnp.int32), (requests, prefix_len)),
         jnp.broadcast_to(lengths[:, None], (requests, slots))], 1)
    limits = limits[:, None, :]
    chunk = offset // count
    full = lambda shape: pl.BlockSpec(shape, lambda r: (0,) * len(shape))
    return pl.pallas_call(
        attention_kernel,
        grid=(1,),
        in_specs=[pl.BlockSpec((count, 1, key_count), lambda r: (chunk, 0, 0)),
                  full((1, key_count)),
                  pl.BlockSpec((count, slots, width), lambda r: (chunk, 0, 0)),
                  full(cosine.shape), full(sine.shape)]
                 + [full((page_len, page_width)) for _ in blocks],
        out_specs=pl.BlockSpec((count, slots, per_group * HD), lambda r: (0, 0, 0)),
        out_shape=jax.ShapeDtypeStruct((count, slots, per_group * HD), jnp.bfloat16),
    )(limits, flags, qkv, cosine, sine, *blocks)

def project(own, w_out, tp_index, n_tp, group_width):
    if n_tp == 4:
        near = swapped(own, "tp", n_tp, 1)
        far = swapped(own, "tp", n_tp, 2)
        farther = swapped(far, "tp", n_tp, 1)
        parts = [(own, tp_index), (near, tp_index ^ 1), (far, tp_index ^ 2), (farther, tp_index ^ 3)]
    else:
        parts = [(own, tp_index)]
        for shift in range(1, n_tp):
            parts.append((shifted(own, "tp", n_tp, shift), (tp_index - shift) % n_tp))
    projected = None
    for block, group in parts:
        rows = lax.dynamic_slice_in_dim(w_out, group * group_width, group_width, 0)
        term = jnp.dot(block, rows, preferred_element_type=jnp.float32)
        projected = term if projected is None else projected + term
    return projected


def on_device(
    hidden, qkv, page_store, page_owner, page_slot, lengths, request_perm, w_out, post_gain,
    *, n_req, n_tp
):
    requests, slots, local_width = hidden.shape
    per_group = qkv.shape[3] // HD - 2
    token_rows = requests * slots
    tp_index = lax.axis_index("tp")

    blocks, valid = gather_prefix(page_store, page_owner, page_slot, n_req)

    device_row = lax.axis_index("req")
    my_requests = lax.dynamic_slice_in_dim(request_perm, device_row * requests, requests)
    matches = my_requests[:, None] == jnp.arange(lengths.shape[0], dtype=jnp.int32)[None, :]
    my_lengths = jnp.sum(jnp.where(matches, lengths[None, :], 0), 1)
    position = jnp.arange(slots, dtype=jnp.int32)
    live_mask = (position[None, :] < my_lengths[:, None]).astype(jnp.float32)

    prefix_len = page_store.shape[1] * page_owner.shape[0]
    cosine, sine = static_tables(prefix_len + np.arange(slots), HD)
    group_width = per_group * HD
    chunk = max(1, requests // 2)
    projected_parts = []
    for start in range(0, requests, chunk):
        attended = attend(qkv[:, :, 0], jnp.asarray(cosine), jnp.asarray(sine), blocks,
                          my_lengths, valid.astype(jnp.int32), start, chunk)
        own = attended.reshape(chunk * slots, per_group * HD)
        projected_parts.append(project(own, w_out, tp_index, n_tp, group_width))
    projected = jnp.concatenate(projected_parts, 0).reshape(requests, slots, local_width)

    squares = jnp.sum(projected * projected, -1)
    branch_total = squares
    for shift in range(1, n_tp):
        branch_total = branch_total + shifted(squares, "tp", n_tp, shift)
    branch = projected * lax.rsqrt(branch_total / D + EPSILON)[..., None] * post_gain
    source = hidden.astype(jnp.float32)
    return ((source + branch) * live_mask[..., None]).astype(jnp.bfloat16)


def solution(mesh):
    placed = (
        P("req", None, "tp"),
        P("req", None, "tp", None),
        P("req", None, "tp", None),
        P(),
        P(),
        P(),
        P(),
        P(None, "tp"),
        P("tp"),
    )
    body = lambda *args: on_device(*args, n_req=mesh.shape["req"], n_tp=mesh.shape["tp"])
    return jax.shard_map(
        body, mesh=mesh, in_specs=placed, out_specs=P("req", None, "tp"), check_vma=False
    )
```

```python
import functools

import numpy as np
import jax
import jax.numpy as jnp
from jax import lax
from jax.experimental import pallas as pl
from jax.experimental.pallas import tpu as pltpu
from jax.sharding import PartitionSpec as P

D = 2304
HD = 256


EPSILON = 1e-06
SOFT_CAP = 50.0


def capped_exp(scores):
    return jnp.exp(SOFT_CAP * jnp.tanh(scores / SOFT_CAP))


def shifted(value, axis, size, shift):
    return lax.ppermute(value, axis, [(i, (i + shift) % size) for i in range(size)])


def swapped(value, axis, size, mask):
    return lax.ppermute(value, axis, [(i, i ^ mask) for i in range(size)])


def gather_prefix(page_store, page_owner, page_slot, n_req):
    device_row = lax.axis_index("req")
    page_count = page_owner.shape[0]
    if n_req <= page_count:
        mine = page_owner == device_row
        slot = jnp.sum(jnp.where(mine, page_slot, 0))
        own = page_store[0, :, 0]
        for index in range(1, page_store.shape[0]):
            own = jnp.where(slot == index, page_store[index, :, 0], own)
        blocks = [own]
        sources = [device_row]
        if n_req == 8:
            for mask in (1, 2, 3, 6):
                blocks.append(swapped(own, "req", n_req, mask))
                sources.append(device_row ^ mask)
            mirror = blocks[-1]
            for mask in (1, 2, 3):
                blocks.append(swapped(mirror, "req", n_req, mask))
                sources.append(device_row ^ 6 ^ mask)
        else:
            for shift in range(1, n_req):
                blocks.append(shifted(own, "req", n_req, shift))
                sources.append((device_row - shift) % n_req)
        sources = jnp.stack(sources)
        valid = jnp.any(page_owner[None, :] == sources[:, None], 1)
        return blocks, valid
    picked = page_store[page_slot][:, :, 0]
    held_here = page_owner == device_row
    offered = jnp.where(held_here[:, None, None], picked, jnp.zeros_like(picked))
    prefix = lax.psum(offered, "req")
    return [prefix[p] for p in range(page_count)], jnp.ones((page_count,), jnp.bool_)


def static_tables(positions, width):
    half_width = width // 2
    exponent = np.arange(half_width, dtype=np.float32) * np.float32(2.0) / np.float32(width)
    frequency = np.power(np.float32(10000.0), -exponent).astype(np.float32)
    angles = positions.astype(np.float32)[:, None] * frequency[None, :]
    return np.cos(angles).astype(np.float32), np.sin(angles).astype(np.float32)


def attention_kernel(limit_ref, flag_ref, qkv_ref, cos_ref, sin_ref, *rest):
    page_refs, out_ref = rest[:-1], rest[-1]
    count, slots = qkv_ref.shape[0], qkv_ref.shape[1]
    per_group = qkv_ref.shape[2] // HD - 2
    half = HD // 2
    cosine = cos_ref[...]
    sine = sin_ref[...]
    pages = [ref[...] for ref in page_refs]
    prefix_keys = [page[:, :HD] for page in pages]
    prefix_values = [page[:, HD:] for page in pages]
    prefix_len = len(pages) * pages[0].shape[0]
    flag = flag_ref[...]

    def rope(part):
        first = part[:, :half]
        second = part[:, half:]
        return jnp.concatenate([first * cosine - second * sine, second * cosine + first * sine], -1)

    queries, fresh = [], []
    for request in range(count):
        values_in = qkv_ref[request].astype(jnp.float32)
        queries.append(jnp.concatenate(
            [(rope(values_in[:, q * HD:(q + 1) * HD]) * HD ** (-0.5)).astype(jnp.bfloat16)
             for q in range(per_group)], 0))
        fresh.append((rope(values_in[:, per_group * HD:(per_group + 1) * HD]).astype(jnp.bfloat16),
                      values_in[:, (per_group + 1) * HD:].astype(jnp.bfloat16)))
    rows = queries[0].shape[0]
    contract = (((1,), (1,)), ((), ()))
    prefix_raw = capped_exp(lax.dot_general(
        jnp.concatenate(queries, 0), jnp.concatenate(prefix_keys, 0), contract,
        preferred_element_type=jnp.float32)) * flag[:, :prefix_len]
    prefix_value_rows = jnp.concatenate(prefix_values, 0)
    for request in range(count):
        fresh_keys, fresh_values = fresh[request]
        scores = lax.dot_general(queries[request], fresh_keys, contract,
                                 preferred_element_type=jnp.float32)
        column = lax.broadcasted_iota(jnp.int32, scores.shape, 1)
        slot = lax.broadcasted_iota(jnp.int32, scores.shape, 0) % slots
        allowed = (column <= slot) & (column < limit_ref[request][:, prefix_len:])
        suffix_raw = jnp.where(allowed, capped_exp(scores), 0.0)
        page_raw = prefix_raw[request * rows:(request + 1) * rows]
        totals = jnp.sum(page_raw, -1, keepdims=True) + jnp.sum(suffix_raw, -1, keepdims=True)
        attended = jnp.dot((page_raw / totals).astype(jnp.bfloat16), prefix_value_rows,
                           preferred_element_type=jnp.float32)
        attended = attended + jnp.dot((suffix_raw / totals).astype(jnp.bfloat16), fresh_values,
                                      preferred_element_type=jnp.float32)
        attended = attended.astype(jnp.bfloat16)
        out_ref[request] = jnp.concatenate(
            [attended[q * slots:(q + 1) * slots] for q in range(per_group)], 1)


def attend(qkv, cosine, sine, blocks, lengths, valid, offset, count):
    requests, slots, width = qkv.shape
    per_group = width // HD - 2
    page_len, page_width = blocks[0].shape
    prefix_len = page_len * len(blocks)
    key_count = prefix_len + slots
    flags = jnp.concatenate([jnp.repeat(valid.astype(jnp.float32), page_len),
                             jnp.ones((slots,), jnp.float32)])
    flags = flags[None, :]
    limits = jnp.concatenate(
        [jnp.broadcast_to(jnp.full((requests, 1), prefix_len + slots, jnp.int32), (requests, prefix_len)),
         jnp.broadcast_to(lengths[:, None], (requests, slots))], 1)
    limits = limits[:, None, :]
    chunk = offset // count
    full = lambda shape: pl.BlockSpec(shape, lambda r: (0,) * len(shape))
    return pl.pallas_call(
        attention_kernel,
        grid=(1,),
        in_specs=[pl.BlockSpec((count, 1, key_count), lambda r: (chunk, 0, 0)),
                  full((1, key_count)),
                  pl.BlockSpec((count, slots, width), lambda r: (chunk, 0, 0)),
                  full(cosine.shape), full(sine.shape)]
                 + [full((page_len, page_width)) for _ in blocks],
        out_specs=pl.BlockSpec((count, slots, per_group * HD), lambda r: (0, 0, 0)),
        out_shape=jax.ShapeDtypeStruct((count, slots, per_group * HD), jnp.bfloat16),
    )(limits, flags, qkv, cosine, sine, *blocks)

def project(own, w_out, tp_index, n_tp, group_width):
    if n_tp == 4:
        near = swapped(own, "tp", n_tp, 1)
        far = swapped(own, "tp", n_tp, 2)
        farther = swapped(far, "tp", n_tp, 1)
        parts = [(own, tp_index), (near, tp_index ^ 1), (far, tp_index ^ 2), (farther, tp_index ^ 3)]
    else:
        parts = [(own, tp_index)]
        for shift in range(1, n_tp):
            parts.append((shifted(own, "tp", n_tp, shift), (tp_index - shift) % n_tp))
    projected = None
    for block, group in parts:
        rows = lax.dynamic_slice_in_dim(w_out, group * group_width, group_width, 0)
        term = jnp.dot(block, rows, preferred_element_type=jnp.float32)
        projected = term if projected is None else projected + term
    return projected


def on_device(
    hidden, qkv, page_store, page_owner, page_slot, lengths, request_perm, w_out, post_gain,
    *, n_req, n_tp
):
    requests, slots, local_width = hidden.shape
    per_group = qkv.shape[3] // HD - 2
    token_rows = requests * slots
    tp_index = lax.axis_index("tp")

    blocks, valid = gather_prefix(page_store, page_owner, page_slot, n_req)

    device_row = lax.axis_index("req")
    my_requests = lax.dynamic_slice_in_dim(request_perm, device_row * requests, requests)
    matches = my_requests[:, None] == jnp.arange(lengths.shape[0], dtype=jnp.int32)[None, :]
    my_lengths = jnp.sum(jnp.where(matches, lengths[None, :], 0), 1)
    position = jnp.arange(slots, dtype=jnp.int32)
    live_mask = (position[None, :] < my_lengths[:, None]).astype(jnp.float32)

    prefix_len = page_store.shape[1] * page_owner.shape[0]
    cosine, sine = static_tables(prefix_len + np.arange(slots), HD)
    group_width = per_group * HD
    chunk = max(1, requests // 2)
    projected_parts = []
    for start in range(0, requests, chunk):
        attended = attend(qkv[:, :, 0], jnp.asarray(cosine), jnp.asarray(sine), blocks,
                          my_lengths, valid.astype(jnp.int32), start, chunk)
        own = attended.reshape(chunk * slots, per_group * HD)
        projected_parts.append(project(own, w_out, tp_index, n_tp, group_width))
    projected = jnp.concatenate(projected_parts, 0).reshape(requests, slots, local_width)

    squares = jnp.sum(projected * projected, -1)
    branch_total = squares
    for shift in range(1, n_tp):
        branch_total = branch_total + shifted(squares, "tp", n_tp, shift)
    branch = projected * lax.rsqrt(branch_total / D + EPSILON)[..., None] * post_gain
    source = hidden.astype(jnp.float32)
    return ((source + branch) * live_mask[..., None]).astype(jnp.bfloat16)


def solution(mesh):
    placed = (
        P("req", None, "tp"),
        P("req", None, "tp", None),
        P("req", None, "tp", None),
        P(),
        P(),
        P(),
        P(),
        P(None, "tp"),
        P("tp"),
    )
    body = lambda *args: on_device(*args, n_req=mesh.shape["req"], n_tp=mesh.shape["tp"])
    return jax.shard_map(
        body, mesh=mesh, in_specs=placed, out_specs=P("req", None, "tp"), check_vma=False
    )
```

```python
import functools

import numpy as np
import jax
import jax.numpy as jnp
from jax import lax
from jax.experimental import pallas as pl
from jax.experimental.pallas import tpu as pltpu
from jax.sharding import PartitionSpec as P

D = 2304
HD = 256


EPSILON = 1e-06
SOFT_CAP = 50.0


def capped_exp(scores):
    return jnp.exp(SOFT_CAP * jnp.tanh(scores / SOFT_CAP))


def shifted(value, axis, size, shift):
    return lax.ppermute(value, axis, [(i, (i + shift) % size) for i in range(size)])


def swapped(value, axis, size, mask):
    return lax.ppermute(value, axis, [(i, i ^ mask) for i in range(size)])


def gather_prefix(page_store, page_owner, page_slot, n_req):
    device_row = lax.axis_index("req")
    page_count = page_owner.shape[0]
    if n_req <= page_count:
        mine = page_owner == device_row
        slot = jnp.sum(jnp.where(mine, page_slot, 0))
        own = page_store[0, :, 0]
        for index in range(1, page_store.shape[0]):
            own = jnp.where(slot == index, page_store[index, :, 0], own)
        blocks = [own]
        sources = [device_row]
        if n_req == 8:
            for mask in (1, 2, 3, 6):
                blocks.append(swapped(own, "req", n_req, mask))
                sources.append(device_row ^ mask)
            mirror = blocks[-1]
            for mask in (1, 2, 3):
                blocks.append(swapped(mirror, "req", n_req, mask))
                sources.append(device_row ^ 6 ^ mask)
        else:
            for shift in range(1, n_req):
                blocks.append(shifted(own, "req", n_req, shift))
                sources.append((device_row - shift) % n_req)
        sources = jnp.stack(sources)
        valid = jnp.any(page_owner[None, :] == sources[:, None], 1)
        return blocks, valid
    picked = page_store[page_slot][:, :, 0]
    held_here = page_owner == device_row
    offered = jnp.where(held_here[:, None, None], picked, jnp.zeros_like(picked))
    prefix = lax.psum(offered, "req")
    return [prefix[p] for p in range(page_count)], jnp.ones((page_count,), jnp.bool_)


def static_tables(positions, width):
    half_width = width // 2
    exponent = np.arange(half_width, dtype=np.float32) * np.float32(2.0) / np.float32(width)
    frequency = np.power(np.float32(10000.0), -exponent).astype(np.float32)
    angles = positions.astype(np.float32)[:, None] * frequency[None, :]
    return np.cos(angles).astype(np.float32), np.sin(angles).astype(np.float32)


def attention_kernel(limit_ref, flag_ref, qkv_ref, cos_ref, sin_ref, *rest):
    page_refs, out_ref = rest[:-1], rest[-1]
    count, slots = qkv_ref.shape[0], qkv_ref.shape[1]
    per_group = qkv_ref.shape[2] // HD - 2
    half = HD // 2
    cosine = cos_ref[...]
    sine = sin_ref[...]
    pages = [ref[...] for ref in page_refs]
    prefix_keys = [page[:, :HD] for page in pages]
    prefix_values = [page[:, HD:] for page in pages]
    prefix_len = len(pages) * pages[0].shape[0]
    flag = flag_ref[...]

    def rope(part):
        first = part[:, :half]
        second = part[:, half:]
        return jnp.concatenate([first * cosine - second * sine, second * cosine + first * sine], -1)

    for request in range(count):
        values_in = qkv_ref[request].astype(jnp.float32)
        queries = jnp.concatenate(
            [(rope(values_in[:, q * HD:(q + 1) * HD]) * HD ** (-0.5)).astype(jnp.bfloat16)
             for q in range(per_group)], 0)
        fresh_keys = rope(values_in[:, per_group * HD:(per_group + 1) * HD]).astype(jnp.bfloat16)
        fresh_values = values_in[:, (per_group + 1) * HD:].astype(jnp.bfloat16)
        keys = jnp.concatenate(prefix_keys + [fresh_keys], 0)
        values = jnp.concatenate(prefix_values + [fresh_values], 0)
        key_count = keys.shape[0]
        rows = queries.shape[0]
        scores = lax.dot_general(queries, keys, (((1,), (1,)), ((), ())),
                                 preferred_element_type=jnp.float32)
        column = lax.broadcasted_iota(jnp.int32, (rows, key_count), 1)
        slot = lax.broadcasted_iota(jnp.int32, (rows, key_count), 0) % slots
        suffix_pos = column - prefix_len
        suffix_ok = (suffix_pos <= slot) & (suffix_pos < limit_ref[request])
        raw = jnp.where(suffix_ok, capped_exp(scores) * flag, 0.0)
        totals = jnp.sum(raw, -1, keepdims=True)
        weights = (raw / totals).astype(jnp.bfloat16)
        attended = jnp.dot(weights, values, preferred_element_type=jnp.float32).astype(jnp.bfloat16)
        out_ref[request] = jnp.concatenate(
            [attended[q * slots:(q + 1) * slots] for q in range(per_group)], 1)


def attend(qkv, cosine, sine, blocks, lengths, valid, offset, count):
    requests, slots, width = qkv.shape
    per_group = width // HD - 2
    page_len, page_width = blocks[0].shape
    prefix_len = page_len * len(blocks)
    key_count = prefix_len + slots
    flags = jnp.concatenate([jnp.repeat(valid.astype(jnp.float32), page_len),
                             jnp.ones((slots,), jnp.float32)])
    flags = flags[None, :]
    limits = jnp.concatenate(
        [jnp.broadcast_to(jnp.full((requests, 1), prefix_len + slots, jnp.int32), (requests, prefix_len)),
         jnp.broadcast_to(lengths[:, None], (requests, slots))], 1)
    limits = limits[:, None, :]
    chunk = offset // count
    full = lambda shape: pl.BlockSpec(shape, lambda r: (0,) * len(shape))
    return pl.pallas_call(
        attention_kernel,
        grid=(1,),
        in_specs=[pl.BlockSpec((count, 1, key_count), lambda r: (chunk, 0, 0)),
                  full((1, key_count)),
                  pl.BlockSpec((count, slots, width), lambda r: (chunk, 0, 0)),
                  full(cosine.shape), full(sine.shape)]
                 + [full((page_len, page_width)) for _ in blocks],
        out_specs=pl.BlockSpec((count, slots, per_group * HD), lambda r: (0, 0, 0)),
        out_shape=jax.ShapeDtypeStruct((count, slots, per_group * HD), jnp.bfloat16),
    )(limits, flags, qkv, cosine, sine, *blocks)

def exchange(own, tp_index, n_tp):
    if n_tp == 4:
        near = swapped(own, "tp", n_tp, 1)
        far = swapped(own, "tp", n_tp, 2)
        farther = swapped(far, "tp", n_tp, 1)
        return [(own, tp_index), (near, tp_index ^ 1), (far, tp_index ^ 2), (farther, tp_index ^ 3)]
    parts = [(own, tp_index)]
    for shift in range(1, n_tp):
        parts.append((shifted(own, "tp", n_tp, shift), (tp_index - shift) % n_tp))
    return parts


def products(parts, w_out, group_width, projected=None):
    for block, group in parts:
        rows = lax.dynamic_slice_in_dim(w_out, group * group_width, group_width, 0)
        term = jnp.dot(block, rows, preferred_element_type=jnp.float32)
        projected = term if projected is None else projected + term
    return projected

def on_device(
    hidden, qkv, page_store, page_owner, page_slot, lengths, request_perm, w_out, post_gain,
    *, n_req, n_tp
):
    requests, slots, local_width = hidden.shape
    per_group = qkv.shape[3] // HD - 2
    token_rows = requests * slots
    tp_index = lax.axis_index("tp")

    blocks, valid = gather_prefix(page_store, page_owner, page_slot, n_req)

    device_row = lax.axis_index("req")
    my_requests = lax.dynamic_slice_in_dim(request_perm, device_row * requests, requests)
    matches = my_requests[:, None] == jnp.arange(lengths.shape[0], dtype=jnp.int32)[None, :]
    my_lengths = jnp.sum(jnp.where(matches, lengths[None, :], 0), 1)
    position = jnp.arange(slots, dtype=jnp.int32)
    live_mask = (position[None, :] < my_lengths[:, None]).astype(jnp.float32)

    prefix_len = page_store.shape[1] * page_owner.shape[0]
    cosine, sine = static_tables(prefix_len + np.arange(slots), HD)
    group_width = per_group * HD
    chunk = max(1, requests // 2)
    qkv_rows = qkv[:, :, 0]
    projected_parts = []
    pending = None
    for start in range(0, requests, chunk):
        if pending is not None:
            early, late = pending
            early, qkv_rows = lax.optimization_barrier((early, qkv_rows))
            projected_parts.append(products(late, w_out, group_width, early))
        attended = attend(qkv_rows, jnp.asarray(cosine), jnp.asarray(sine), blocks,
                          my_lengths, valid.astype(jnp.int32), start, chunk)
        parts = exchange(attended.reshape(chunk * slots, per_group * HD), tp_index, n_tp)
        pending = (products(parts[:2], w_out, group_width), parts[2:])
    projected_parts.append(products(pending[1], w_out, group_width, pending[0]))
    projected = jnp.concatenate(projected_parts, 0).reshape(requests, slots, local_width)

    squares = jnp.sum(projected * projected, -1)
    branch_total = squares
    for shift in range(1, n_tp):
        branch_total = branch_total + shifted(squares, "tp", n_tp, shift)
    branch = projected * lax.rsqrt(branch_total / D + EPSILON)[..., None] * post_gain
    source = hidden.astype(jnp.float32)
    return ((source + branch) * live_mask[..., None]).astype(jnp.bfloat16)


def solution(mesh):
    placed = (
        P("req", None, "tp"),
        P("req", None, "tp", None),
        P("req", None, "tp", None),
        P(),
        P(),
        P(),
        P(),
        P(None, "tp"),
        P("tp"),
    )
    body = lambda *args: on_device(*args, n_req=mesh.shape["req"], n_tp=mesh.shape["tp"])
    return jax.shard_map(
        body, mesh=mesh, in_specs=placed, out_specs=P("req", None, "tp"), check_vma=False
    )
```

```python
import functools

import numpy as np
import jax
import jax.numpy as jnp
from jax import lax
from jax.experimental import pallas as pl
from jax.experimental.pallas import tpu as pltpu
from jax.sharding import PartitionSpec as P

D = 2304
HD = 256


EPSILON = 1e-06
SOFT_CAP = 50.0


def capped_exp(scores):
    return jnp.exp(SOFT_CAP * jnp.tanh(scores / SOFT_CAP))


def shifted(value, axis, size, shift):
    return lax.ppermute(value, axis, [(i, (i + shift) % size) for i in range(size)])


def swapped(value, axis, size, mask):
    return lax.ppermute(value, axis, [(i, i ^ mask) for i in range(size)])


def gather_prefix(page_store, page_owner, page_slot, n_req):
    device_row = lax.axis_index("req")
    page_count = page_owner.shape[0]
    if n_req <= page_count:
        mine = page_owner == device_row
        slot = jnp.sum(jnp.where(mine, page_slot, 0))
        own = page_store[0, :, 0]
        for index in range(1, page_store.shape[0]):
            own = jnp.where(slot == index, page_store[index, :, 0], own)
        blocks = [own]
        sources = [device_row]
        if n_req == 8:
            for mask in (1, 2, 3, 6):
                blocks.append(swapped(own, "req", n_req, mask))
                sources.append(device_row ^ mask)
            mirror = blocks[-1]
            for mask in (1, 2, 3):
                blocks.append(swapped(mirror, "req", n_req, mask))
                sources.append(device_row ^ 6 ^ mask)
        else:
            for shift in range(1, n_req):
                blocks.append(shifted(own, "req", n_req, shift))
                sources.append((device_row - shift) % n_req)
        sources = jnp.stack(sources)
        valid = jnp.any(page_owner[None, :] == sources[:, None], 1)
        return blocks, valid
    picked = page_store[page_slot][:, :, 0]
    held_here = page_owner == device_row
    offered = jnp.where(held_here[:, None, None], picked, jnp.zeros_like(picked))
    prefix = lax.psum(offered, "req")
    return [prefix[p] for p in range(page_count)], jnp.ones((page_count,), jnp.bool_)


def static_tables(positions, width):
    half_width = width // 2
    exponent = np.arange(half_width, dtype=np.float32) * np.float32(2.0) / np.float32(width)
    frequency = np.power(np.float32(10000.0), -exponent).astype(np.float32)
    angles = positions.astype(np.float32)[:, None] * frequency[None, :]
    return np.cos(angles).astype(np.float32), np.sin(angles).astype(np.float32)


def attention_kernel(limit_ref, flag_ref, qkv_ref, cos_ref, sin_ref, *rest):
    page_count = (len(rest) - 3)
    page_refs, out_ref, page_scratch, page_sems = rest[:page_count], rest[page_count], rest[-2], rest[-1]
    copies = [pltpu.make_async_copy(ref, page_scratch.at[index], page_sems.at[index])
              for index, ref in enumerate(page_refs)]
    for copy in copies:
        copy.start()
    count, slots = qkv_ref.shape[0], qkv_ref.shape[1]
    per_group = qkv_ref.shape[2] // HD - 2
    half = HD // 2
    cosine = cos_ref[...]
    sine = sin_ref[...]
    def rope(part):
        first = part[:, :half]
        second = part[:, half:]
        return jnp.concatenate([first * cosine - second * sine, second * cosine + first * sine], -1)

    ropes = []
    for request in range(count):
        values_in = qkv_ref[request].astype(jnp.float32)
        ropes.append((
            jnp.concatenate(
                [(rope(values_in[:, q * HD:(q + 1) * HD]) * HD ** (-0.5)).astype(jnp.bfloat16)
                 for q in range(per_group)], 0),
            rope(values_in[:, per_group * HD:(per_group + 1) * HD]).astype(jnp.bfloat16),
            values_in[:, (per_group + 1) * HD:].astype(jnp.bfloat16)))
    for copy in copies:
        copy.wait()
    pages = [page_scratch[index] for index in range(page_count)]
    prefix_keys = [page[:, :HD] for page in pages]
    prefix_values = [page[:, HD:] for page in pages]
    prefix_len = len(pages) * pages[0].shape[0]
    flag = flag_ref[...]

    for request in range(count):
        queries, fresh_keys, fresh_values = ropes[request]
        keys = jnp.concatenate(prefix_keys + [fresh_keys], 0)
        values = jnp.concatenate(prefix_values + [fresh_values], 0)
        key_count = keys.shape[0]
        rows = queries.shape[0]
        scores = lax.dot_general(queries, keys, (((1,), (1,)), ((), ())),
                                 preferred_element_type=jnp.float32)
        column = lax.broadcasted_iota(jnp.int32, (rows, key_count), 1)
        slot = lax.broadcasted_iota(jnp.int32, (rows, key_count), 0) % slots
        suffix_pos = column - prefix_len
        suffix_ok = (suffix_pos <= slot) & (suffix_pos < limit_ref[request])
        raw = jnp.where(suffix_ok, capped_exp(scores) * flag, 0.0)
        totals = jnp.sum(raw, -1, keepdims=True)
        weights = (raw / totals).astype(jnp.bfloat16)
        attended = jnp.dot(weights, values, preferred_element_type=jnp.float32).astype(jnp.bfloat16)
        out_ref[request] = jnp.concatenate(
            [attended[q * slots:(q + 1) * slots] for q in range(per_group)], 1)


def attend(qkv, cosine, sine, blocks, lengths, valid, offset, count):
    requests, slots, width = qkv.shape
    per_group = width // HD - 2
    page_len, page_width = blocks[0].shape
    prefix_len = page_len * len(blocks)
    key_count = prefix_len + slots
    flags = jnp.concatenate([jnp.repeat(valid.astype(jnp.float32), page_len),
                             jnp.ones((slots,), jnp.float32)])
    flags = flags[None, :]
    limits = jnp.concatenate(
        [jnp.broadcast_to(jnp.full((requests, 1), prefix_len + slots, jnp.int32), (requests, prefix_len)),
         jnp.broadcast_to(lengths[:, None], (requests, slots))], 1)
    limits = limits[:, None, :]
    chunk = offset // count
    full = lambda shape: pl.BlockSpec(shape, lambda r: (0,) * len(shape))
    return pl.pallas_call(
        attention_kernel,
        grid=(1,),
        in_specs=[pl.BlockSpec((count, 1, key_count), lambda r: (chunk, 0, 0)),
                  full((1, key_count)),
                  pl.BlockSpec((count, slots, width), lambda r: (chunk, 0, 0)),
                  full(cosine.shape), full(sine.shape)]
                 + [pl.BlockSpec(memory_space=pl.ANY) for _ in blocks],
        out_specs=pl.BlockSpec((count, slots, per_group * HD), lambda r: (0, 0, 0)),
        scratch_shapes=[pltpu.VMEM((len(blocks), page_len, page_width), jnp.bfloat16),
                        pltpu.SemaphoreType.DMA((len(blocks),))],
        out_shape=jax.ShapeDtypeStruct((count, slots, per_group * HD), jnp.bfloat16),
    )(limits, flags, qkv, cosine, sine, *blocks)

def project(own, w_out, tp_index, n_tp, group_width):
    if n_tp == 4:
        near = swapped(own, "tp", n_tp, 1)
        far = swapped(own, "tp", n_tp, 2)
        farther = swapped(far, "tp", n_tp, 1)
        parts = [(own, tp_index), (near, tp_index ^ 1), (far, tp_index ^ 2), (farther, tp_index ^ 3)]
    else:
        parts = [(own, tp_index)]
        for shift in range(1, n_tp):
            parts.append((shifted(own, "tp", n_tp, shift), (tp_index - shift) % n_tp))
    projected = None
    for block, group in parts:
        rows = lax.dynamic_slice_in_dim(w_out, group * group_width, group_width, 0)
        term = jnp.dot(block, rows, preferred_element_type=jnp.float32)
        projected = term if projected is None else projected + term
    return projected


def on_device(
    hidden, qkv, page_store, page_owner, page_slot, lengths, request_perm, w_out, post_gain,
    *, n_req, n_tp
):
    requests, slots, local_width = hidden.shape
    per_group = qkv.shape[3] // HD - 2
    token_rows = requests * slots
    tp_index = lax.axis_index("tp")

    blocks, valid = gather_prefix(page_store, page_owner, page_slot, n_req)

    device_row = lax.axis_index("req")
    my_requests = lax.dynamic_slice_in_dim(request_perm, device_row * requests, requests)
    matches = my_requests[:, None] == jnp.arange(lengths.shape[0], dtype=jnp.int32)[None, :]
    my_lengths = jnp.sum(jnp.where(matches, lengths[None, :], 0), 1)
    position = jnp.arange(slots, dtype=jnp.int32)
    live_mask = (position[None, :] < my_lengths[:, None]).astype(jnp.float32)

    prefix_len = page_store.shape[1] * page_owner.shape[0]
    cosine, sine = static_tables(prefix_len + np.arange(slots), HD)
    group_width = per_group * HD
    chunk = max(1, requests // 2)
    projected_parts = []
    for start in range(0, requests, chunk):
        attended = attend(qkv[:, :, 0], jnp.asarray(cosine), jnp.asarray(sine), blocks,
                          my_lengths, valid.astype(jnp.int32), start, chunk)
        own = attended.reshape(chunk * slots, per_group * HD)
        projected_parts.append(project(own, w_out, tp_index, n_tp, group_width))
    projected = jnp.concatenate(projected_parts, 0).reshape(requests, slots, local_width)

    squares = jnp.sum(projected * projected, -1)
    branch_total = squares
    for shift in range(1, n_tp):
        branch_total = branch_total + shifted(squares, "tp", n_tp, shift)
    branch = projected * lax.rsqrt(branch_total / D + EPSILON)[..., None] * post_gain
    source = hidden.astype(jnp.float32)
    return ((source + branch) * live_mask[..., None]).astype(jnp.bfloat16)


def solution(mesh):
    placed = (
        P("req", None, "tp"),
        P("req", None, "tp", None),
        P("req", None, "tp", None),
        P(),
        P(),
        P(),
        P(),
        P(None, "tp"),
        P("tp"),
    )
    body = lambda *args: on_device(*args, n_req=mesh.shape["req"], n_tp=mesh.shape["tp"])
    return jax.shard_map(
        body, mesh=mesh, in_specs=placed, out_specs=P("req", None, "tp"), check_vma=False
    )
```

```python
import functools

import numpy as np
import jax
import jax.numpy as jnp
from jax import lax
from jax.experimental import pallas as pl
from jax.experimental.pallas import tpu as pltpu
from jax.sharding import PartitionSpec as P

D = 2304
HD = 256


EPSILON = 1e-06
SOFT_CAP = 50.0


def capped_exp(scores):
    return jnp.exp(SOFT_CAP * jnp.tanh(scores / SOFT_CAP))


def shifted(value, axis, size, shift):
    return lax.ppermute(value, axis, [(i, (i + shift) % size) for i in range(size)])


def swapped(value, axis, size, mask):
    return lax.ppermute(value, axis, [(i, i ^ mask) for i in range(size)])


def gather_prefix(page_store, page_owner, page_slot, n_req):
    device_row = lax.axis_index("req")
    page_count = page_owner.shape[0]
    if n_req <= page_count:
        mine = page_owner == device_row
        slot = jnp.sum(jnp.where(mine, page_slot, 0))
        own = page_store[0, :, 0]
        for index in range(1, page_store.shape[0]):
            own = jnp.where(slot == index, page_store[index, :, 0], own)
        blocks = [own]
        sources = [device_row]
        if n_req == 8:
            for mask in (1, 2, 3, 6):
                blocks.append(swapped(own, "req", n_req, mask))
                sources.append(device_row ^ mask)
            mirror = blocks[-1]
            for mask in (1, 2, 3):
                blocks.append(swapped(mirror, "req", n_req, mask))
                sources.append(device_row ^ 6 ^ mask)
        else:
            for shift in range(1, n_req):
                blocks.append(shifted(own, "req", n_req, shift))
                sources.append((device_row - shift) % n_req)
        sources = jnp.stack(sources)
        valid = jnp.any(page_owner[None, :] == sources[:, None], 1)
        return blocks, valid
    picked = page_store[page_slot][:, :, 0]
    held_here = page_owner == device_row
    offered = jnp.where(held_here[:, None, None], picked, jnp.zeros_like(picked))
    prefix = lax.psum(offered, "req")
    return [prefix[p] for p in range(page_count)], jnp.ones((page_count,), jnp.bool_)


def static_tables(positions, width):
    half_width = width // 2
    exponent = np.arange(half_width, dtype=np.float32) * np.float32(2.0) / np.float32(width)
    frequency = np.power(np.float32(10000.0), -exponent).astype(np.float32)
    angles = positions.astype(np.float32)[:, None] * frequency[None, :]
    return np.cos(angles).astype(np.float32), np.sin(angles).astype(np.float32)


def attention_kernel(limit_ref, flag_ref, qkv_ref, cos_ref, sin_ref, *rest):
    page_refs, out_ref = rest[:-1], rest[-1]
    count, slots = qkv_ref.shape[0], qkv_ref.shape[1]
    per_group = qkv_ref.shape[2] // HD - 2
    half = HD // 2
    cosine = cos_ref[...]
    sine = sin_ref[...]
    pages = [ref[...] for ref in page_refs]
    prefix_keys = [page[:, :HD] for page in pages]
    prefix_values = [page[:, HD:] for page in pages]
    prefix_len = len(pages) * pages[0].shape[0]
    flag = flag_ref[...]

    def rope(part):
        first = part[:, :half]
        second = part[:, half:]
        return jnp.concatenate([first * cosine - second * sine, second * cosine + first * sine], -1)

    for request in range(count):
        values_in = qkv_ref[request].astype(jnp.float32)
        queries = jnp.concatenate(
            [(rope(values_in[:, q * HD:(q + 1) * HD]) * HD ** (-0.5)).astype(jnp.bfloat16)
             for q in range(per_group)], 0)
        fresh_keys = rope(values_in[:, per_group * HD:(per_group + 1) * HD]).astype(jnp.bfloat16)
        fresh_values = values_in[:, (per_group + 1) * HD:].astype(jnp.bfloat16)
        keys = jnp.concatenate(prefix_keys + [fresh_keys], 0)
        values = jnp.concatenate(prefix_values + [fresh_values], 0)
        key_count = keys.shape[0]
        rows = queries.shape[0]
        scores = lax.dot_general(queries, keys, (((1,), (1,)), ((), ())),
                                 preferred_element_type=jnp.float32)
        column = lax.broadcasted_iota(jnp.int32, (rows, key_count), 1)
        slot = lax.broadcasted_iota(jnp.int32, (rows, key_count), 0) % slots
        suffix_pos = column - prefix_len
        suffix_ok = (suffix_pos <= slot) & (suffix_pos < limit_ref[request])
        raw = jnp.where(suffix_ok, capped_exp(scores) * flag, 0.0)
        totals = jnp.sum(raw, -1, keepdims=True)
        weights = (raw / totals).astype(jnp.bfloat16)
        attended = jnp.dot(weights, values, preferred_element_type=jnp.float32).astype(jnp.bfloat16)
        out_ref[request] = jnp.concatenate(
            [attended[q * slots:(q + 1) * slots] for q in range(per_group)], 1)


def attend(qkv, cosine, sine, blocks, lengths, valid, offset, count):
    requests, slots, width = qkv.shape
    per_group = width // HD - 2
    page_len, page_width = blocks[0].shape
    prefix_len = page_len * len(blocks)
    key_count = prefix_len + slots
    flags = jnp.concatenate([jnp.repeat(valid.astype(jnp.float32), page_len),
                             jnp.ones((slots,), jnp.float32)])
    flags = flags[None, :]
    limits = jnp.concatenate(
        [jnp.broadcast_to(jnp.full((requests, 1), prefix_len + slots, jnp.int32), (requests, prefix_len)),
         jnp.broadcast_to(lengths[:, None], (requests, slots))], 1)
    limits = limits[:, None, :]
    chunk = offset // count
    full = lambda shape: pl.BlockSpec(shape, lambda r: (0,) * len(shape))
    return pl.pallas_call(
        attention_kernel,
        grid=(1,),
        in_specs=[pl.BlockSpec((count, 1, key_count), lambda r: (chunk, 0, 0)),
                  full((1, key_count)),
                  pl.BlockSpec((count, slots, width), lambda r: (chunk, 0, 0)),
                  full(cosine.shape), full(sine.shape)]
                 + [full((page_len, page_width)) for _ in blocks],
        out_specs=pl.BlockSpec((count, slots, per_group * HD), lambda r: (0, 0, 0)),
        out_shape=jax.ShapeDtypeStruct((count, slots, per_group * HD), jnp.bfloat16),
    )(limits, flags, qkv, cosine, sine, *blocks)

def project(own, w_out, tp_index, n_tp, group_width):
    if n_tp == 4:
        near = swapped(own, "tp", n_tp, 1)
        far = swapped(own, "tp", n_tp, 2)
        farther = swapped(far, "tp", n_tp, 1)
        parts = [(own, tp_index), (near, tp_index ^ 1), (far, tp_index ^ 2), (farther, tp_index ^ 3)]
    else:
        parts = [(own, tp_index)]
        for shift in range(1, n_tp):
            parts.append((shifted(own, "tp", n_tp, shift), (tp_index - shift) % n_tp))
    projected = None
    for block, group in parts:
        rows = lax.dynamic_slice_in_dim(w_out, group * group_width, group_width, 0)
        term = jnp.dot(block, rows, preferred_element_type=jnp.float32)
        projected = term if projected is None else projected + term
    return projected


def on_device(
    hidden, qkv, page_store, page_owner, page_slot, lengths, request_perm, w_out, post_gain,
    *, n_req, n_tp
):
    requests, slots, local_width = hidden.shape
    per_group = qkv.shape[3] // HD - 2
    token_rows = requests * slots
    tp_index = lax.axis_index("tp")

    blocks, valid = gather_prefix(page_store, page_owner, page_slot, n_req)

    device_row = lax.axis_index("req")
    my_requests = lax.dynamic_slice_in_dim(request_perm, device_row * requests, requests)
    matches = my_requests[:, None] == jnp.arange(lengths.shape[0], dtype=jnp.int32)[None, :]
    my_lengths = jnp.sum(jnp.where(matches, lengths[None, :], 0), 1)
    position = jnp.arange(slots, dtype=jnp.int32)
    live_mask = (position[None, :] < my_lengths[:, None]).astype(jnp.float32)

    prefix_len = page_store.shape[1] * page_owner.shape[0]
    cosine, sine = static_tables(prefix_len + np.arange(slots), HD)
    group_width = per_group * HD
    chunk = max(1, requests // 2)
    projected_parts = []
    for start in range(0, requests, chunk):
        attended = attend(qkv[:, :, 0], jnp.asarray(cosine), jnp.asarray(sine), blocks,
                          my_lengths, valid.astype(jnp.int32), start, chunk)
        own = attended.reshape(chunk * slots, per_group * HD)
        projected_parts.append(project(own, w_out, tp_index, n_tp, group_width))
    projected = jnp.concatenate(projected_parts, 0).reshape(requests, slots, local_width)

    squares = jnp.sum(projected * projected, -1)
    if n_tp == 4:
        branch_total = squares + swapped(squares, "tp", n_tp, 2)
        branch_total = branch_total + swapped(branch_total, "tp", n_tp, 1)
    else:
        branch_total = squares
        for shift in range(1, n_tp):
            branch_total = branch_total + shifted(squares, "tp", n_tp, shift)
    branch = projected * lax.rsqrt(branch_total / D + EPSILON)[..., None] * post_gain
    source = hidden.astype(jnp.float32)
    return ((source + branch) * live_mask[..., None]).astype(jnp.bfloat16)


def solution(mesh):
    placed = (
        P("req", None, "tp"),
        P("req", None, "tp", None),
        P("req", None, "tp", None),
        P(),
        P(),
        P(),
        P(),
        P(None, "tp"),
        P("tp"),
    )
    body = lambda *args: on_device(*args, n_req=mesh.shape["req"], n_tp=mesh.shape["tp"])
    return jax.shard_map(
        body, mesh=mesh, in_specs=placed, out_specs=P("req", None, "tp"), check_vma=False
    )
```

```python
import functools

import numpy as np
import jax
import jax.numpy as jnp
from jax import lax
from jax.experimental import pallas as pl
from jax.experimental.pallas import tpu as pltpu
from jax.sharding import PartitionSpec as P

D = 2304
HD = 256


EPSILON = 1e-06
SOFT_CAP = 50.0


def capped_exp(scores):
    return jnp.exp(SOFT_CAP * jnp.tanh(scores / SOFT_CAP))


def shifted(value, axis, size, shift):
    return lax.ppermute(value, axis, [(i, (i + shift) % size) for i in range(size)])


def swapped(value, axis, size, mask):
    return lax.ppermute(value, axis, [(i, i ^ mask) for i in range(size)])


def gather_prefix(page_store, page_owner, page_slot, n_req):
    device_row = lax.axis_index("req")
    page_count = page_owner.shape[0]
    if n_req <= page_count:
        mine = page_owner == device_row
        slot = jnp.sum(jnp.where(mine, page_slot, 0))
        own = page_store[0, :, 0]
        for index in range(1, page_store.shape[0]):
            own = jnp.where(slot == index, page_store[index, :, 0], own)
        blocks = [own]
        sources = [device_row]
        if n_req == 8:
            for mask in (1, 2, 3, 6):
                blocks.append(swapped(own, "req", n_req, mask))
                sources.append(device_row ^ mask)
            mirror = blocks[-1]
            for mask in (1, 2, 3):
                blocks.append(swapped(mirror, "req", n_req, mask))
                sources.append(device_row ^ 6 ^ mask)
        else:
            for shift in range(1, n_req):
                blocks.append(shifted(own, "req", n_req, shift))
                sources.append((device_row - shift) % n_req)
        sources = jnp.stack(sources)
        valid = jnp.any(page_owner[None, :] == sources[:, None], 1)
        return blocks, valid
    picked = page_store[page_slot][:, :, 0]
    held_here = page_owner == device_row
    offered = jnp.where(held_here[:, None, None], picked, jnp.zeros_like(picked))
    prefix = lax.psum(offered, "req")
    return [prefix[p] for p in range(page_count)], jnp.ones((page_count,), jnp.bool_)


def static_tables(positions, width):
    half_width = width // 2
    exponent = np.arange(half_width, dtype=np.float32) * np.float32(2.0) / np.float32(width)
    frequency = np.power(np.float32(10000.0), -exponent).astype(np.float32)
    angles = positions.astype(np.float32)[:, None] * frequency[None, :]
    return np.cos(angles).astype(np.float32), np.sin(angles).astype(np.float32)


def attention_kernel(limit_ref, flag_ref, qkv_ref, cos_ref, sin_ref, *rest):
    page_refs, out_ref = rest[:-1], rest[-1]
    count, slots = qkv_ref.shape[0], qkv_ref.shape[1]
    per_group = qkv_ref.shape[2] // HD - 2
    half = HD // 2
    cosine = cos_ref[...]
    sine = sin_ref[...]
    pages = [ref[...] for ref in page_refs]
    prefix_keys = [page[:, :HD] for page in pages]
    prefix_values = [page[:, HD:] for page in pages]
    prefix_len = len(pages) * pages[0].shape[0]
    flag = flag_ref[...]

    def rope(part):
        first = part[:, :half]
        second = part[:, half:]
        return jnp.concatenate([first * cosine - second * sine, second * cosine + first * sine], -1)

    for request in range(count):
        values_in = qkv_ref[request].astype(jnp.float32)
        queries = jnp.concatenate(
            [(rope(values_in[:, q * HD:(q + 1) * HD]) * HD ** (-0.5)).astype(jnp.bfloat16)
             for q in range(per_group)], 0)
        fresh_keys = rope(values_in[:, per_group * HD:(per_group + 1) * HD]).astype(jnp.bfloat16)
        fresh_values = values_in[:, (per_group + 1) * HD:].astype(jnp.bfloat16)
        keys = jnp.concatenate(prefix_keys + [fresh_keys], 0)
        values = jnp.concatenate(prefix_values + [fresh_values], 0)
        key_count = keys.shape[0]
        rows = queries.shape[0]
        scores = lax.dot_general(queries, keys, (((1,), (1,)), ((), ())),
                                 preferred_element_type=jnp.float32)
        exps = capped_exp(scores) * flag
        suffix_shape = (rows, key_count - prefix_len)
        column = lax.broadcasted_iota(jnp.int32, suffix_shape, 1)
        slot = lax.broadcasted_iota(jnp.int32, suffix_shape, 0) % slots
        allowed = (column <= slot) & (column < limit_ref[request][:, prefix_len:])
        prefix_raw = exps[:, :prefix_len]
        suffix_raw = jnp.where(allowed, exps[:, prefix_len:], 0.0)
        totals = jnp.sum(prefix_raw, -1, keepdims=True) + jnp.sum(suffix_raw, -1, keepdims=True)
        inverse = 1.0 / totals
        weights = jnp.concatenate([(prefix_raw * inverse).astype(jnp.bfloat16),
                                   (suffix_raw * inverse).astype(jnp.bfloat16)], 1)
        attended = jnp.dot(weights, values, preferred_element_type=jnp.float32).astype(jnp.bfloat16)
        out_ref[request] = jnp.concatenate(
            [attended[q * slots:(q + 1) * slots] for q in range(per_group)], 1)


def attend(qkv, cosine, sine, blocks, lengths, valid, offset, count):
    requests, slots, width = qkv.shape
    per_group = width // HD - 2
    page_len, page_width = blocks[0].shape
    prefix_len = page_len * len(blocks)
    key_count = prefix_len + slots
    flags = jnp.concatenate([jnp.repeat(valid.astype(jnp.float32), page_len),
                             jnp.ones((slots,), jnp.float32)])
    flags = flags[None, :]
    limits = jnp.concatenate(
        [jnp.broadcast_to(jnp.full((requests, 1), prefix_len + slots, jnp.int32), (requests, prefix_len)),
         jnp.broadcast_to(lengths[:, None], (requests, slots))], 1)
    limits = limits[:, None, :]
    chunk = offset // count
    full = lambda shape: pl.BlockSpec(shape, lambda r: (0,) * len(shape))
    return pl.pallas_call(
        attention_kernel,
        grid=(1,),
        in_specs=[pl.BlockSpec((count, 1, key_count), lambda r: (chunk, 0, 0)),
                  full((1, key_count)),
                  pl.BlockSpec((count, slots, width), lambda r: (chunk, 0, 0)),
                  full(cosine.shape), full(sine.shape)]
                 + [full((page_len, page_width)) for _ in blocks],
        out_specs=pl.BlockSpec((count, slots, per_group * HD), lambda r: (0, 0, 0)),
        out_shape=jax.ShapeDtypeStruct((count, slots, per_group * HD), jnp.bfloat16),
    )(limits, flags, qkv, cosine, sine, *blocks)

def project(own, w_out, tp_index, n_tp, group_width):
    if n_tp == 4:
        near = swapped(own, "tp", n_tp, 1)
        far = swapped(own, "tp", n_tp, 2)
        farther = swapped(far, "tp", n_tp, 1)
        parts = [(own, tp_index), (near, tp_index ^ 1), (far, tp_index ^ 2), (farther, tp_index ^ 3)]
    else:
        parts = [(own, tp_index)]
        for shift in range(1, n_tp):
            parts.append((shifted(own, "tp", n_tp, shift), (tp_index - shift) % n_tp))
    projected = None
    for block, group in parts:
        rows = lax.dynamic_slice_in_dim(w_out, group * group_width, group_width, 0)
        term = jnp.dot(block, rows, preferred_element_type=jnp.float32)
        projected = term if projected is None else projected + term
    return projected


def on_device(
    hidden, qkv, page_store, page_owner, page_slot, lengths, request_perm, w_out, post_gain,
    *, n_req, n_tp
):
    requests, slots, local_width = hidden.shape
    per_group = qkv.shape[3] // HD - 2
    token_rows = requests * slots
    tp_index = lax.axis_index("tp")

    blocks, valid = gather_prefix(page_store, page_owner, page_slot, n_req)

    device_row = lax.axis_index("req")
    my_requests = lax.dynamic_slice_in_dim(request_perm, device_row * requests, requests)
    matches = my_requests[:, None] == jnp.arange(lengths.shape[0], dtype=jnp.int32)[None, :]
    my_lengths = jnp.sum(jnp.where(matches, lengths[None, :], 0), 1)
    position = jnp.arange(slots, dtype=jnp.int32)
    live_mask = (position[None, :] < my_lengths[:, None]).astype(jnp.float32)

    prefix_len = page_store.shape[1] * page_owner.shape[0]
    cosine, sine = static_tables(prefix_len + np.arange(slots), HD)
    group_width = per_group * HD
    chunk = max(1, requests // 2)
    projected_parts = []
    for start in range(0, requests, chunk):
        attended = attend(qkv[:, :, 0], jnp.asarray(cosine), jnp.asarray(sine), blocks,
                          my_lengths, valid.astype(jnp.int32), start, chunk)
        own = attended.reshape(chunk * slots, per_group * HD)
        projected_parts.append(project(own, w_out, tp_index, n_tp, group_width))
    projected = jnp.concatenate(projected_parts, 0).reshape(requests, slots, local_width)

    squares = jnp.sum(projected * projected, -1)
    branch_total = squares
    for shift in range(1, n_tp):
        branch_total = branch_total + shifted(squares, "tp", n_tp, shift)
    branch = projected * lax.rsqrt(branch_total / D + EPSILON)[..., None] * post_gain
    source = hidden.astype(jnp.float32)
    return ((source + branch) * live_mask[..., None]).astype(jnp.bfloat16)


def solution(mesh):
    placed = (
        P("req", None, "tp"),
        P("req", None, "tp", None),
        P("req", None, "tp", None),
        P(),
        P(),
        P(),
        P(),
        P(None, "tp"),
        P("tp"),
    )
    body = lambda *args: on_device(*args, n_req=mesh.shape["req"], n_tp=mesh.shape["tp"])
    return jax.shard_map(
        body, mesh=mesh, in_specs=placed, out_specs=P("req", None, "tp"), check_vma=False
    )
```

```python
import functools

import numpy as np
import jax
import jax.numpy as jnp
from jax import lax
from jax.experimental import pallas as pl
from jax.experimental.pallas import tpu as pltpu
from jax.sharding import PartitionSpec as P

D = 2304
HD = 256


EPSILON = 1e-06
SOFT_CAP = 50.0


def capped_exp(scores):
    return jnp.exp(SOFT_CAP * jnp.tanh(scores / SOFT_CAP))


def shifted(value, axis, size, shift):
    return lax.ppermute(value, axis, [(i, (i + shift) % size) for i in range(size)])


def swapped(value, axis, size, mask):
    return lax.ppermute(value, axis, [(i, i ^ mask) for i in range(size)])


def gather_prefix(page_store, page_owner, page_slot, n_req):
    device_row = lax.axis_index("req")
    page_count = page_owner.shape[0]
    if n_req <= page_count:
        mine = page_owner == device_row
        slot = jnp.sum(jnp.where(mine, page_slot, 0))
        own = page_store[0, :, 0]
        for index in range(1, page_store.shape[0]):
            own = jnp.where(slot == index, page_store[index, :, 0], own)
        blocks = [own]
        sources = [device_row]
        if n_req == 8:
            for mask in (1, 2, 3, 6):
                blocks.append(swapped(own, "req", n_req, mask))
                sources.append(device_row ^ mask)
            mirror = blocks[-1]
            for mask in (1, 2, 3):
                blocks.append(swapped(mirror, "req", n_req, mask))
                sources.append(device_row ^ 6 ^ mask)
        else:
            for shift in range(1, n_req):
                blocks.append(shifted(own, "req", n_req, shift))
                sources.append((device_row - shift) % n_req)
        sources = jnp.stack(sources)
        valid = jnp.any(page_owner[None, :] == sources[:, None], 1)
        return blocks, valid
    picked = page_store[page_slot][:, :, 0]
    held_here = page_owner == device_row
    offered = jnp.where(held_here[:, None, None], picked, jnp.zeros_like(picked))
    prefix = lax.psum(offered, "req")
    return [prefix[p] for p in range(page_count)], jnp.ones((page_count,), jnp.bool_)


def static_tables(positions, width):
    half_width = width // 2
    exponent = np.arange(half_width, dtype=np.float32) * np.float32(2.0) / np.float32(width)
    frequency = np.power(np.float32(10000.0), -exponent).astype(np.float32)
    angles = positions.astype(np.float32)[:, None] * frequency[None, :]
    return np.cos(angles).astype(np.float32), np.sin(angles).astype(np.float32)


def attention_kernel(limit_ref, flag_ref, qkv_ref, cos_ref, sin_ref, *rest):
    page_refs, out_ref = rest[:-1], rest[-1]
    count, slots = qkv_ref.shape[0], qkv_ref.shape[1]
    per_group = qkv_ref.shape[2] // HD - 2
    half = HD // 2
    cosine = cos_ref[...]
    sine = sin_ref[...]
    pages = [ref[...] for ref in page_refs]
    prefix_keys = [page[:, :HD] for page in pages]
    prefix_values = [page[:, HD:] for page in pages]
    prefix_len = len(pages) * pages[0].shape[0]
    flag = flag_ref[...]

    def rope(part):
        first = part[:, :half]
        second = part[:, half:]
        return jnp.concatenate([first * cosine - second * sine, second * cosine + first * sine], -1)

    for request in range(count):
        values_in = qkv_ref[request].astype(jnp.float32)
        queries = jnp.concatenate(
            [(rope(values_in[:, q * HD:(q + 1) * HD]) * HD ** (-0.5)).astype(jnp.bfloat16)
             for q in range(per_group)], 0)
        fresh_keys = rope(values_in[:, per_group * HD:(per_group + 1) * HD]).astype(jnp.bfloat16)
        fresh_values = values_in[:, (per_group + 1) * HD:].astype(jnp.bfloat16)
        keys = jnp.concatenate(prefix_keys + [fresh_keys], 0)
        values = jnp.concatenate(prefix_values + [fresh_values], 0)
        key_count = keys.shape[0]
        rows = queries.shape[0]
        scores = lax.dot_general(queries, keys, (((1,), (1,)), ((), ())),
                                 preferred_element_type=jnp.float32)
        column = lax.broadcasted_iota(jnp.int32, (rows, key_count), 1)
        slot = lax.broadcasted_iota(jnp.int32, (rows, key_count), 0) % slots
        suffix_pos = column - prefix_len
        suffix_ok = (suffix_pos <= slot) & (suffix_pos < limit_ref[request])
        raw = jnp.where(suffix_ok, capped_exp(scores) * flag, 0.0)
        totals = jnp.sum(raw, -1, keepdims=True)
        weights = (raw / totals).astype(jnp.bfloat16)
        attended = jnp.dot(weights, values, preferred_element_type=jnp.float32).astype(jnp.bfloat16)
        out_ref[request] = jnp.concatenate(
            [attended[q * slots:(q + 1) * slots] for q in range(per_group)], 1)


def attend(qkv, cosine, sine, blocks, lengths, valid, offset, count):
    requests, slots, width = qkv.shape
    per_group = width // HD - 2
    page_len, page_width = blocks[0].shape
    prefix_len = page_len * len(blocks)
    key_count = prefix_len + slots
    flags = jnp.concatenate([jnp.repeat(valid.astype(jnp.float32), page_len),
                             jnp.ones((slots,), jnp.float32)])
    flags = flags[None, :]
    limits = jnp.concatenate(
        [jnp.broadcast_to(jnp.full((requests, 1), prefix_len + slots, jnp.int32), (requests, prefix_len)),
         jnp.broadcast_to(lengths[:, None], (requests, slots))], 1)
    limits = limits[:, None, :]
    chunk = offset // count
    full = lambda shape: pl.BlockSpec(shape, lambda r: (0,) * len(shape))
    return pl.pallas_call(
        attention_kernel,
        grid=(1,),
        in_specs=[pl.BlockSpec((count, 1, key_count), lambda r: (chunk, 0, 0)),
                  full((1, key_count)),
                  pl.BlockSpec((count, slots, width), lambda r: (chunk, 0, 0)),
                  full(cosine.shape), full(sine.shape)]
                 + [full((page_len, page_width)) for _ in blocks],
        out_specs=pl.BlockSpec((count, slots, per_group * HD), lambda r: (0, 0, 0)),
        out_shape=jax.ShapeDtypeStruct((count, slots, per_group * HD), jnp.bfloat16),
    )(limits, flags, qkv, cosine, sine, *blocks)

def project(own, w_out, tp_index, n_tp, group_width):
    if n_tp == 4:
        near = swapped(own, "tp", n_tp, 1)
        far = swapped(own, "tp", n_tp, 2)
        farther = swapped(far, "tp", n_tp, 1)
        parts = [(own, tp_index), (near, tp_index ^ 1), (far, tp_index ^ 2), (farther, tp_index ^ 3)]
    else:
        parts = [(own, tp_index)]
        for shift in range(1, n_tp):
            parts.append((shifted(own, "tp", n_tp, shift), (tp_index - shift) % n_tp))
    projected = None
    for block, group in parts:
        rows = lax.dynamic_slice_in_dim(w_out, group * group_width, group_width, 0)
        term = jnp.dot(block, rows, preferred_element_type=jnp.float32)
        projected = term if projected is None else projected + term
    return projected


def on_device(
    hidden, qkv, page_store, page_owner, page_slot, lengths, request_perm, w_out, post_gain,
    *, n_req, n_tp
):
    requests, slots, local_width = hidden.shape
    per_group = qkv.shape[3] // HD - 2
    token_rows = requests * slots
    tp_index = lax.axis_index("tp")

    blocks, valid = gather_prefix(page_store, page_owner, page_slot, n_req)

    device_row = lax.axis_index("req")
    my_requests = lax.dynamic_slice_in_dim(request_perm, device_row * requests, requests)
    matches = my_requests[:, None] == jnp.arange(lengths.shape[0], dtype=jnp.int32)[None, :]
    my_lengths = jnp.sum(jnp.where(matches, lengths[None, :], 0), 1)
    position = jnp.arange(slots, dtype=jnp.int32)
    live_mask = (position[None, :] < my_lengths[:, None]).astype(jnp.float32)

    prefix_len = page_store.shape[1] * page_owner.shape[0]
    cosine, sine = static_tables(prefix_len + np.arange(slots), HD)
    group_width = per_group * HD
    chunk = max(1, requests // 2)
    chunk_parts = []
    for start in range(0, requests, chunk):
        attended = attend(qkv[:, :, 0], jnp.asarray(cosine), jnp.asarray(sine), blocks,
                          my_lengths, valid.astype(jnp.int32), start, chunk)
        own = attended.reshape(chunk * slots, per_group * HD)
        if n_tp == 4:
            near = swapped(own, "tp", n_tp, 1)
            far = swapped(own, "tp", n_tp, 2)
            chunk_parts.append([(own, tp_index), (near, tp_index ^ 1), (far, tp_index ^ 2),
                                (swapped(far, "tp", n_tp, 1), tp_index ^ 3)])
        else:
            chunk_parts.append([(own, tp_index)] + [
                (shifted(own, "tp", n_tp, shift), (tp_index - shift) % n_tp)
                for shift in range(1, n_tp)])
    projected = None
    for number in range(n_tp):
        block = jnp.concatenate([parts[number][0] for parts in chunk_parts], 0)
        rows = lax.dynamic_slice_in_dim(w_out, chunk_parts[0][number][1] * group_width, group_width, 0)
        term = jnp.dot(block, rows, preferred_element_type=jnp.float32)
        projected = term if projected is None else projected + term
    projected = projected.reshape(requests, slots, local_width)

    squares = jnp.sum(projected * projected, -1)
    branch_total = squares
    for shift in range(1, n_tp):
        branch_total = branch_total + shifted(squares, "tp", n_tp, shift)
    branch = projected * lax.rsqrt(branch_total / D + EPSILON)[..., None] * post_gain
    source = hidden.astype(jnp.float32)
    return ((source + branch) * live_mask[..., None]).astype(jnp.bfloat16)


def solution(mesh):
    placed = (
        P("req", None, "tp"),
        P("req", None, "tp", None),
        P("req", None, "tp", None),
        P(),
        P(),
        P(),
        P(),
        P(None, "tp"),
        P("tp"),
    )
    body = lambda *args: on_device(*args, n_req=mesh.shape["req"], n_tp=mesh.shape["tp"])
    return jax.shard_map(
        body, mesh=mesh, in_specs=placed, out_specs=P("req", None, "tp"), check_vma=False
    )
```
